32 devices in a mesh: segment: 4 (over z), dp: 8 (over y, x, core).
Axes of the slice: x: 2, y: 2, z: 4, core: 2. Of those that a mesh axis runs over, the one named last changes fastest.
Arguments:
- x_in: bfloat16 [2, 512, 8192], P(None, 'dp'), may hold values from -6 to 6
- cotangent: bfloat16 [2, 512, 8192], P(None, 'dp'), may hold values from -6 to 6
- weights: bfloat16 [1024, 128, 128], P('segment'), may hold values from -0.375 to 0.375
- block_index: int32 [1024, 3], P('segment'), may hold values from 0 to 63, as said below
Outputs:
- weight_grad: float32 [1024, 128, 128], P(('segment', 'dp'))
The draws below stay inside these ranges and needn't reach their ends.
Inputs may be any that keep to these rules, and one draw needn't show every extreme that they name: `block_index`: within each segment's 2 * 128 rows, layer slot j takes rows j * 128 to (j + 1) * 128 - 1. A segment holds 1 to 2 layers, the first ones; the rest have all flags 0; some segment holds 2. A held layer has 32 to 128 kept slots, flags 1 first; some layer keeps 128. The (row, column) pairs of one layer's slots are distinct. Rows and columns of empty slots are arbitrary.
All inputs are finite; a program needn't handle non-finite values.
Results may differ from the reference program's by a relative error of at most 0.013.
Values may be sent and summed in bfloat16 or wider, within the bound.
No kernel may reach another device: no remote copies, remote signals or barrier semaphores. Data moves between devices by JAX's collectives and lax.ppermute only.
A program may use at most 192 MiB of HBM per device.

```python
import jax
import jax.numpy as jnp
from jax import lax

D = 8192
BLK = 128
LSLOT = 2
KMAX = 128
MB = 2
TOKENS = 512
SLOTS = 1024
N_SEGMENT = 4


def draw_block_index(key, part):
    base = jax.random.fold_in(key, 7)
    k_lay, k_cnt, k_pick, k_top = jax.random.split(base, 4)
    nbr = D // BLK
    layers = jax.random.randint(k_lay, (N_SEGMENT,), 1, LSLOT + 1)
    top_segment = jax.random.randint(k_top, (), 0, N_SEGMENT)
    segment_ids = jnp.arange(N_SEGMENT)
    layers = jnp.where(segment_ids == top_segment, LSLOT, layers)
    counts = jax.random.randint(k_cnt, (N_SEGMENT, LSLOT), KMAX // 4, KMAX + 1)
    first_top = (segment_ids[:, None] == top_segment) & (jnp.arange(LSLOT)[None, :] == 0)
    counts = jnp.where(first_top, KMAX, counts)
    active = jnp.arange(LSLOT)[None, :] < layers[:, None]
    counts = jnp.where(active, counts, 0)
    keys = jax.random.split(k_pick, N_SEGMENT * LSLOT)
    picks = jax.vmap(lambda one: jax.random.permutation(one, nbr * nbr)[:KMAX])(keys)
    picks = picks.reshape(N_SEGMENT, LSLOT, KMAX)
    valid = (jnp.arange(KMAX)[None, None, :] < counts[:, :, None]).astype(jnp.int32)
    stacked = jnp.stack([picks // nbr, picks % nbr, valid], axis=-1)
    return stacked.reshape(N_SEGMENT * LSLOT * KMAX, 3).astype(jnp.int32)


def level_of(stream_key, shape, cuts, least, high):
    factor_of = 1.0
    for axis_at, blocks in cuts:
        draws = jax.random.uniform(jax.random.fold_in(jax.random.fold_in(stream_key, 6), axis_at), (blocks,), jnp.float32, least / len(cuts), high / len(cuts))
        factor_of = factor_of * jnp.repeat(jnp.exp(draws), shape[axis_at] // blocks).reshape((-1,) + (1,) * (len(shape) - 1 - axis_at))
    return factor_of


def noise(stream_key, shape, scale, most, cuts=(), held_as=jnp.bfloat16):
    values = jax.random.normal(stream_key, shape, jnp.float32) * scale
    if len(cuts) > 0:
        values = level_of(stream_key, shape, cuts, -0.22, 0.18) * values
    return jnp.clip(values, min=-most, max=most).astype(held_as)


def setup_inputs(seed: int = 0) -> dict:
    key_of = jax.random.split(jax.random.key(seed), 5)
    return {
        "x_in": noise(key_of[0], (MB, TOKENS, D), 1.0, 6.0, ((1, 8),)),
        "cotangent": noise(key_of[1], (MB, TOKENS, D), 1.0, 6.0, ((1, 8),)),
        "weights": noise(key_of[2], (SLOTS, BLK, BLK), (2 * BLK) ** -0.5, 0.375, ((0, 4),)),
        "block_index": draw_block_index(jax.random.fold_in(key_of[4], 71), 0),
    }


def layer_pre(h, wl, il, nbr):
    rows = il[:, 0]
    cols = il[:, 1]
    valid = (il[:, 2] > 0).astype(jnp.float32)
    hb = h.reshape(h.shape[0], nbr, BLK)[:, rows, :].astype(jnp.float32)
    prod = jnp.einsum("nkd,kde->nke", hb, wl.astype(jnp.float32))
    place = (cols[:, None] == jnp.arange(nbr)[None, :]).astype(jnp.float32) * valid[:, None]
    y = jnp.einsum("nke,kc->nce", prod, place, precision=lax.Precision.HIGHEST)
    return y.reshape(h.shape[0], nbr * BLK), hb


def reference(x_in, cotangent, weights, block_index):
    nbr = D // BLK
    total_layers = N_SEGMENT * LSLOT
    wts = weights.reshape(total_layers, KMAX, BLK, BLK)
    idx = block_index.reshape(total_layers, KMAX, 3)
    h = x_in.reshape(-1, D)
    inputs = []
    for layer in range(total_layers):
        y, hb = layer_pre(h, wts[layer], idx[layer], nbr)
        inputs.append(h)
        h = (h.astype(jnp.float32) + jax.nn.silu(y)).astype(jnp.bfloat16)
    g = cotangent.reshape(-1, D)
    grads = [None] * total_layers
    for layer in reversed(range(total_layers)):
        il = idx[layer]
        valid = (il[:, 2] > 0).astype(jnp.float32)
        y, hb = layer_pre(inputs[layer], wts[layer], il, nbr)
        sig = jax.nn.sigmoid(y)
        s = (g.astype(jnp.float32) * sig * (1.0 + y * (1.0 - sig))).astype(jnp.bfloat16)
        sb = s.reshape(s.shape[0], nbr, BLK)[:, il[:, 1], :].astype(jnp.float32)
        grads[layer] = jnp.einsum("nkd,nke->kde", hb, sb) * valid[:, None, None]
        back = jnp.einsum("nke,kde->nkd", sb, wts[layer].astype(jnp.float32))
        rowmask = (il[:, 0][:, None] == jnp.arange(nbr)[None, :]).astype(jnp.float32) * valid[:, None]
        spread = jnp.einsum("nkd,kr->nrd", back, rowmask, precision=lax.Precision.HIGHEST).reshape(-1, D)
        g = (g.astype(jnp.float32) + spread).astype(jnp.bfloat16)
    return jnp.stack(grads).reshape(N_SEGMENT * LSLOT * KMAX, BLK, BLK)
```

```python
import functools

import jax
import jax.numpy as jnp
from jax import lax
from jax.experimental import pallas as pl
from jax.experimental.pallas import tpu as pltpu
from jax.sharding import PartitionSpec as P

BLK = 128
LSLOT = 2
KMAX = 128
CH = 512
VMEM_LIMIT = 60 * 1024 * 1024

_SMEM = pl.BlockSpec(memory_space=pltpu.SMEM)
_VMEM = pl.BlockSpec(memory_space=pltpu.VMEM)


def shifted(value, axis, steps):
    count = lax.axis_size(axis)
    leading, last = (max(0, -steps), min(count, count - steps))
    return lax.ppermute(value, axis, [(source, source + steps) for source in range(leading, last)])


def _blk(i):
    return pl.ds(pl.multiple_of(i * BLK, BLK), BLK)


def _chunk(j):
    return pl.ds(pl.multiple_of(j * CH, CH), CH)


def _fwd_kernel(idx_ref, h_ref, w_ref, hout_ref, y_ref):
    width = h_ref.shape[1]
    y_ref[...] = jnp.zeros_like(y_ref)

    def slot(k, carry):
        r = idx_ref[3 * k]
        c = idx_ref[3 * k + 1]
        v = idx_ref[3 * k + 2]

        @pl.when(v > 0)
        def _():
            p = jnp.dot(h_ref[:, _blk(r)], w_ref[k], preferred_element_type=jnp.float32)
            y_ref[:, _blk(c)] += p

        return carry

    lax.fori_loop(0, w_ref.shape[0], slot, 0)

    def epi(j, carry):
        y = y_ref[:, _chunk(j)]
        h = h_ref[:, _chunk(j)].astype(jnp.float32)
        hout_ref[:, _chunk(j)] = (h + y / (1.0 + jnp.exp(-y))).astype(hout_ref.dtype)
        return carry

    lax.fori_loop(0, width // CH, epi, 0)


def layer_forward(h, wl, il):
    rows, width = h.shape
    return pl.pallas_call(
        _fwd_kernel,
        out_shape=(
            jax.ShapeDtypeStruct((rows, width), jnp.bfloat16),
            jax.ShapeDtypeStruct((rows, width), jnp.float32),
        ),
        in_specs=[_SMEM, _VMEM, _VMEM],
        out_specs=(_VMEM, _VMEM),
        compiler_params=pltpu.CompilerParams(vmem_limit_bytes=VMEM_LIMIT),
    )(il.reshape(-1), h, wl)


def _bwd_kernel(idx_ref, g_ref, y_ref, w_ref, gout_ref, s_ref, sp_ref):
    width = g_ref.shape[1]

    def pre(j, carry):
        y = y_ref[:, _chunk(j)]
        sig = 1.0 / (1.0 + jnp.exp(-y))
        g = g_ref[:, _chunk(j)].astype(jnp.float32)
        s_ref[:, _chunk(j)] = (g * sig * (1.0 + y * (1.0 - sig))).astype(s_ref.dtype)
        sp_ref[:, _chunk(j)] = jnp.zeros((g_ref.shape[0], CH), jnp.float32)
        return carry

    lax.fori_loop(0, width // CH, pre, 0)

    def slot(k, carry):
        r = idx_ref[3 * k]
        c = idx_ref[3 * k + 1]
        v = idx_ref[3 * k + 2]

        @pl.when(v > 0)
        def _():
            back = lax.dot_general(
                s_ref[:, _blk(c)],
                w_ref[k],
                (((1,), (1,)), ((), ())),
                preferred_element_type=jnp.float32,
            )
            sp_ref[:, _blk(r)] += back

        return carry

    lax.fori_loop(0, w_ref.shape[0], slot, 0)

    def epi(j, carry):
        g = g_ref[:, _chunk(j)].astype(jnp.float32)
        gout_ref[:, _chunk(j)] = (g + sp_ref[:, _chunk(j)]).astype(gout_ref.dtype)
        return carry

    lax.fori_loop(0, width // CH, epi, 0)


def layer_backward(g, y, wl, il):
    rows, width = g.shape
    return pl.pallas_call(
        _bwd_kernel,
        out_shape=(
            jax.ShapeDtypeStruct((rows, width), jnp.bfloat16),
            jax.ShapeDtypeStruct((rows, width), jnp.bfloat16),
        ),
        in_specs=[_SMEM, _VMEM, _VMEM, _VMEM],
        out_specs=(_VMEM, _VMEM),
        scratch_shapes=[pltpu.VMEM((rows, width), jnp.float32)],
        compiler_params=pltpu.CompilerParams(vmem_limit_bytes=VMEM_LIMIT),
    )(il.reshape(-1), g, y, wl)


def _dw_kernel(idx_ref, h_ref, s_ref, dw_ref):
    def slot(k, carry):
        r = idx_ref[3 * k]
        c = idx_ref[3 * k + 1]
        v = idx_ref[3 * k + 2]

        @pl.when(v > 0)
        def _():
            dw_ref[k] = lax.dot_general(
                h_ref[:, _blk(r)],
                s_ref[:, _blk(c)],
                (((0,), (0,)), ((), ())),
                preferred_element_type=jnp.float32,
            )

        @pl.when(v <= 0)
        def _():
            dw_ref[k] = jnp.zeros((BLK, BLK), jnp.float32)

        return carry

    lax.fori_loop(0, dw_ref.shape[0], slot, 0)


def layer_dw(h_all, s_all, il):
    return pl.pallas_call(
        _dw_kernel,
        out_shape=jax.ShapeDtypeStruct((il.shape[0], BLK, BLK), jnp.float32),
        in_specs=[_SMEM, _VMEM, _VMEM],
        out_specs=_VMEM,
        compiler_params=pltpu.CompilerParams(vmem_limit_bytes=VMEM_LIMIT),
    )(il.reshape(-1), h_all, s_all)


def on_device(x_in, cotangent, weights, block_index):
    segments = lax.axis_size("segment")
    me_segment = lax.axis_index("segment")
    mbs, rows_dev, width = x_in.shape
    wts = weights.reshape(LSLOT, KMAX, BLK, BLK)
    idx = block_index.reshape(LSLOT, KMAX, 3)
    ticks = mbs + segments - 1

    def segment_forward(start):
        h = start
        inputs = []
        preacts = []
        for layer in range(LSLOT):
            h_next, y = layer_forward(h, wts[layer], idx[layer])
            inputs.append(h)
            preacts.append(y)
            h = h_next
        return (h, jnp.stack(inputs), jnp.stack(preacts))

    def skip_forward(start):
        return (
            start,
            jnp.zeros((LSLOT, rows_dev, width), jnp.bfloat16),
            jnp.zeros((LSLOT, rows_dev, width), jnp.float32),
        )

    stash_h = jnp.zeros((mbs, LSLOT, rows_dev, width), jnp.bfloat16)
    stash_y = jnp.zeros((mbs, LSLOT, rows_dev, width), jnp.float32)

    def forward_tick(tick, carry):
        received, saved_h, saved_y = carry
        micro = tick - me_segment
        live = (micro >= 0) & (micro < mbs)
        place_at = jnp.clip(micro, 0, mbs - 1)
        first = lax.dynamic_index_in_dim(x_in, place_at, 0, keepdims=False)
        start = jnp.where(me_segment == 0, first, received)
        h_out, inputs, preacts = lax.cond(live, segment_forward, skip_forward, start)
        saved_h = jnp.where(
            live, lax.dynamic_update_index_in_dim(saved_h, inputs, place_at, 0), saved_h
        )
        saved_y = jnp.where(
            live, lax.dynamic_update_index_in_dim(saved_y, preacts, place_at, 0), saved_y
        )
        received = shifted(h_out, "segment", 1)
        return (received, saved_h, saved_y)

    blank = jnp.zeros((rows_dev, width), jnp.bfloat16)
    unused_recv, stash_h, stash_y = lax.fori_loop(
        0, ticks, forward_tick, (blank, stash_h, stash_y)
    )
    stash_s = jnp.zeros((mbs, LSLOT, rows_dev, width), jnp.bfloat16)

    def backward_tick(tick, carry):
        received, saved_s = carry
        micro = tick - (segments - 1 - me_segment)
        live = (micro >= 0) & (micro < mbs)
        place_at = jnp.clip(micro, 0, mbs - 1)
        top = lax.dynamic_index_in_dim(cotangent, place_at, 0, keepdims=False)
        grad_in = jnp.where(me_segment == segments - 1, top, received)
        layer_y = lax.dynamic_index_in_dim(stash_y, place_at, 0, keepdims=False)

        def run_back(grad):
            s_parts = [None] * LSLOT
            for layer in reversed(range(LSLOT)):
                grad, s_parts[layer] = layer_backward(grad, layer_y[layer], wts[layer], idx[layer])
            return (grad, jnp.stack(s_parts))

        def skip_back(grad):
            return (grad, jnp.zeros((LSLOT, rows_dev, width), jnp.bfloat16))

        grad_out, s_all = lax.cond(live, run_back, skip_back, grad_in)
        saved_s = jnp.where(
            live, lax.dynamic_update_index_in_dim(saved_s, s_all, place_at, 0), saved_s
        )
        received = shifted(grad_out, "segment", -1)
        return (received, saved_s)

    unused_grad, stash_s = lax.fori_loop(0, ticks, backward_tick, (blank, stash_s))
    dws = []
    for layer in range(LSLOT):
        h_all = stash_h[:, layer].reshape(mbs * rows_dev, width)
        s_all = stash_s[:, layer].reshape(mbs * rows_dev, width)
        dws.append(layer_dw(h_all, s_all, idx[layer]))
    acc = jnp.concatenate(dws, axis=0)
    return lax.psum_scatter(acc, "dp", scatter_dimension=0, tiled=True)


def solution(mesh):
    return jax.shard_map(
        on_device,
        mesh=mesh,
        in_specs=(
            P(None, "dp", None),
            P(None, "dp", None),
            P("segment", None, None),
            P("segment", None),
        ),
        out_specs=P(("segment", "dp"), None, None),
        check_vma=False,
    )
```

```python
import functools

import jax
import jax.numpy as jnp
from jax import lax
from jax.experimental import pallas as pl
from jax.experimental.pallas import tpu as pltpu
from jax.sharding import PartitionSpec as P

BLK = 128
LSLOT = 2
KMAX = 128
CH = 512
NSUB = 16
VMEM_LIMIT = 60 * 1024 * 1024

_SMEM = pl.BlockSpec(memory_space=pltpu.SMEM)
_VMEM = pl.BlockSpec(memory_space=pltpu.VMEM)
_ANY = pl.BlockSpec(memory_space=pl.ANY)


def shifted(value, axis, steps):
    count = lax.axis_size(axis)
    leading, last = (max(0, -steps), min(count, count - steps))
    return lax.ppermute(value, axis, [(source, source + steps) for source in range(leading, last)])


def _blk(i):
    return pl.ds(pl.multiple_of(i * BLK, BLK), BLK)


def _chunk(j):
    return pl.ds(pl.multiple_of(j * CH, CH), CH)


def _flag(idx_ref, k):
    return jnp.where(idx_ref[3 * k + 2] > 0, 1.0, 0.0).astype(jnp.float32)


def _w_copies(w_hbm, base, w_vmem, sems):
    copies = []
    for j in range(w_vmem.shape[0] // NSUB):
        copy = pltpu.make_async_copy(
            w_hbm.at[pl.ds(base + j * NSUB, NSUB)], w_vmem.at[pl.ds(j * NSUB, NSUB)], sems.at[j]
        )
        copy.start()
        copies.append(copy)
    return copies


def _slot_chunks(idx_ref, copies, body):
    for j, copy in enumerate(copies):
        copy.wait()

        @pl.when(idx_ref[3 * j * NSUB + 2] > 0)
        def _():
            for k in range(j * NSUB, (j + 1) * NSUB):
                body(k)


def _fwd_kernel(base, idx_ref, h_ref, w_hbm, hout_ref, y_ref, w_vmem, sems):
    width = h_ref.shape[1]
    copies = _w_copies(w_hbm, base, w_vmem, sems)
    y_ref[...] = jnp.zeros_like(y_ref)

    def body(k):
        r = idx_ref[3 * k]
        c = idx_ref[3 * k + 1]
        p = jnp.dot(h_ref[:, _blk(r)], w_vmem[k], preferred_element_type=jnp.float32)
        y_ref[:, _blk(c)] += p * _flag(idx_ref, k)

    _slot_chunks(idx_ref, copies, body)

    def epi(j, carry):
        y = y_ref[:, _chunk(j)]
        h = h_ref[:, _chunk(j)].astype(jnp.float32)
        hout_ref[:, _chunk(j)] = (h + y / (1.0 + jnp.exp(-y))).astype(hout_ref.dtype)
        return carry

    lax.fori_loop(0, width // CH, epi, 0)


def layer_forward(h, weights, layer, il):
    rows, width = h.shape
    return pl.pallas_call(
        functools.partial(_fwd_kernel, layer * KMAX),
        out_shape=(
            jax.ShapeDtypeStruct((rows, width), jnp.bfloat16),
            jax.ShapeDtypeStruct((rows, width), jnp.float32),
        ),
        in_specs=[_SMEM, _VMEM, _ANY],
        out_specs=(_VMEM, _VMEM),
        scratch_shapes=[
            pltpu.VMEM((KMAX, BLK, BLK), weights.dtype),
            pltpu.SemaphoreType.DMA((KMAX // NSUB,)),
        ],
        compiler_params=pltpu.CompilerParams(vmem_limit_bytes=VMEM_LIMIT),
    )(il.reshape(-1), h, weights)


def _bwd_kernel(base, idx_ref, g_ref, y_ref, w_hbm, gout_ref, s_ref, sp_ref, w_vmem, sems):
    width = g_ref.shape[1]
    copies = _w_copies(w_hbm, base, w_vmem, sems)

    def pre(j, carry):
        y = y_ref[:, _chunk(j)]
        sig = 1.0 / (1.0 + jnp.exp(-y))
        g = g_ref[:, _chunk(j)].astype(jnp.float32)
        s_ref[:, _chunk(j)] = (g * sig * (1.0 + y * (1.0 - sig))).astype(s_ref.dtype)
        sp_ref[:, _chunk(j)] = jnp.zeros((g_ref.shape[0], CH), jnp.float32)
        return carry

    lax.fori_loop(0, width // CH, pre, 0)

    def body(k):
        r = idx_ref[3 * k]
        c = idx_ref[3 * k + 1]
        back = lax.dot_general(
            s_ref[:, _blk(c)],
            w_vmem[k],
            (((1,), (1,)), ((), ())),
            preferred_element_type=jnp.float32,
        )
        sp_ref[:, _blk(r)] += back * _flag(idx_ref, k)

    _slot_chunks(idx_ref, copies, body)

    def epi(j, carry):
        g = g_ref[:, _chunk(j)].astype(jnp.float32)
        gout_ref[:, _chunk(j)] = (g + sp_ref[:, _chunk(j)]).astype(gout_ref.dtype)
        return carry

    lax.fori_loop(0, width // CH, epi, 0)


def layer_backward(g, y, weights, layer, il):
    rows, width = g.shape
    return pl.pallas_call(
        functools.partial(_bwd_kernel, layer * KMAX),
        out_shape=(
            jax.ShapeDtypeStruct((rows, width), jnp.bfloat16),
            jax.ShapeDtypeStruct((rows, width), jnp.bfloat16),
        ),
        in_specs=[_SMEM, _VMEM, _VMEM, _ANY],
        out_specs=(_VMEM, _VMEM),
        scratch_shapes=[
            pltpu.VMEM((rows, width), jnp.float32),
            pltpu.VMEM((KMAX, BLK, BLK), weights.dtype),
            pltpu.SemaphoreType.DMA((KMAX // NSUB,)),
        ],
        compiler_params=pltpu.CompilerParams(vmem_limit_bytes=VMEM_LIMIT),
    )(il.reshape(-1), g, y, weights)


def _dw_kernel(idx_ref, h_ref, s_ref, dw_ref):
    for j in range(dw_ref.shape[0] // NSUB):

        @pl.when(idx_ref[3 * j * NSUB + 2] > 0)
        def _():
            for k in range(j * NSUB, (j + 1) * NSUB):
                r = idx_ref[3 * k]
                c = idx_ref[3 * k + 1]
                dw_ref[k] = lax.dot_general(
                    h_ref[:, _blk(r)],
                    s_ref[:, _blk(c)],
                    (((0,), (0,)), ((), ())),
                    preferred_element_type=jnp.float32,
                ) * _flag(idx_ref, k)

        @pl.when(idx_ref[3 * j * NSUB + 2] <= 0)
        def _():
            dw_ref[pl.ds(j * NSUB, NSUB)] = jnp.zeros((NSUB, BLK, BLK), jnp.float32)


def layer_dw(h_all, s_all, il):
    return pl.pallas_call(
        _dw_kernel,
        out_shape=jax.ShapeDtypeStruct((il.shape[0], BLK, BLK), jnp.float32),
        in_specs=[_SMEM, _VMEM, _VMEM],
        out_specs=_VMEM,
        compiler_params=pltpu.CompilerParams(vmem_limit_bytes=VMEM_LIMIT),
    )(il.reshape(-1), h_all, s_all)


def on_device(x_in, cotangent, weights, block_index):
    segments = lax.axis_size("segment")
    me_segment = lax.axis_index("segment")
    mbs, rows_dev, width = x_in.shape
    idx = block_index.reshape(LSLOT, KMAX, 3)
    ticks = mbs + segments - 1

    def segment_forward(start):
        h = start
        inputs = []
        preacts = []
        for layer in range(LSLOT):
            h_next, y = layer_forward(h, weights, layer, idx[layer])
            inputs.append(h)
            preacts.append(y)
            h = h_next
        return (h, jnp.stack(inputs), jnp.stack(preacts))

    def skip_forward(start):
        return (
            start,
            jnp.zeros((LSLOT, rows_dev, width), jnp.bfloat16),
            jnp.zeros((LSLOT, rows_dev, width), jnp.float32),
        )

    stash_h = jnp.zeros((mbs + 1, LSLOT, rows_dev, width), jnp.bfloat16)
    stash_y = jnp.zeros((mbs + 1, LSLOT, rows_dev, width), jnp.float32)

    def forward_tick(tick, carry):
        received, saved_h, saved_y = carry
        micro = tick - me_segment
        live = (micro >= 0) & (micro < mbs)
        place_at = jnp.clip(micro, 0, mbs - 1)
        first = lax.dynamic_index_in_dim(x_in, place_at, 0, keepdims=False)
        start = jnp.where(me_segment == 0, first, received)
        h_out, inputs, preacts = lax.cond(live, segment_forward, skip_forward, start)
        store_at = jnp.where(live, place_at, mbs)
        saved_h = lax.dynamic_update_index_in_dim(saved_h, inputs, store_at, 0)
        saved_y = lax.dynamic_update_index_in_dim(saved_y, preacts, store_at, 0)
        received = shifted(h_out, "segment", 1)
        return (received, saved_h, saved_y)

    blank = jnp.zeros((rows_dev, width), jnp.bfloat16)
    unused_recv, stash_h, stash_y = lax.fori_loop(
        0, ticks, forward_tick, (blank, stash_h, stash_y)
    )
    stash_s = jnp.zeros((mbs + 1, LSLOT, rows_dev, width), jnp.bfloat16)

    def backward_tick(tick, carry):
        received, saved_s = carry
        micro = tick - (segments - 1 - me_segment)
        live = (micro >= 0) & (micro < mbs)
        place_at = jnp.clip(micro, 0, mbs - 1)
        top = lax.dynamic_index_in_dim(cotangent, place_at, 0, keepdims=False)
        grad_in = jnp.where(me_segment == segments - 1, top, received)
        layer_y = lax.dynamic_index_in_dim(stash_y, place_at, 0, keepdims=False)

        def run_back(grad):
            s_parts = [None] * LSLOT
            for layer in reversed(range(LSLOT)):
                grad, s_parts[layer] = layer_backward(grad, layer_y[layer], weights, layer, idx[layer])
            return (grad, jnp.stack(s_parts))

        def skip_back(grad):
            return (grad, jnp.zeros((LSLOT, rows_dev, width), jnp.bfloat16))

        grad_out, s_all = lax.cond(live, run_back, skip_back, grad_in)
        saved_s = lax.dynamic_update_index_in_dim(saved_s, s_all, jnp.where(live, place_at, mbs), 0)
        received = shifted(grad_out, "segment", -1)
        return (received, saved_s)

    unused_grad, stash_s = lax.fori_loop(0, ticks, backward_tick, (blank, stash_s))
    dws = []
    for layer in range(LSLOT):
        h_all = stash_h[:mbs, layer].reshape(mbs * rows_dev, width)
        s_all = stash_s[:mbs, layer].reshape(mbs * rows_dev, width)
        dws.append(layer_dw(h_all, s_all, idx[layer]))
    acc = jnp.concatenate(dws, axis=0).astype(jnp.bfloat16)
    return lax.psum_scatter(acc, "dp", scatter_dimension=0, tiled=True).astype(jnp.float32)


def solution(mesh):
    return jax.shard_map(
        on_device,
        mesh=mesh,
        in_specs=(
            P(None, "dp", None),
            P(None, "dp", None),
            P("segment", None, None),
            P("segment", None),
        ),
        out_specs=P(("segment", "dp"), None, None),
        check_vma=False,
    )
```

```python
import functools

import jax
import jax.numpy as jnp
from jax import lax
from jax.experimental import pallas as pl
from jax.experimental.pallas import tpu as pltpu
from jax.sharding import PartitionSpec as P

BLK = 128
LSLOT = 2
KMAX = 128
CH = 512
NSUB = 16
VMEM_LIMIT = 60 * 1024 * 1024

_SMEM = pl.BlockSpec(memory_space=pltpu.SMEM)
_VMEM = pl.BlockSpec(memory_space=pltpu.VMEM)
_ANY = pl.BlockSpec(memory_space=pl.ANY)


def shifted(value, axis, steps):
    count = lax.axis_size(axis)
    leading, last = (max(0, -steps), min(count, count - steps))
    return lax.ppermute(value, axis, [(source, source + steps) for source in range(leading, last)])


def _blk(i):
    return pl.ds(pl.multiple_of(i * BLK, BLK), BLK)


def _chunk(j):
    return pl.ds(pl.multiple_of(j * CH, CH), CH)


def _flag(idx_ref, k):
    return jnp.where(idx_ref[3 * k + 2] > 0, 1.0, 0.0).astype(jnp.float32)


def _w_copies(w_hbm, base, w_vmem, sems):
    copies = []
    for j in range(w_vmem.shape[0] // NSUB):
        copy = pltpu.make_async_copy(
            w_hbm.at[pl.ds(base + j * NSUB, NSUB)], w_vmem.at[pl.ds(j * NSUB, NSUB)], sems.at[j]
        )
        copy.start()
        copies.append(copy)
    return copies


def _slot_chunks(idx_ref, copies, body):
    for j, copy in enumerate(copies):
        copy.wait()

        @pl.when(idx_ref[3 * j * NSUB + 2] > 0)
        def _():
            for k in range(j * NSUB, (j + 1) * NSUB):
                body(k)


def _fwd_kernel(base, idx_ref, h_ref, w_hbm, hout_ref, y_ref, w_vmem, sems):
    width = h_ref.shape[1]
    copies = _w_copies(w_hbm, base, w_vmem, sems)
    y_ref[...] = jnp.zeros_like(y_ref)

    def body(k):
        r = idx_ref[3 * k]
        c = idx_ref[3 * k + 1]
        p = jnp.dot(h_ref[:, _blk(r)], w_vmem[k], preferred_element_type=jnp.float32)
        y_ref[:, _blk(c)] += p * _flag(idx_ref, k)

    _slot_chunks(idx_ref, copies, body)

    def epi(j, carry):
        y = y_ref[:, _chunk(j)]
        h = h_ref[:, _chunk(j)].astype(jnp.float32)
        hout_ref[:, _chunk(j)] = (h + y / (1.0 + jnp.exp(-y))).astype(hout_ref.dtype)
        return carry

    lax.fori_loop(0, width // CH, epi, 0)


def layer_forward(h, weights, layer, il):
    rows, width = h.shape
    return pl.pallas_call(
        functools.partial(_fwd_kernel, layer * KMAX),
        out_shape=(
            jax.ShapeDtypeStruct((rows, width), jnp.bfloat16),
            jax.ShapeDtypeStruct((rows, width), jnp.float32),
        ),
        in_specs=[_SMEM, _VMEM, _ANY],
        out_specs=(_VMEM, _VMEM),
        scratch_shapes=[
            pltpu.VMEM((KMAX, BLK, BLK), weights.dtype),
            pltpu.SemaphoreType.DMA((KMAX // NSUB,)),
        ],
        compiler_params=pltpu.CompilerParams(vmem_limit_bytes=VMEM_LIMIT),
    )(il.reshape(-1), h, weights)


def _bwd_kernel(base, idx_ref, g_ref, y_ref, w_hbm, gout_ref, s_ref, sp_ref, w_vmem, sems):
    width = g_ref.shape[1]
    copies = _w_copies(w_hbm, base, w_vmem, sems)

    def pre(j, carry):
        y = y_ref[:, _chunk(j)]
        sig = 1.0 / (1.0 + jnp.exp(-y))
        g = g_ref[:, _chunk(j)].astype(jnp.float32)
        s_ref[:, _chunk(j)] = (g * sig * (1.0 + y * (1.0 - sig))).astype(s_ref.dtype)
        sp_ref[:, _chunk(j)] = jnp.zeros((g_ref.shape[0], CH), jnp.float32)
        return carry

    lax.fori_loop(0, width // CH, pre, 0)

    def body(k):
        r = idx_ref[3 * k]
        c = idx_ref[3 * k + 1]
        back = lax.dot_general(
            s_ref[:, _blk(c)],
            w_vmem[k],
            (((1,), (1,)), ((), ())),
            preferred_element_type=jnp.float32,
        )
        sp_ref[:, _blk(r)] += back * _flag(idx_ref, k)

    _slot_chunks(idx_ref, copies, body)

    def epi(j, carry):
        g = g_ref[:, _chunk(j)].astype(jnp.float32)
        gout_ref[:, _chunk(j)] = (g + sp_ref[:, _chunk(j)]).astype(gout_ref.dtype)
        return carry

    lax.fori_loop(0, width // CH, epi, 0)


def layer_backward(g, y, weights, layer, il):
    rows, width = g.shape
    return pl.pallas_call(
        functools.partial(_bwd_kernel, layer * KMAX),
        out_shape=(
            jax.ShapeDtypeStruct((rows, width), jnp.bfloat16),
            jax.ShapeDtypeStruct((rows, width), jnp.bfloat16),
        ),
        in_specs=[_SMEM, _VMEM, _VMEM, _ANY],
        out_specs=(_VMEM, _VMEM),
        scratch_shapes=[
            pltpu.VMEM((rows, width), jnp.float32),
            pltpu.VMEM((KMAX, BLK, BLK), weights.dtype),
            pltpu.SemaphoreType.DMA((KMAX // NSUB,)),
        ],
        compiler_params=pltpu.CompilerParams(vmem_limit_bytes=VMEM_LIMIT),
    )(il.reshape(-1), g, y, weights)


def _dw_kernel(mbs, idx_ref, h_ref, s_ref, dw_ref):
    for j in range(dw_ref.shape[0] // NSUB):
        layer = j * NSUB // KMAX

        @pl.when(idx_ref[3 * j * NSUB + 2] > 0)
        def _():
            for k in range(j * NSUB, (j + 1) * NSUB):
                r = idx_ref[3 * k]
                c = idx_ref[3 * k + 1]
                total = None
                for m in range(mbs):
                    part = lax.dot_general(
                        h_ref[m, layer, :, _blk(r)],
                        s_ref[m, layer, :, _blk(c)],
                        (((0,), (0,)), ((), ())),
                        preferred_element_type=jnp.float32,
                    )
                    total = part if total is None else total + part
                dw_ref[k] = total * _flag(idx_ref, k)

        @pl.when(idx_ref[3 * j * NSUB + 2] <= 0)
        def _():
            dw_ref[pl.ds(j * NSUB, NSUB)] = jnp.zeros((NSUB, BLK, BLK), jnp.float32)


def segment_dw(stash_h, stash_s, block_index, mbs):
    return pl.pallas_call(
        functools.partial(_dw_kernel, mbs),
        out_shape=jax.ShapeDtypeStruct((block_index.shape[0], BLK, BLK), jnp.float32),
        in_specs=[_SMEM, _VMEM, _VMEM],
        out_specs=_VMEM,
        compiler_params=pltpu.CompilerParams(vmem_limit_bytes=VMEM_LIMIT),
    )(block_index.reshape(-1), stash_h, stash_s)


def _exchange(send, pairs):
    return lax.ppermute(send.astype(jnp.bfloat16), "dp", pairs).astype(jnp.float32)


def dp_reduce_scatter(acc):
    n = lax.axis_size("dp")
    if n != 8:
        return lax.psum_scatter(
            acc.astype(jnp.bfloat16), "dp", scatter_dimension=0, tiled=True
        ).astype(jnp.float32)
    d = lax.axis_index("dp")
    d0, d1, d2 = d % 2, (d // 2) % 2, d // 4
    pick = lambda a, i, axis: lax.dynamic_index_in_dim(a, i, axis, keepdims=False)
    x = acc.reshape((2, 2, 2, acc.shape[0] // 8) + acc.shape[1:])
    x = pick(x, d0, 2) + _exchange(pick(x, 1 - d0, 2), [(i, i ^ 1) for i in range(8)])
    core0 = d0 == 0
    keep = jnp.where(core0, pick(x, d1, 1), pick(x, d2, 0))
    send = jnp.where(core0, pick(x, 1 - d1, 1), pick(x, 1 - d2, 0))
    x = keep + _exchange(send, [(i, i ^ (2 if i % 2 == 0 else 4)) for i in range(8)])
    rem = jnp.where(core0, d2, d1)
    send = pick(x, 1 - rem, 0)
    return pick(x, rem, 0) + _exchange(send, [(i, i ^ (4 if i % 2 == 0 else 2)) for i in range(8)])


def on_device(x_in, cotangent, weights, block_index):
    segments = lax.axis_size("segment")
    me_segment = lax.axis_index("segment")
    mbs, rows_dev, width = x_in.shape
    idx = block_index.reshape(LSLOT, KMAX, 3)
    ticks = mbs + segments - 1

    def segment_forward(start):
        h = start
        inputs = []
        preacts = []
        for layer in range(LSLOT):
            h_next, y = layer_forward(h, weights, layer, idx[layer])
            inputs.append(h)
            preacts.append(y)
            h = h_next
        return (h, jnp.stack(inputs), jnp.stack(preacts))

    def skip_forward(start):
        return (
            start,
            jnp.zeros((LSLOT, rows_dev, width), jnp.bfloat16),
            jnp.zeros((LSLOT, rows_dev, width), jnp.float32),
        )

    stash_h = jnp.zeros((mbs + 1, LSLOT, rows_dev, width), jnp.bfloat16)
    stash_y = jnp.zeros((mbs + 1, LSLOT, rows_dev, width), jnp.float32)

    def forward_tick(tick, carry):
        received, saved_h, saved_y = carry
        micro = tick - me_segment
        live = (micro >= 0) & (micro < mbs)
        place_at = jnp.clip(micro, 0, mbs - 1)
        first = lax.dynamic_index_in_dim(x_in, place_at, 0, keepdims=False)
        start = jnp.where(me_segment == 0, first, received)
        h_out, inputs, preacts = lax.cond(live, segment_forward, skip_forward, start)
        store_at = jnp.where(live, place_at, mbs)
        saved_h = lax.dynamic_update_index_in_dim(saved_h, inputs, store_at, 0)
        saved_y = lax.dynamic_update_index_in_dim(saved_y, preacts, store_at, 0)
        received = shifted(h_out, "segment", 1)
        return (received, saved_h, saved_y)

    blank = jnp.zeros((rows_dev, width), jnp.bfloat16)
    unused_recv, stash_h, stash_y = lax.fori_loop(
        0, ticks, forward_tick, (blank, stash_h, stash_y)
    )
    stash_s = jnp.zeros((mbs + 1, LSLOT, rows_dev, width), jnp.bfloat16)

    def backward_tick(tick, carry):
        received, saved_s = carry
        micro = tick - (segments - 1 - me_segment)
        live = (micro >= 0) & (micro < mbs)
        place_at = jnp.clip(micro, 0, mbs - 1)
        top = lax.dynamic_index_in_dim(cotangent, place_at, 0, keepdims=False)
        grad_in = jnp.where(me_segment == segments - 1, top, received)
        layer_y = lax.dynamic_index_in_dim(stash_y, place_at, 0, keepdims=False)

        def run_back(grad):
            s_parts = [None] * LSLOT
            for layer in reversed(range(LSLOT)):
                grad, s_parts[layer] = layer_backward(grad, layer_y[layer], weights, layer, idx[layer])
            return (grad, jnp.stack(s_parts))

        def skip_back(grad):
            return (grad, jnp.zeros((LSLOT, rows_dev, width), jnp.bfloat16))

        grad_out, s_all = lax.cond(live, run_back, skip_back, grad_in)
        saved_s = lax.dynamic_update_index_in_dim(saved_s, s_all, jnp.where(live, place_at, mbs), 0)
        received = shifted(grad_out, "segment", -1)
        return (received, saved_s)

    unused_grad, stash_s = lax.fori_loop(0, ticks, backward_tick, (blank, stash_s))
    acc = segment_dw(stash_h, stash_s, block_index, mbs)
    return dp_reduce_scatter(acc)


def solution(mesh):
    return jax.shard_map(
        on_device,
        mesh=mesh,
        in_specs=(
            P(None, "dp", None),
            P(None, "dp", None),
            P("segment", None, None),
            P("segment", None),
        ),
        out_specs=P(("segment", "dp"), None, None),
        check_vma=False,
    )
```

```python
import functools

import jax
import jax.numpy as jnp
from jax import lax
from jax.experimental import pallas as pl
from jax.experimental.pallas import tpu as pltpu
from jax.sharding import PartitionSpec as P

BLK = 128
LSLOT = 2
KMAX = 128
CH = 512
NSUB = 16
VMEM_LIMIT = 60 * 1024 * 1024

_SMEM = pl.BlockSpec(memory_space=pltpu.SMEM)
_VMEM = pl.BlockSpec(memory_space=pltpu.VMEM)
_ANY = pl.BlockSpec(memory_space=pl.ANY)


def shifted(value, axis, steps):
    count = lax.axis_size(axis)
    leading, last = (max(0, -steps), min(count, count - steps))
    return lax.ppermute(value, axis, [(source, source + steps) for source in range(leading, last)])


def _blk(i):
    return pl.ds(pl.multiple_of(i * BLK, BLK), BLK)


def _chunk(j):
    return pl.ds(pl.multiple_of(j * CH, CH), CH)


def _flag(idx_ref, k):
    return jnp.where(idx_ref[3 * k + 2] > 0, 1.0, 0.0).astype(jnp.float32)


def _w_copies(w_hbm, base, w_vmem, sems):
    copies = []
    for j in range(w_vmem.shape[0] // NSUB):
        copy = pltpu.make_async_copy(
            w_hbm.at[pl.ds(base + j * NSUB, NSUB)], w_vmem.at[pl.ds(j * NSUB, NSUB)], sems.at[j]
        )
        copy.start()
        copies.append(copy)
    return copies


def _slot_chunks(idx_ref, base, copies, body):
    for j, copy in enumerate(copies):
        copy.wait()

        @pl.when(idx_ref[3 * (base + j * NSUB) + 2] > 0)
        def _():
            for k in range(j * NSUB, (j + 1) * NSUB):
                body(k)


def _fwd_kernel(base, layer, at_ref, idx_ref, h_ref, w_hbm, sh_in, sy_in, hout_ref, sh_ref, sy_ref, w_vmem, y_vmem, sems, io_sems):
    del sh_in, sy_in
    width = h_ref.shape[1]
    at = at_ref[0]
    copies = _w_copies(w_hbm, base, w_vmem, sems)
    save_h = pltpu.make_async_copy(h_ref, sh_ref.at[at, layer], io_sems.at[0])
    save_h.start()
    y_vmem[...] = jnp.zeros_like(y_vmem)

    def body(k):
        r = idx_ref[3 * (base + k)]
        c = idx_ref[3 * (base + k) + 1]
        p = jnp.dot(h_ref[:, _blk(r)], w_vmem[k], preferred_element_type=jnp.float32)
        y_vmem[:, _blk(c)] += p * _flag(idx_ref, base + k)

    _slot_chunks(idx_ref, base, copies, body)
    save_y = pltpu.make_async_copy(y_vmem, sy_ref.at[at, layer], io_sems.at[1])
    save_y.start()

    def epi(j, carry):
        y = y_vmem[:, _chunk(j)]
        h = h_ref[:, _chunk(j)].astype(jnp.float32)
        hout_ref[:, _chunk(j)] = (h + y / (1.0 + jnp.exp(-y))).astype(hout_ref.dtype)
        return carry

    lax.fori_loop(0, width // CH, epi, 0)
    save_h.wait()
    save_y.wait()


def layer_forward(h, weights, layer, block_index, at, stash_h, stash_y):
    rows, width = h.shape
    return pl.pallas_call(
        functools.partial(_fwd_kernel, layer * KMAX, layer),
        out_shape=(
            jax.ShapeDtypeStruct((rows, width), jnp.bfloat16),
            jax.ShapeDtypeStruct(stash_h.shape, stash_h.dtype),
            jax.ShapeDtypeStruct(stash_y.shape, stash_y.dtype),
        ),
        in_specs=[_SMEM, _SMEM, _VMEM, _ANY, _ANY, _ANY],
        out_specs=(_VMEM, _ANY, _ANY),
        scratch_shapes=[
            pltpu.VMEM((KMAX, BLK, BLK), weights.dtype),
            pltpu.VMEM((rows, width), jnp.float32),
            pltpu.SemaphoreType.DMA((KMAX // NSUB,)),
            pltpu.SemaphoreType.DMA((2,)),
        ],
        input_output_aliases={4: 1, 5: 2},
        compiler_params=pltpu.CompilerParams(vmem_limit_bytes=VMEM_LIMIT),
    )(at.reshape(1), block_index.reshape(-1), h, weights, stash_h, stash_y)


def _bwd_kernel(base, layer, at_ref, idx_ref, g_ref, sy_hbm, w_hbm, ss_in, gout_ref, ss_ref, y_vmem, s_vmem, sp_ref, w_vmem, sems, io_sems):
    del ss_in
    width = g_ref.shape[1]
    at = at_ref[0]
    load_y = pltpu.make_async_copy(sy_hbm.at[at, layer], y_vmem, io_sems.at[0])
    load_y.start()
    copies = _w_copies(w_hbm, base, w_vmem, sems)
    load_y.wait()

    def pre(j, carry):
        y = y_vmem[:, _chunk(j)]
        sig = 1.0 / (1.0 + jnp.exp(-y))
        g = g_ref[:, _chunk(j)].astype(jnp.float32)
        s_vmem[:, _chunk(j)] = (g * sig * (1.0 + y * (1.0 - sig))).astype(s_vmem.dtype)
        sp_ref[:, _chunk(j)] = jnp.zeros((g_ref.shape[0], CH), jnp.float32)
        return carry

    lax.fori_loop(0, width // CH, pre, 0)
    save_s = pltpu.make_async_copy(s_vmem, ss_ref.at[at, layer], io_sems.at[1])
    save_s.start()

    def body(k):
        r = idx_ref[3 * (base + k)]
        c = idx_ref[3 * (base + k) + 1]
        back = lax.dot_general(
            s_vmem[:, _blk(c)],
            w_vmem[k],
            (((1,), (1,)), ((), ())),
            preferred_element_type=jnp.float32,
        )
        sp_ref[:, _blk(r)] += back * _flag(idx_ref, base + k)

    _slot_chunks(idx_ref, base, copies, body)

    def epi(j, carry):
        g = g_ref[:, _chunk(j)].astype(jnp.float32)
        gout_ref[:, _chunk(j)] = (g + sp_ref[:, _chunk(j)]).astype(gout_ref.dtype)
        return carry

    lax.fori_loop(0, width // CH, epi, 0)
    save_s.wait()


def layer_backward(g, stash_y, weights, layer, block_index, at, stash_s):
    rows, width = g.shape
    return pl.pallas_call(
        functools.partial(_bwd_kernel, layer * KMAX, layer),
        out_shape=(
            jax.ShapeDtypeStruct((rows, width), jnp.bfloat16),
            jax.ShapeDtypeStruct(stash_s.shape, stash_s.dtype),
        ),
        in_specs=[_SMEM, _SMEM, _VMEM, _ANY, _ANY, _ANY],
        out_specs=(_VMEM, _ANY),
        scratch_shapes=[
            pltpu.VMEM((rows, width), jnp.float32),
            pltpu.VMEM((rows, width), jnp.bfloat16),
            pltpu.VMEM((rows, width), jnp.float32),
            pltpu.VMEM((KMAX, BLK, BLK), weights.dtype),
            pltpu.SemaphoreType.DMA((KMAX // NSUB,)),
            pltpu.SemaphoreType.DMA((2,)),
        ],
        input_output_aliases={5: 1},
        compiler_params=pltpu.CompilerParams(vmem_limit_bytes=VMEM_LIMIT),
    )(at.reshape(1), block_index.reshape(-1), g, stash_y, weights, stash_s)


def _dw_kernel(mbs, idx_ref, h_ref, s_ref, dw_ref):
    for j in range(dw_ref.shape[0] // NSUB):
        layer = j * NSUB // KMAX

        @pl.when(idx_ref[3 * j * NSUB + 2] > 0)
        def _():
            for k in range(j * NSUB, (j + 1) * NSUB):
                r = idx_ref[3 * k]
                c = idx_ref[3 * k + 1]
                total = None
                for m in range(mbs):
                    part = lax.dot_general(
                        h_ref[m, layer, :, _blk(r)],
                        s_ref[m, layer, :, _blk(c)],
                        (((0,), (0,)), ((), ())),
                        preferred_element_type=jnp.float32,
                    )
                    total = part if total is None else total + part
                dw_ref[k] = total * _flag(idx_ref, k)

        @pl.when(idx_ref[3 * j * NSUB + 2] <= 0)
        def _():
            dw_ref[pl.ds(j * NSUB, NSUB)] = jnp.zeros((NSUB, BLK, BLK), jnp.float32)


def segment_dw(stash_h, stash_s, block_index, mbs):
    return pl.pallas_call(
        functools.partial(_dw_kernel, mbs),
        out_shape=jax.ShapeDtypeStruct((block_index.shape[0], BLK, BLK), jnp.float32),
        in_specs=[_SMEM, _VMEM, _VMEM],
        out_specs=_VMEM,
        compiler_params=pltpu.CompilerParams(vmem_limit_bytes=VMEM_LIMIT),
    )(block_index.reshape(-1), stash_h, stash_s)


def _exchange(send, pairs):
    return lax.ppermute(send.astype(jnp.bfloat16), "dp", pairs).astype(jnp.float32)


def dp_reduce_scatter(acc):
    n = lax.axis_size("dp")
    if n != 8:
        return lax.psum_scatter(
            acc.astype(jnp.bfloat16), "dp", scatter_dimension=0, tiled=True
        ).astype(jnp.float32)
    d = lax.axis_index("dp")
    d0, d1, d2 = d % 2, (d // 2) % 2, d // 4
    pick = lambda a, i, axis: lax.dynamic_index_in_dim(a, i, axis, keepdims=False)
    x = acc.reshape((2, 2, 2, acc.shape[0] // 8) + acc.shape[1:])
    x = pick(x, d0, 2) + _exchange(pick(x, 1 - d0, 2), [(i, i ^ 1) for i in range(8)])
    core0 = d0 == 0
    keep = jnp.where(core0, pick(x, d1, 1), pick(x, d2, 0))
    send = jnp.where(core0, pick(x, 1 - d1, 1), pick(x, 1 - d2, 0))
    x = keep + _exchange(send, [(i, i ^ (2 if i % 2 == 0 else 4)) for i in range(8)])
    rem = jnp.where(core0, d2, d1)
    send = pick(x, 1 - rem, 0)
    return pick(x, rem, 0) + _exchange(send, [(i, i ^ (4 if i % 2 == 0 else 2)) for i in range(8)])


def on_device(x_in, cotangent, weights, block_index):
    segments = lax.axis_size("segment")
    me_segment = lax.axis_index("segment")
    mbs, rows_dev, width = x_in.shape
    idx = block_index.reshape(LSLOT, KMAX, 3)
    ticks = mbs + segments - 1

    def forward_tick(tick, carry):
        received, saved_h, saved_y = carry
        micro = tick - me_segment
        live = (micro >= 0) & (micro < mbs)
        place_at = jnp.clip(micro, 0, mbs - 1)
        first = lax.dynamic_index_in_dim(x_in, place_at, 0, keepdims=False)
        start = jnp.where(me_segment == 0, first, received)

        def run(operands):
            h, sh, sy = operands
            for layer in range(LSLOT):
                h, sh, sy = layer_forward(h, weights, layer, block_index, place_at, sh, sy)
            return (h, sh, sy)

        h_out, saved_h, saved_y = lax.cond(live, run, lambda ops: ops, (start, saved_h, saved_y))
        received = shifted(h_out, "segment", 1)
        return (received, saved_h, saved_y)

    stash_h = jnp.zeros((mbs, LSLOT, rows_dev, width), jnp.bfloat16)
    stash_y = jnp.zeros((mbs, LSLOT, rows_dev, width), jnp.float32)
    blank = jnp.zeros((rows_dev, width), jnp.bfloat16)
    unused_recv, stash_h, stash_y = lax.fori_loop(
        0, ticks, forward_tick, (blank, stash_h, stash_y)
    )
    stash_s = jnp.zeros((mbs, LSLOT, rows_dev, width), jnp.bfloat16)

    def backward_tick(tick, carry):
        received, saved_s = carry
        micro = tick - (segments - 1 - me_segment)
        live = (micro >= 0) & (micro < mbs)
        place_at = jnp.clip(micro, 0, mbs - 1)
        top = lax.dynamic_index_in_dim(cotangent, place_at, 0, keepdims=False)
        grad_in = jnp.where(me_segment == segments - 1, top, received)

        def run(operands):
            grad, ss = operands
            for layer in reversed(range(LSLOT)):
                grad, ss = layer_backward(grad, stash_y, weights, layer, block_index, place_at, ss)
            return (grad, ss)

        grad_out, saved_s = lax.cond(live, run, lambda ops: ops, (grad_in, saved_s))
        received = shifted(grad_out, "segment", -1)
        return (received, saved_s)

    unused_grad, stash_s = lax.fori_loop(0, ticks, backward_tick, (blank, stash_s))
    acc = segment_dw(stash_h, stash_s, block_index, mbs)
    return dp_reduce_scatter(acc)


def solution(mesh):
    return jax.shard_map(
        on_device,
        mesh=mesh,
        in_specs=(
            P(None, "dp", None),
            P(None, "dp", None),
            P("segment", None, None),
            P("segment", None),
        ),
        out_specs=P(("segment", "dp"), None, None),
        check_vma=False,
    )
```

```python
import functools

import jax
import jax.numpy as jnp
from jax import lax
from jax.experimental import pallas as pl
from jax.experimental.pallas import tpu as pltpu
from jax.sharding import PartitionSpec as P

BLK = 128
LSLOT = 2
KMAX = 128
CH = 512
NSUB = 16
SPLIT = 2
VMEM_LIMIT = 60 * 1024 * 1024

_SMEM = pl.BlockSpec(memory_space=pltpu.SMEM)
_VMEM = pl.BlockSpec(memory_space=pltpu.VMEM)
_ANY = pl.BlockSpec(memory_space=pl.ANY)


def shifted(value, axis, steps):
    count = lax.axis_size(axis)
    leading, last = (max(0, -steps), min(count, count - steps))
    return lax.ppermute(value, axis, [(source, source + steps) for source in range(leading, last)])


def _blk(i):
    return pl.ds(pl.multiple_of(i * BLK, BLK), BLK)


def _chunk(j):
    return pl.ds(pl.multiple_of(j * CH, CH), CH)


def _flag(idx_ref, k):
    return jnp.where(idx_ref[3 * k + 2] > 0, 1.0, 0.0).astype(jnp.float32)


def _w_copies(w_hbm, base, w_vmem, sems):
    copies = []
    for j in range(w_vmem.shape[0] // NSUB):
        copy = pltpu.make_async_copy(
            w_hbm.at[pl.ds(base + j * NSUB, NSUB)], w_vmem.at[pl.ds(j * NSUB, NSUB)], sems.at[j]
        )
        copy.start()
        copies.append(copy)
    return copies


def _slot_chunks(idx_ref, base, copies, body):
    for j, copy in enumerate(copies):
        copy.wait()

        @pl.when(idx_ref[3 * (base + j * NSUB) + 2] > 0)
        def _():
            for k in range(j * NSUB, (j + 1) * NSUB):
                body(k)


def _fwd_kernel(base, layer, at_ref, idx_ref, h_ref, w_hbm, sh_in, sy_in, hout_ref, sh_ref, sy_ref, w_vmem, y_vmem, sems, io_sems):
    del sh_in, sy_in
    width = h_ref.shape[1]
    at = at_ref[0]
    copies = _w_copies(w_hbm, base, w_vmem, sems)
    save_h = pltpu.make_async_copy(h_ref, sh_ref.at[layer, at], io_sems.at[0])
    save_h.start()
    y_vmem[...] = jnp.zeros_like(y_vmem)

    def body(k):
        r = idx_ref[3 * (base + k)]
        c = idx_ref[3 * (base + k) + 1]
        p = jnp.dot(h_ref[:, _blk(r)], w_vmem[k], preferred_element_type=jnp.float32)
        y_vmem[:, _blk(c)] += p * _flag(idx_ref, base + k)

    _slot_chunks(idx_ref, base, copies, body)
    save_y = pltpu.make_async_copy(y_vmem, sy_ref.at[layer, at], io_sems.at[1])
    save_y.start()

    def epi(j, carry):
        y = y_vmem[:, _chunk(j)]
        h = h_ref[:, _chunk(j)].astype(jnp.float32)
        hout_ref[:, _chunk(j)] = (h + y / (1.0 + jnp.exp(-y))).astype(hout_ref.dtype)
        return carry

    lax.fori_loop(0, width // CH, epi, 0)
    save_h.wait()
    save_y.wait()


def layer_forward(h, weights, layer, block_index, at, stash_h, stash_y):
    rows, width = h.shape
    return pl.pallas_call(
        functools.partial(_fwd_kernel, layer * KMAX, layer),
        out_shape=(
            jax.ShapeDtypeStruct((rows, width), jnp.bfloat16),
            jax.ShapeDtypeStruct(stash_h.shape, stash_h.dtype),
            jax.ShapeDtypeStruct(stash_y.shape, stash_y.dtype),
        ),
        in_specs=[_SMEM, _SMEM, _VMEM, _ANY, _ANY, _ANY],
        out_specs=(_VMEM, _ANY, _ANY),
        scratch_shapes=[
            pltpu.VMEM((KMAX, BLK, BLK), weights.dtype),
            pltpu.VMEM((rows, width), jnp.float32),
            pltpu.SemaphoreType.DMA((KMAX // NSUB,)),
            pltpu.SemaphoreType.DMA((2,)),
        ],
        input_output_aliases={4: 1, 5: 2},
        compiler_params=pltpu.CompilerParams(vmem_limit_bytes=VMEM_LIMIT),
    )(at.reshape(1), block_index.reshape(-1), h, weights, stash_h, stash_y)


def _bwd_kernel(base, layer, at_ref, idx_ref, g_ref, sy_hbm, w_hbm, ss_in, gout_ref, ss_ref, y_vmem, s_vmem, sp_ref, w_vmem, sems, io_sems):
    del ss_in
    width = g_ref.shape[1]
    at = at_ref[0]
    load_y = pltpu.make_async_copy(sy_hbm.at[layer, at], y_vmem, io_sems.at[0])
    load_y.start()
    copies = _w_copies(w_hbm, base, w_vmem, sems)
    load_y.wait()

    def pre(j, carry):
        y = y_vmem[:, _chunk(j)]
        sig = 1.0 / (1.0 + jnp.exp(-y))
        g = g_ref[:, _chunk(j)].astype(jnp.float32)
        s_vmem[:, _chunk(j)] = (g * sig * (1.0 + y * (1.0 - sig))).astype(s_vmem.dtype)
        sp_ref[:, _chunk(j)] = jnp.zeros((g_ref.shape[0], CH), jnp.float32)
        return carry

    lax.fori_loop(0, width // CH, pre, 0)
    save_s = pltpu.make_async_copy(s_vmem, ss_ref.at[layer, at], io_sems.at[1])
    save_s.start()

    def body(k):
        r = idx_ref[3 * (base + k)]
        c = idx_ref[3 * (base + k) + 1]
        back = lax.dot_general(
            s_vmem[:, _blk(c)],
            w_vmem[k],
            (((1,), (1,)), ((), ())),
            preferred_element_type=jnp.float32,
        )
        sp_ref[:, _blk(r)] += back * _flag(idx_ref, base + k)

    _slot_chunks(idx_ref, base, copies, body)

    def epi(j, carry):
        g = g_ref[:, _chunk(j)].astype(jnp.float32)
        gout_ref[:, _chunk(j)] = (g + sp_ref[:, _chunk(j)]).astype(gout_ref.dtype)
        return carry

    lax.fori_loop(0, width // CH, epi, 0)
    save_s.wait()


def layer_backward(g, stash_y, weights, layer, block_index, at, stash_s):
    rows, width = g.shape
    return pl.pallas_call(
        functools.partial(_bwd_kernel, layer * KMAX, layer),
        out_shape=(
            jax.ShapeDtypeStruct((rows, width), jnp.bfloat16),
            jax.ShapeDtypeStruct(stash_s.shape, stash_s.dtype),
        ),
        in_specs=[_SMEM, _SMEM, _VMEM, _ANY, _ANY, _ANY],
        out_specs=(_VMEM, _ANY),
        scratch_shapes=[
            pltpu.VMEM((rows, width), jnp.float32),
            pltpu.VMEM((rows, width), jnp.bfloat16),
            pltpu.VMEM((rows, width), jnp.float32),
            pltpu.VMEM((KMAX, BLK, BLK), weights.dtype),
            pltpu.SemaphoreType.DMA((KMAX // NSUB,)),
            pltpu.SemaphoreType.DMA((2,)),
        ],
        input_output_aliases={5: 1},
        compiler_params=pltpu.CompilerParams(vmem_limit_bytes=VMEM_LIMIT),
    )(at.reshape(1), block_index.reshape(-1), g, stash_y, weights, stash_s)


def _dw_kernel(mbs, idx_ref, h_ref, s_ref, dw_ref):
    rows = h_ref.shape[1] * h_ref.shape[2]
    for j in range(dw_ref.shape[0] // NSUB):
        layer = j * NSUB // KMAX

        @pl.when(idx_ref[3 * j * NSUB + 2] > 0)
        def _():
            for k in range(j * NSUB, (j + 1) * NSUB):
                r = idx_ref[3 * k]
                c = idx_ref[3 * k + 1]
                hb = h_ref[layer, :, :, _blk(r)]
                sb = s_ref[layer, :, :, _blk(c)]
                dw_ref[k] = lax.dot_general(
                    hb.reshape(rows, BLK),
                    sb.reshape(rows, BLK),
                    (((0,), (0,)), ((), ())),
                    preferred_element_type=jnp.float32,
                ) * _flag(idx_ref, k)

        @pl.when(idx_ref[3 * j * NSUB + 2] <= 0)
        def _():
            dw_ref[pl.ds(j * NSUB, NSUB)] = jnp.zeros((NSUB, BLK, BLK), jnp.float32)


def segment_dw(stash_h, stash_s, block_index, mbs):
    return pl.pallas_call(
        functools.partial(_dw_kernel, mbs),
        out_shape=jax.ShapeDtypeStruct((block_index.shape[0], BLK, BLK), jnp.float32),
        in_specs=[_SMEM, _VMEM, _VMEM],
        out_specs=_VMEM,
        compiler_params=pltpu.CompilerParams(vmem_limit_bytes=VMEM_LIMIT),
    )(block_index.reshape(-1), stash_h, stash_s)


def _exchange(send, pairs):
    return lax.ppermute(send.astype(jnp.bfloat16), "dp", pairs).astype(jnp.float32)


def dp_reduce_scatter(acc):
    n = lax.axis_size("dp")
    if n != 8:
        return lax.psum_scatter(
            acc.astype(jnp.bfloat16), "dp", scatter_dimension=0, tiled=True
        ).astype(jnp.float32)
    d = lax.axis_index("dp")
    d0, d1, d2 = d % 2, (d // 2) % 2, d // 4
    pick = lambda a, i, axis: lax.dynamic_index_in_dim(a, i, axis, keepdims=False)
    x = acc.reshape((2, 2, 2, acc.shape[0] // 8) + acc.shape[1:])
    x = pick(x, d0, 2) + _exchange(pick(x, 1 - d0, 2), [(i, i ^ 1) for i in range(8)])
    core0 = d0 == 0
    keep = jnp.where(core0, pick(x, d1, 1), pick(x, d2, 0))
    send = jnp.where(core0, pick(x, 1 - d1, 1), pick(x, 1 - d2, 0))
    x = keep + _exchange(send, [(i, i ^ (2 if i % 2 == 0 else 4)) for i in range(8)])
    rem = jnp.where(core0, d2, d1)
    send = pick(x, 1 - rem, 0)
    return pick(x, rem, 0) + _exchange(send, [(i, i ^ (4 if i % 2 == 0 else 2)) for i in range(8)])


def on_device(x_in, cotangent, weights, block_index):
    segments = lax.axis_size("segment")
    me_segment = lax.axis_index("segment")
    mbs, rows_dev, width = x_in.shape
    mbs, rows_dev = mbs * SPLIT, rows_dev // SPLIT
    x_in = x_in.reshape(mbs, rows_dev, width)
    cotangent = cotangent.reshape(mbs, rows_dev, width)
    idx = block_index.reshape(LSLOT, KMAX, 3)
    ticks = mbs + segments - 1

    def forward_tick(tick, carry):
        received, saved_h, saved_y = carry
        micro = tick - me_segment
        live = (micro >= 0) & (micro < mbs)
        place_at = jnp.clip(micro, 0, mbs - 1)
        first = lax.dynamic_index_in_dim(x_in, place_at, 0, keepdims=False)
        start = jnp.where(me_segment == 0, first, received)

        def run(operands):
            h, sh, sy = operands
            for layer in range(LSLOT):
                h, sh, sy = layer_forward(h, weights, layer, block_index, place_at, sh, sy)
            return (h, sh, sy)

        h_out, saved_h, saved_y = lax.cond(live, run, lambda ops: ops, (start, saved_h, saved_y))
        received = shifted(h_out, "segment", 1)
        return (received, saved_h, saved_y)

    stash_h = jnp.zeros((LSLOT, mbs, rows_dev, width), jnp.bfloat16)
    stash_y = jnp.zeros((LSLOT, mbs, rows_dev, width), jnp.float32)
    blank = jnp.zeros((rows_dev, width), jnp.bfloat16)
    unused_recv, stash_h, stash_y = lax.fori_loop(
        0, ticks, forward_tick, (blank, stash_h, stash_y)
    )
    stash_s = jnp.zeros((LSLOT, mbs, rows_dev, width), jnp.bfloat16)

    def backward_tick(tick, carry):
        received, saved_s = carry
        micro = tick - (segments - 1 - me_segment)
        live = (micro >= 0) & (micro < mbs)
        place_at = jnp.clip(micro, 0, mbs - 1)
        top = lax.dynamic_index_in_dim(cotangent, place_at, 0, keepdims=False)
        grad_in = jnp.where(me_segment == segments - 1, top, received)

        def run(operands):
            grad, ss = operands
            for layer in reversed(range(LSLOT)):
                grad, ss = layer_backward(grad, stash_y, weights, layer, block_index, place_at, ss)
            return (grad, ss)

        grad_out, saved_s = lax.cond(live, run, lambda ops: ops, (grad_in, saved_s))
        received = shifted(grad_out, "segment", -1)
        return (received, saved_s)

    unused_grad, stash_s = lax.fori_loop(0, ticks, backward_tick, (blank, stash_s))
    acc = segment_dw(stash_h, stash_s, block_index, mbs)
    return dp_reduce_scatter(acc)


def solution(mesh):
    return jax.shard_map(
        on_device,
        mesh=mesh,
        in_specs=(
            P(None, "dp", None),
            P(None, "dp", None),
            P("segment", None, None),
            P("segment", None),
        ),
        out_specs=P(("segment", "dp"), None, None),
        check_vma=False,
    )
```

```python
import functools

import jax
import jax.numpy as jnp
from jax import lax
from jax.experimental import pallas as pl
from jax.experimental.pallas import tpu as pltpu
from jax.sharding import PartitionSpec as P

BLK = 128
LSLOT = 2
KMAX = 128
CH = 512
NSUB = 16
SPLIT = 2
GROUP = 8
VMEM_LIMIT = 60 * 1024 * 1024

_SMEM = pl.BlockSpec(memory_space=pltpu.SMEM)
_VMEM = pl.BlockSpec(memory_space=pltpu.VMEM)
_ANY = pl.BlockSpec(memory_space=pl.ANY)


def shifted(value, axis, steps):
    count = lax.axis_size(axis)
    leading, last = (max(0, -steps), min(count, count - steps))
    return lax.ppermute(value, axis, [(source, source + steps) for source in range(leading, last)])


def _blk(i):
    return pl.ds(pl.multiple_of(i * BLK, BLK), BLK)


def _chunk(j):
    return pl.ds(pl.multiple_of(j * CH, CH), CH)


def _flag(idx_ref, k):
    return jnp.where(idx_ref[3 * k + 2] > 0, 1.0, 0.0).astype(jnp.float32)


def _w_copies(w_hbm, base, w_vmem, sems):
    copies = []
    for j in range(w_vmem.shape[0] // NSUB):
        copy = pltpu.make_async_copy(
            w_hbm.at[pl.ds(base + j * NSUB, NSUB)], w_vmem.at[pl.ds(j * NSUB, NSUB)], sems.at[j]
        )
        copy.start()
        copies.append(copy)
    return copies


def _slot_chunks(idx_ref, base, copies, product, update):
    for j, copy in enumerate(copies):
        copy.wait()

        @pl.when(idx_ref[3 * (base + j * NSUB) + 2] > 0)
        def _():
            for g in range(j * NSUB, (j + 1) * NSUB, GROUP):
                parts = [product(k) for k in range(g, g + GROUP)]
                for k, part in zip(range(g, g + GROUP), parts):
                    update(k, part)


def _fwd_kernel(base, layer, at_ref, idx_ref, h_ref, w_hbm, sh_in, sy_in, hout_ref, sh_ref, sy_ref, w_vmem, y_vmem, sems, io_sems):
    del sh_in, sy_in
    width = h_ref.shape[1]
    at = at_ref[0]
    copies = _w_copies(w_hbm, base, w_vmem, sems)
    save_h = pltpu.make_async_copy(h_ref, sh_ref.at[layer, at], io_sems.at[0])
    save_h.start()
    y_vmem[...] = jnp.zeros_like(y_vmem)

    def product(k):
        r = idx_ref[3 * (base + k)]
        return jnp.dot(h_ref[:, _blk(r)], w_vmem[k], preferred_element_type=jnp.float32)

    def update(k, p):
        c = idx_ref[3 * (base + k) + 1]
        y_vmem[:, _blk(c)] += p * _flag(idx_ref, base + k)

    _slot_chunks(idx_ref, base, copies, product, update)
    save_y = pltpu.make_async_copy(y_vmem, sy_ref.at[layer, at], io_sems.at[1])
    save_y.start()

    def epi(j, carry):
        y = y_vmem[:, _chunk(j)]
        h = h_ref[:, _chunk(j)].astype(jnp.float32)
        hout_ref[:, _chunk(j)] = (h + y / (1.0 + jnp.exp(-y))).astype(hout_ref.dtype)
        return carry

    lax.fori_loop(0, width // CH, epi, 0)
    save_h.wait()
    save_y.wait()


def layer_forward(h, weights, layer, block_index, at, stash_h, stash_y):
    rows, width = h.shape
    return pl.pallas_call(
        functools.partial(_fwd_kernel, layer * KMAX, layer),
        out_shape=(
            jax.ShapeDtypeStruct((rows, width), jnp.bfloat16),
            jax.ShapeDtypeStruct(stash_h.shape, stash_h.dtype),
            jax.ShapeDtypeStruct(stash_y.shape, stash_y.dtype),
        ),
        in_specs=[_SMEM, _SMEM, _VMEM, _ANY, _ANY, _ANY],
        out_specs=(_VMEM, _ANY, _ANY),
        scratch_shapes=[
            pltpu.VMEM((KMAX, BLK, BLK), weights.dtype),
            pltpu.VMEM((rows, width), jnp.float32),
            pltpu.SemaphoreType.DMA((KMAX // NSUB,)),
            pltpu.SemaphoreType.DMA((2,)),
        ],
        input_output_aliases={4: 1, 5: 2},
        compiler_params=pltpu.CompilerParams(vmem_limit_bytes=VMEM_LIMIT),
    )(at.reshape(1), block_index.reshape(-1), h, weights, stash_h, stash_y)


def _bwd_kernel(base, layer, at_ref, idx_ref, g_ref, sy_hbm, w_hbm, ss_in, gout_ref, ss_ref, y_vmem, s_vmem, sp_ref, w_vmem, sems, io_sems):
    del ss_in
    width = g_ref.shape[1]
    at = at_ref[0]
    load_y = pltpu.make_async_copy(sy_hbm.at[layer, at], y_vmem, io_sems.at[0])
    load_y.start()
    copies = _w_copies(w_hbm, base, w_vmem, sems)
    load_y.wait()

    def pre(j, carry):
        y = y_vmem[:, _chunk(j)]
        sig = 1.0 / (1.0 + jnp.exp(-y))
        g = g_ref[:, _chunk(j)].astype(jnp.float32)
        s_vmem[:, _chunk(j)] = (g * sig * (1.0 + y * (1.0 - sig))).astype(s_vmem.dtype)
        sp_ref[:, _chunk(j)] = jnp.zeros((g_ref.shape[0], CH), jnp.float32)
        return carry

    lax.fori_loop(0, width // CH, pre, 0)
    save_s = pltpu.make_async_copy(s_vmem, ss_ref.at[layer, at], io_sems.at[1])
    save_s.start()

    def product(k):
        c = idx_ref[3 * (base + k) + 1]
        return lax.dot_general(
            s_vmem[:, _blk(c)],
            w_vmem[k],
            (((1,), (1,)), ((), ())),
            preferred_element_type=jnp.float32,
        )

    def update(k, back):
        r = idx_ref[3 * (base + k)]
        sp_ref[:, _blk(r)] += back * _flag(idx_ref, base + k)

    _slot_chunks(idx_ref, base, copies, product, update)

    def epi(j, carry):
        g = g_ref[:, _chunk(j)].astype(jnp.float32)
        gout_ref[:, _chunk(j)] = (g + sp_ref[:, _chunk(j)]).astype(gout_ref.dtype)
        return carry

    lax.fori_loop(0, width // CH, epi, 0)
    save_s.wait()


def layer_backward(g, stash_y, weights, layer, block_index, at, stash_s):
    rows, width = g.shape
    return pl.pallas_call(
        functools.partial(_bwd_kernel, layer * KMAX, layer),
        out_shape=(
            jax.ShapeDtypeStruct((rows, width), jnp.bfloat16),
            jax.ShapeDtypeStruct(stash_s.shape, stash_s.dtype),
        ),
        in_specs=[_SMEM, _SMEM, _VMEM, _ANY, _ANY, _ANY],
        out_specs=(_VMEM, _ANY),
        scratch_shapes=[
            pltpu.VMEM((rows, width), jnp.float32),
            pltpu.VMEM((rows, width), jnp.bfloat16),
            pltpu.VMEM((rows, width), jnp.float32),
            pltpu.VMEM((KMAX, BLK, BLK), weights.dtype),
            pltpu.SemaphoreType.DMA((KMAX // NSUB,)),
            pltpu.SemaphoreType.DMA((2,)),
        ],
        input_output_aliases={5: 1},
        compiler_params=pltpu.CompilerParams(vmem_limit_bytes=VMEM_LIMIT),
    )(at.reshape(1), block_index.reshape(-1), g, stash_y, weights, stash_s)


def _dw_kernel(mbs, idx_ref, h_ref, s_ref, dw_ref):
    rows = h_ref.shape[1] * h_ref.shape[2]
    for j in range(dw_ref.shape[0] // NSUB):
        layer = j * NSUB // KMAX

        @pl.when(idx_ref[3 * j * NSUB + 2] > 0)
        def _():
            for k in range(j * NSUB, (j + 1) * NSUB):
                r = idx_ref[3 * k]
                c = idx_ref[3 * k + 1]
                hb = h_ref[layer, :, :, _blk(r)]
                sb = s_ref[layer, :, :, _blk(c)]
                dw_ref[k] = lax.dot_general(
                    hb.reshape(rows, BLK),
                    sb.reshape(rows, BLK),
                    (((0,), (0,)), ((), ())),
                    preferred_element_type=jnp.float32,
                ) * _flag(idx_ref, k)

        @pl.when(idx_ref[3 * j * NSUB + 2] <= 0)
        def _():
            dw_ref[pl.ds(j * NSUB, NSUB)] = jnp.zeros((NSUB, BLK, BLK), jnp.float32)


def segment_dw(stash_h, stash_s, block_index, mbs):
    return pl.pallas_call(
        functools.partial(_dw_kernel, mbs),
        out_shape=jax.ShapeDtypeStruct((block_index.shape[0], BLK, BLK), jnp.float32),
        in_specs=[_SMEM, _VMEM, _VMEM],
        out_specs=_VMEM,
        compiler_params=pltpu.CompilerParams(vmem_limit_bytes=VMEM_LIMIT),
    )(block_index.reshape(-1), stash_h, stash_s)


def _exchange(send, pairs):
    return lax.ppermute(send.astype(jnp.bfloat16), "dp", pairs).astype(jnp.float32)


def dp_reduce_scatter(acc):
    n = lax.axis_size("dp")
    if n != 8:
        return lax.psum_scatter(
            acc.astype(jnp.bfloat16), "dp", scatter_dimension=0, tiled=True
        ).astype(jnp.float32)
    d = lax.axis_index("dp")
    d0, d1, d2 = d % 2, (d // 2) % 2, d // 4
    pick = lambda a, i, axis: lax.dynamic_index_in_dim(a, i, axis, keepdims=False)
    x = acc.reshape((2, 2, 2, acc.shape[0] // 8) + acc.shape[1:])
    x = pick(x, d0, 2) + _exchange(pick(x, 1 - d0, 2), [(i, i ^ 1) for i in range(8)])
    core0 = d0 == 0
    keep = jnp.where(core0, pick(x, d1, 1), pick(x, d2, 0))
    send = jnp.where(core0, pick(x, 1 - d1, 1), pick(x, 1 - d2, 0))
    x = keep + _exchange(send, [(i, i ^ (2 if i % 2 == 0 else 4)) for i in range(8)])
    rem = jnp.where(core0, d2, d1)
    send = pick(x, 1 - rem, 0)
    return pick(x, rem, 0) + _exchange(send, [(i, i ^ (4 if i % 2 == 0 else 2)) for i in range(8)])


def on_device(x_in, cotangent, weights, block_index):
    segments = lax.axis_size("segment")
    me_segment = lax.axis_index("segment")
    mbs, rows_dev, width = x_in.shape
    mbs, rows_dev = mbs * SPLIT, rows_dev // SPLIT
    x_in = x_in.reshape(mbs, rows_dev, width)
    cotangent = cotangent.reshape(mbs, rows_dev, width)
    idx = block_index.reshape(LSLOT, KMAX, 3)
    ticks = mbs + segments - 1

    def forward_tick(tick, carry):
        received, saved_h, saved_y = carry
        micro = tick - me_segment
        live = (micro >= 0) & (micro < mbs)
        place_at = jnp.clip(micro, 0, mbs - 1)
        first = lax.dynamic_index_in_dim(x_in, place_at, 0, keepdims=False)
        start = jnp.where(me_segment == 0, first, received)

        def run(operands):
            h, sh, sy = operands
            for layer in range(LSLOT):
                h, sh, sy = layer_forward(h, weights, layer, block_index, place_at, sh, sy)
            return (h, sh, sy)

        h_out, saved_h, saved_y = lax.cond(live, run, lambda ops: ops, (start, saved_h, saved_y))
        received = shifted(h_out, "segment", 1)
        return (received, saved_h, saved_y)

    stash_h = jnp.zeros((LSLOT, mbs, rows_dev, width), jnp.bfloat16)
    stash_y = jnp.zeros((LSLOT, mbs, rows_dev, width), jnp.float32)
    blank = jnp.zeros((rows_dev, width), jnp.bfloat16)
    unused_recv, stash_h, stash_y = lax.fori_loop(
        0, ticks, forward_tick, (blank, stash_h, stash_y)
    )
    stash_s = jnp.zeros((LSLOT, mbs, rows_dev, width), jnp.bfloat16)

    def backward_tick(tick, carry):
        received, saved_s = carry
        micro = tick - (segments - 1 - me_segment)
        live = (micro >= 0) & (micro < mbs)
        place_at = jnp.clip(micro, 0, mbs - 1)
        top = lax.dynamic_index_in_dim(cotangent, place_at, 0, keepdims=False)
        grad_in = jnp.where(me_segment == segments - 1, top, received)

        def run(operands):
            grad, ss = operands
            for layer in reversed(range(LSLOT)):
                grad, ss = layer_backward(grad, stash_y, weights, layer, block_index, place_at, ss)
            return (grad, ss)

        grad_out, saved_s = lax.cond(live, run, lambda ops: ops, (grad_in, saved_s))
        received = shifted(grad_out, "segment", -1)
        return (received, saved_s)

    unused_grad, stash_s = lax.fori_loop(0, ticks, backward_tick, (blank, stash_s))
    acc = segment_dw(stash_h, stash_s, block_index, mbs)
    return dp_reduce_scatter(acc)


def solution(mesh):
    return jax.shard_map(
        on_device,
        mesh=mesh,
        in_specs=(
            P(None, "dp", None),
            P(None, "dp", None),
            P("segment", None, None),
            P("segment", None),
        ),
        out_specs=P(("segment", "dp"), None, None),
        check_vma=False,
    )
```

```python
import functools

import jax
import jax.numpy as jnp
from jax import lax
from jax.experimental import pallas as pl
from jax.experimental.pallas import tpu as pltpu
from jax.sharding import PartitionSpec as P

BLK = 128
LSLOT = 2
KMAX = 128
CH = 512
NSUB = 16
SPLIT = 2
GROUP = 8
VMEM_LIMIT = 60 * 1024 * 1024

_SMEM = pl.BlockSpec(memory_space=pltpu.SMEM)
_VMEM = pl.BlockSpec(memory_space=pltpu.VMEM)
_ANY = pl.BlockSpec(memory_space=pl.ANY)


def shifted(value, axis, steps):
    count = lax.axis_size(axis)
    leading, last = (max(0, -steps), min(count, count - steps))
    return lax.ppermute(value, axis, [(source, source + steps) for source in range(leading, last)])


def _blk(i):
    return pl.ds(pl.multiple_of(i * BLK, BLK), BLK)


def _chunk(j):
    return pl.ds(pl.multiple_of(j * CH, CH), CH)


def _flag(idx_ref, k):
    return jnp.where(idx_ref[3 * k + 2] > 0, 1.0, 0.0).astype(jnp.float32)


def _w_copies(w_hbm, base, w_vmem, sems):
    copies = []
    for j in range(w_vmem.shape[0] // NSUB):
        copy = pltpu.make_async_copy(
            w_hbm.at[pl.ds(base + j * NSUB, NSUB)], w_vmem.at[pl.ds(j * NSUB, NSUB)], sems.at[j]
        )
        copy.start()
        copies.append(copy)
    return copies


def _slot_chunks(idx_ref, base, copies, product, update):
    for j, copy in enumerate(copies):
        copy.wait()

        @pl.when(idx_ref[3 * (base + j * NSUB) + 2] > 0)
        def _():
            for g in range(j * NSUB, (j + 1) * NSUB, GROUP):
                parts = [product(k) for k in range(g, g + GROUP)]
                for k, part in zip(range(g, g + GROUP), parts):
                    update(k, part)


def _fwd_kernel(base, layer, at_ref, idx_ref, h_ref, w_hbm, sh_in, sy_in, hout_ref, sh_ref, sy_ref, w_vmem, y_vmem, sems, io_sems):
    del sh_in, sy_in
    width = h_ref.shape[1]
    at = at_ref[0]
    copies = _w_copies(w_hbm, base, w_vmem, sems)
    save_h = pltpu.make_async_copy(h_ref, sh_ref.at[layer, at], io_sems.at[0])
    save_h.start()
    y_vmem[...] = jnp.zeros_like(y_vmem)

    def product(k):
        r = idx_ref[3 * (base + k)]
        return jnp.dot(h_ref[:, _blk(r)], w_vmem[k], preferred_element_type=jnp.float32)

    def update(k, p):
        c = idx_ref[3 * (base + k) + 1]
        y_vmem[:, _blk(c)] += p * _flag(idx_ref, base + k)

    _slot_chunks(idx_ref, base, copies, product, update)
    save_y = pltpu.make_async_copy(y_vmem, sy_ref.at[layer, at], io_sems.at[1])
    save_y.start()

    def epi(j, carry):
        y = y_vmem[:, _chunk(j)]
        h = h_ref[:, _chunk(j)].astype(jnp.float32)
        hout_ref[:, _chunk(j)] = (h + y / (1.0 + jnp.exp(-y))).astype(hout_ref.dtype)
        return carry

    lax.fori_loop(0, width // CH, epi, 0)
    save_h.wait()
    save_y.wait()


def layer_forward(h, weights, layer, block_index, at, stash_h, stash_y):
    rows, width = h.shape
    return pl.pallas_call(
        functools.partial(_fwd_kernel, layer * KMAX, layer),
        out_shape=(
            jax.ShapeDtypeStruct((rows, width), jnp.bfloat16),
            jax.ShapeDtypeStruct(stash_h.shape, stash_h.dtype),
            jax.ShapeDtypeStruct(stash_y.shape, stash_y.dtype),
        ),
        in_specs=[_SMEM, _SMEM, _VMEM, _ANY, _ANY, _ANY],
        out_specs=(_VMEM, _ANY, _ANY),
        scratch_shapes=[
            pltpu.VMEM((KMAX, BLK, BLK), weights.dtype),
            pltpu.VMEM((rows, width), jnp.float32),
            pltpu.SemaphoreType.DMA((KMAX // NSUB,)),
            pltpu.SemaphoreType.DMA((2,)),
        ],
        input_output_aliases={4: 1, 5: 2},
        compiler_params=pltpu.CompilerParams(vmem_limit_bytes=VMEM_LIMIT),
    )(at.reshape(1), block_index.reshape(-1), h, weights, stash_h, stash_y)


def _bwd_kernel(base, layer, at_ref, idx_ref, g_ref, sy_hbm, w_hbm, ss_in, gout_ref, ss_ref, y_vmem, s_vmem, sp_ref, w_vmem, sems, io_sems):
    del ss_in
    width = g_ref.shape[1]
    at = at_ref[0]
    load_y = pltpu.make_async_copy(sy_hbm.at[layer, at], y_vmem, io_sems.at[0])
    load_y.start()
    copies = _w_copies(w_hbm, base, w_vmem, sems)
    load_y.wait()

    def pre(j, carry):
        y = y_vmem[:, _chunk(j)]
        sig = 1.0 / (1.0 + jnp.exp(-y))
        g = g_ref[:, _chunk(j)].astype(jnp.float32)
        s_vmem[:, _chunk(j)] = (g * sig * (1.0 + y * (1.0 - sig))).astype(s_vmem.dtype)
        sp_ref[:, _chunk(j)] = jnp.zeros((g_ref.shape[0], CH), jnp.float32)
        return carry

    lax.fori_loop(0, width // CH, pre, 0)
    save_s = pltpu.make_async_copy(s_vmem, ss_ref.at[layer, at], io_sems.at[1])
    save_s.start()

    def product(k):
        c = idx_ref[3 * (base + k) + 1]
        return lax.dot_general(
            s_vmem[:, _blk(c)],
            w_vmem[k],
            (((1,), (1,)), ((), ())),
            preferred_element_type=jnp.float32,
        )

    def update(k, back):
        r = idx_ref[3 * (base + k)]
        sp_ref[:, _blk(r)] += back * _flag(idx_ref, base + k)

    _slot_chunks(idx_ref, base, copies, product, update)

    def epi(j, carry):
        g = g_ref[:, _chunk(j)].astype(jnp.float32)
        gout_ref[:, _chunk(j)] = (g + sp_ref[:, _chunk(j)]).astype(gout_ref.dtype)
        return carry

    lax.fori_loop(0, width // CH, epi, 0)
    save_s.wait()


def layer_backward(g, stash_y, weights, layer, block_index, at, stash_s):
    rows, width = g.shape
    return pl.pallas_call(
        functools.partial(_bwd_kernel, layer * KMAX, layer),
        out_shape=(
            jax.ShapeDtypeStruct((rows, width), jnp.bfloat16),
            jax.ShapeDtypeStruct(stash_s.shape, stash_s.dtype),
        ),
        in_specs=[_SMEM, _SMEM, _VMEM, _ANY, _ANY, _ANY],
        out_specs=(_VMEM, _ANY),
        scratch_shapes=[
            pltpu.VMEM((rows, width), jnp.float32),
            pltpu.VMEM((rows, width), jnp.bfloat16),
            pltpu.VMEM((rows, width), jnp.float32),
            pltpu.VMEM((KMAX, BLK, BLK), weights.dtype),
            pltpu.SemaphoreType.DMA((KMAX // NSUB,)),
            pltpu.SemaphoreType.DMA((2,)),
        ],
        input_output_aliases={5: 1},
        compiler_params=pltpu.CompilerParams(vmem_limit_bytes=VMEM_LIMIT),
    )(at.reshape(1), block_index.reshape(-1), g, stash_y, weights, stash_s)


def _dw_kernel(mbs, idx_ref, h_ref, s_ref, dw_ref):
    rows = h_ref.shape[1] * h_ref.shape[2]
    for j in range(dw_ref.shape[0] // NSUB):
        layer = j * NSUB // KMAX

        @pl.when(idx_ref[3 * j * NSUB + 2] > 0)
        def _():
            for k in range(j * NSUB, (j + 1) * NSUB):
                r = idx_ref[3 * k]
                c = idx_ref[3 * k + 1]
                hb = h_ref[layer, :, :, _blk(r)]
                sb = s_ref[layer, :, :, _blk(c)]
                dw_ref[k] = lax.dot_general(
                    hb.reshape(rows, BLK),
                    sb.reshape(rows, BLK),
                    (((0,), (0,)), ((), ())),
                    preferred_element_type=jnp.float32,
                ) * _flag(idx_ref, k)

        @pl.when(idx_ref[3 * j * NSUB + 2] <= 0)
        def _():
            dw_ref[pl.ds(j * NSUB, NSUB)] = jnp.zeros((NSUB, BLK, BLK), jnp.float32)


def segment_dw(stash_h, stash_s, block_index, mbs):
    return pl.pallas_call(
        functools.partial(_dw_kernel, mbs),
        out_shape=jax.ShapeDtypeStruct((block_index.shape[0], BLK, BLK), jnp.float32),
        in_specs=[_SMEM, _VMEM, _VMEM],
        out_specs=_VMEM,
        compiler_params=pltpu.CompilerParams(vmem_limit_bytes=VMEM_LIMIT),
    )(block_index.reshape(-1), stash_h, stash_s)


def _exchange(send, pairs):
    return lax.ppermute(send.astype(jnp.bfloat16), "dp", pairs).astype(jnp.float32)


def dp_reduce_scatter(acc):
    n = lax.axis_size("dp")
    if n != 8:
        return lax.psum_scatter(
            acc.astype(jnp.bfloat16), "dp", scatter_dimension=0, tiled=True
        ).astype(jnp.float32)
    d = lax.axis_index("dp")
    d0, d1, d2 = d % 2, (d // 2) % 2, d // 4
    pick = lambda a, i, axis: lax.dynamic_index_in_dim(a, i, axis, keepdims=False)
    x = acc.reshape((2, 2, 2, acc.shape[0] // 8) + acc.shape[1:])
    x = pick(x, d0, 2) + _exchange(pick(x, 1 - d0, 2), [(i, i ^ 1) for i in range(8)])
    core0 = d0 == 0
    keep = jnp.where(core0, pick(x, d1, 1), pick(x, d2, 0))
    send = jnp.where(core0, pick(x, 1 - d1, 1), pick(x, 1 - d2, 0))
    x = keep + _exchange(send, [(i, i ^ (2 if i % 2 == 0 else 4)) for i in range(8)])
    rem = jnp.where(core0, d2, d1)
    send = pick(x, 1 - rem, 0)
    return pick(x, rem, 0) + _exchange(send, [(i, i ^ (4 if i % 2 == 0 else 2)) for i in range(8)])


def on_device(x_in, cotangent, weights, block_index):
    segments = lax.axis_size("segment")
    me_segment = lax.axis_index("segment")
    mbs, rows_dev, width = x_in.shape
    mbs, rows_dev = mbs * SPLIT, rows_dev // SPLIT
    x_in = x_in.reshape(mbs, rows_dev, width)
    cotangent = cotangent.reshape(mbs, rows_dev, width)
    idx = block_index.reshape(LSLOT, KMAX, 3)

    def tick_body(tick, carry):
        recv_f, recv_b, saved_h, saved_y, saved_s = carry
        micro_f = tick - me_segment
        live_f = (micro_f >= 0) & (micro_f < mbs)
        at_f = jnp.clip(micro_f, 0, mbs - 1)
        first = lax.dynamic_index_in_dim(x_in, at_f, 0, keepdims=False)
        start = jnp.where(me_segment == 0, first, recv_f)

        def run_f(operands):
            h, sh, sy = operands
            for layer in range(LSLOT):
                h, sh, sy = layer_forward(h, weights, layer, block_index, at_f, sh, sy)
            return (h, sh, sy)

        h_out, saved_h, saved_y = lax.cond(live_f, run_f, lambda ops: ops, (start, saved_h, saved_y))
        send_f = shifted(h_out, "segment", 1)

        micro_b = tick - (2 * segments - 2 - me_segment)
        live_b = (micro_b >= 0) & (micro_b < mbs)
        at_b = jnp.clip(micro_b, 0, mbs - 1)
        top = lax.dynamic_index_in_dim(cotangent, at_b, 0, keepdims=False)
        grad_in = jnp.where(me_segment == segments - 1, top, recv_b)
        stash_y_now = saved_y

        def run_b(operands):
            grad, ss = operands
            for layer in reversed(range(LSLOT)):
                grad, ss = layer_backward(grad, stash_y_now, weights, layer, block_index, at_b, ss)
            return (grad, ss)

        grad_out, saved_s = lax.cond(live_b, run_b, lambda ops: ops, (grad_in, saved_s))
        send_b = shifted(grad_out, "segment", -1)
        return (send_f, send_b, saved_h, saved_y, saved_s)

    stash_h = jnp.zeros((LSLOT, mbs, rows_dev, width), jnp.bfloat16)
    stash_y = jnp.zeros((LSLOT, mbs, rows_dev, width), jnp.float32)
    stash_s = jnp.zeros((LSLOT, mbs, rows_dev, width), jnp.bfloat16)
    blank = jnp.zeros((rows_dev, width), jnp.bfloat16)
    ticks = mbs + 2 * segments - 2
    carry = (blank, blank, stash_h, stash_y, stash_s)
    for tick in range(ticks):
        carry = tick_body(tick, carry)
    unused_f, unused_b, stash_h, stash_y, stash_s = carry
    acc = segment_dw(stash_h, stash_s, block_index, mbs)
    return dp_reduce_scatter(acc)


def solution(mesh):
    return jax.shard_map(
        on_device,
        mesh=mesh,
        in_specs=(
            P(None, "dp", None),
            P(None, "dp", None),
            P("segment", None, None),
            P("segment", None),
        ),
        out_specs=P(("segment", "dp"), None, None),
        check_vma=False,
    )
```

```python
import functools

import jax
import jax.numpy as jnp
from jax import lax
from jax.experimental import pallas as pl
from jax.experimental.pallas import tpu as pltpu
from jax.sharding import PartitionSpec as P

BLK = 128
LSLOT = 2
KMAX = 128
CH = 512
NSUB = 16
SPLIT = 1
GROUP = 8
VMEM_LIMIT = 60 * 1024 * 1024

_SMEM = pl.BlockSpec(memory_space=pltpu.SMEM)
_VMEM = pl.BlockSpec(memory_space=pltpu.VMEM)
_ANY = pl.BlockSpec(memory_space=pl.ANY)


def shifted(value, axis, steps):
    count = lax.axis_size(axis)
    leading, last = (max(0, -steps), min(count, count - steps))
    return lax.ppermute(value, axis, [(source, source + steps) for source in range(leading, last)])


def _blk(i):
    return pl.ds(pl.multiple_of(i * BLK, BLK), BLK)


def _chunk(j):
    return pl.ds(pl.multiple_of(j * CH, CH), CH)


def _flag(idx_ref, k):
    return jnp.where(idx_ref[3 * k + 2] > 0, 1.0, 0.0).astype(jnp.float32)


def _w_copies(w_hbm, base, w_vmem, sems):
    copies = []
    for j in range(w_vmem.shape[0] // NSUB):
        copy = pltpu.make_async_copy(
            w_hbm.at[pl.ds(base + j * NSUB, NSUB)], w_vmem.at[pl.ds(j * NSUB, NSUB)], sems.at[j]
        )
        copy.start()
        copies.append(copy)
    return copies


def _slot_chunks(idx_ref, base, copies, product, update):
    for j, copy in enumerate(copies):
        copy.wait()

        @pl.when(idx_ref[3 * (base + j * NSUB) + 2] > 0)
        def _():
            for g in range(j * NSUB, (j + 1) * NSUB, GROUP):
                parts = [product(k) for k in range(g, g + GROUP)]
                for k, part in zip(range(g, g + GROUP), parts):
                    update(k, part)


def _fwd_kernel(base, layer, at_ref, idx_ref, h_ref, w_hbm, sh_in, sy_in, hout_ref, sh_ref, sy_ref, w_vmem, y_vmem, sems, io_sems):
    del sh_in, sy_in
    width = h_ref.shape[1]
    at = at_ref[0]
    copies = _w_copies(w_hbm, base, w_vmem, sems)
    save_h = pltpu.make_async_copy(h_ref, sh_ref.at[layer, at], io_sems.at[0])
    save_h.start()
    y_vmem[...] = jnp.zeros_like(y_vmem)

    def product(k):
        r = idx_ref[3 * (base + k)]
        return jnp.dot(h_ref[:, _blk(r)], w_vmem[k], preferred_element_type=jnp.float32)

    def update(k, p):
        c = idx_ref[3 * (base + k) + 1]
        y_vmem[:, _blk(c)] += p * _flag(idx_ref, base + k)

    _slot_chunks(idx_ref, base, copies, product, update)
    save_y = pltpu.make_async_copy(y_vmem, sy_ref.at[layer, at], io_sems.at[1])
    save_y.start()

    def epi(j, carry):
        y = y_vmem[:, _chunk(j)]
        h = h_ref[:, _chunk(j)].astype(jnp.float32)
        hout_ref[:, _chunk(j)] = (h + y / (1.0 + jnp.exp(-y))).astype(hout_ref.dtype)
        return carry

    lax.fori_loop(0, width // CH, epi, 0)
    save_h.wait()
    save_y.wait()


def layer_forward(h, weights, layer, block_index, at, stash_h, stash_y):
    rows, width = h.shape
    return pl.pallas_call(
        functools.partial(_fwd_kernel, layer * KMAX, layer),
        out_shape=(
            jax.ShapeDtypeStruct((rows, width), jnp.bfloat16),
            jax.ShapeDtypeStruct(stash_h.shape, stash_h.dtype),
            jax.ShapeDtypeStruct(stash_y.shape, stash_y.dtype),
        ),
        in_specs=[_SMEM, _SMEM, _VMEM, _ANY, _ANY, _ANY],
        out_specs=(_VMEM, _ANY, _ANY),
        scratch_shapes=[
            pltpu.VMEM((KMAX, BLK, BLK), weights.dtype),
            pltpu.VMEM((rows, width), jnp.float32),
            pltpu.SemaphoreType.DMA((KMAX // NSUB,)),
            pltpu.SemaphoreType.DMA((2,)),
        ],
        input_output_aliases={4: 1, 5: 2},
        compiler_params=pltpu.CompilerParams(vmem_limit_bytes=VMEM_LIMIT),
    )(at.reshape(1), block_index.reshape(-1), h, weights, stash_h, stash_y)


def _bwd_kernel(base, layer, at_ref, idx_ref, g_ref, sy_hbm, w_hbm, ss_in, gout_ref, ss_ref, y_vmem, s_vmem, sp_ref, w_vmem, sems, io_sems):
    del ss_in
    width = g_ref.shape[1]
    at = at_ref[0]
    load_y = pltpu.make_async_copy(sy_hbm.at[layer, at], y_vmem, io_sems.at[0])
    load_y.start()
    copies = _w_copies(w_hbm, base, w_vmem, sems)
    load_y.wait()

    def pre(j, carry):
        y = y_vmem[:, _chunk(j)]
        sig = 1.0 / (1.0 + jnp.exp(-y))
        g = g_ref[:, _chunk(j)].astype(jnp.float32)
        s_vmem[:, _chunk(j)] = (g * sig * (1.0 + y * (1.0 - sig))).astype(s_vmem.dtype)
        sp_ref[:, _chunk(j)] = jnp.zeros((g_ref.shape[0], CH), jnp.float32)
        return carry

    lax.fori_loop(0, width // CH, pre, 0)
    save_s = pltpu.make_async_copy(s_vmem, ss_ref.at[layer, at], io_sems.at[1])
    save_s.start()

    def product(k):
        c = idx_ref[3 * (base + k) + 1]
        return lax.dot_general(
            s_vmem[:, _blk(c)],
            w_vmem[k],
            (((1,), (1,)), ((), ())),
            preferred_element_type=jnp.float32,
        )

    def update(k, back):
        r = idx_ref[3 * (base + k)]
        sp_ref[:, _blk(r)] += back * _flag(idx_ref, base + k)

    _slot_chunks(idx_ref, base, copies, product, update)

    def epi(j, carry):
        g = g_ref[:, _chunk(j)].astype(jnp.float32)
        gout_ref[:, _chunk(j)] = (g + sp_ref[:, _chunk(j)]).astype(gout_ref.dtype)
        return carry

    lax.fori_loop(0, width // CH, epi, 0)
    save_s.wait()


def layer_backward(g, stash_y, weights, layer, block_index, at, stash_s):
    rows, width = g.shape
    return pl.pallas_call(
        functools.partial(_bwd_kernel, layer * KMAX, layer),
        out_shape=(
            jax.ShapeDtypeStruct((rows, width), jnp.bfloat16),
            jax.ShapeDtypeStruct(stash_s.shape, stash_s.dtype),
        ),
        in_specs=[_SMEM, _SMEM, _VMEM, _ANY, _ANY, _ANY],
        out_specs=(_VMEM, _ANY),
        scratch_shapes=[
            pltpu.VMEM((rows, width), jnp.float32),
            pltpu.VMEM((rows, width), jnp.bfloat16),
            pltpu.VMEM((rows, width), jnp.float32),
            pltpu.VMEM((KMAX, BLK, BLK), weights.dtype),
            pltpu.SemaphoreType.DMA((KMAX // NSUB,)),
            pltpu.SemaphoreType.DMA((2,)),
        ],
        input_output_aliases={5: 1},
        compiler_params=pltpu.CompilerParams(vmem_limit_bytes=VMEM_LIMIT),
    )(at.reshape(1), block_index.reshape(-1), g, stash_y, weights, stash_s)


def _dw_kernel(mbs, idx_ref, h_ref, s_ref, dw_ref):
    rows = h_ref.shape[1] * h_ref.shape[2]
    for j in range(dw_ref.shape[0] // NSUB):
        layer = j * NSUB // KMAX

        @pl.when(idx_ref[3 * j * NSUB + 2] > 0)
        def _():
            for k in range(j * NSUB, (j + 1) * NSUB):
                r = idx_ref[3 * k]
                c = idx_ref[3 * k + 1]
                hb = h_ref[layer, :, :, _blk(r)]
                sb = s_ref[layer, :, :, _blk(c)]
                dw_ref[k] = lax.dot_general(
                    hb.reshape(rows, BLK),
                    sb.reshape(rows, BLK),
                    (((0,), (0,)), ((), ())),
                    preferred_element_type=jnp.float32,
                ) * _flag(idx_ref, k)

        @pl.when(idx_ref[3 * j * NSUB + 2] <= 0)
        def _():
            dw_ref[pl.ds(j * NSUB, NSUB)] = jnp.zeros((NSUB, BLK, BLK), jnp.float32)


def segment_dw(stash_h, stash_s, block_index, mbs):
    return pl.pallas_call(
        functools.partial(_dw_kernel, mbs),
        out_shape=jax.ShapeDtypeStruct((block_index.shape[0], BLK, BLK), jnp.float32),
        in_specs=[_SMEM, _VMEM, _VMEM],
        out_specs=_VMEM,
        compiler_params=pltpu.CompilerParams(vmem_limit_bytes=VMEM_LIMIT),
    )(block_index.reshape(-1), stash_h, stash_s)


def _exchange(send, pairs):
    return lax.ppermute(send.astype(jnp.bfloat16), "dp", pairs).astype(jnp.float32)


def dp_reduce_scatter(acc):
    n = lax.axis_size("dp")
    if n != 8:
        return lax.psum_scatter(
            acc.astype(jnp.bfloat16), "dp", scatter_dimension=0, tiled=True
        ).astype(jnp.float32)
    d = lax.axis_index("dp")
    d0, d1, d2 = d % 2, (d // 2) % 2, d // 4
    pick = lambda a, i, axis: lax.dynamic_index_in_dim(a, i, axis, keepdims=False)
    x = acc.reshape((2, 2, 2, acc.shape[0] // 8) + acc.shape[1:])
    x = pick(x, d0, 2) + _exchange(pick(x, 1 - d0, 2), [(i, i ^ 1) for i in range(8)])
    core0 = d0 == 0
    keep = jnp.where(core0, pick(x, d1, 1), pick(x, d2, 0))
    send = jnp.where(core0, pick(x, 1 - d1, 1), pick(x, 1 - d2, 0))
    x = keep + _exchange(send, [(i, i ^ (2 if i % 2 == 0 else 4)) for i in range(8)])
    rem = jnp.where(core0, d2, d1)
    send = pick(x, 1 - rem, 0)
    return pick(x, rem, 0) + _exchange(send, [(i, i ^ (4 if i % 2 == 0 else 2)) for i in range(8)])


def on_device(x_in, cotangent, weights, block_index):
    segments = lax.axis_size("segment")
    me_segment = lax.axis_index("segment")
    mbs, rows_dev, width = x_in.shape
    mbs, rows_dev = mbs * SPLIT, rows_dev // SPLIT
    x_in = x_in.reshape(mbs, rows_dev, width)
    cotangent = cotangent.reshape(mbs, rows_dev, width)
    idx = block_index.reshape(LSLOT, KMAX, 3)

    def tick_body(tick, carry):
        recv_f, recv_b, saved_h, saved_y, saved_s = carry
        micro_f = tick - me_segment
        live_f = (micro_f >= 0) & (micro_f < mbs)
        at_f = jnp.clip(micro_f, 0, mbs - 1)
        first = lax.dynamic_index_in_dim(x_in, at_f, 0, keepdims=False)
        start = jnp.where(me_segment == 0, first, recv_f)

        def run_f(operands):
            h, sh, sy = operands
            for layer in range(LSLOT):
                h, sh, sy = layer_forward(h, weights, layer, block_index, at_f, sh, sy)
            return (h, sh, sy)

        h_out, saved_h, saved_y = lax.cond(live_f, run_f, lambda ops: ops, (start, saved_h, saved_y))
        send_f = shifted(h_out, "segment", 1)

        micro_b = tick - (2 * segments - 2 - me_segment)
        live_b = (micro_b >= 0) & (micro_b < mbs)
        at_b = jnp.clip(micro_b, 0, mbs - 1)
        top = lax.dynamic_index_in_dim(cotangent, at_b, 0, keepdims=False)
        grad_in = jnp.where(me_segment == segments - 1, top, recv_b)
        stash_y_now = saved_y

        def run_b(operands):
            grad, ss = operands
            for layer in reversed(range(LSLOT)):
                grad, ss = layer_backward(grad, stash_y_now, weights, layer, block_index, at_b, ss)
            return (grad, ss)

        grad_out, saved_s = lax.cond(live_b, run_b, lambda ops: ops, (grad_in, saved_s))
        send_b = shifted(grad_out, "segment", -1)
        return (send_f, send_b, saved_h, saved_y, saved_s)

    stash_h = jnp.zeros((LSLOT, mbs, rows_dev, width), jnp.bfloat16)
    stash_y = jnp.zeros((LSLOT, mbs, rows_dev, width), jnp.float32)
    stash_s = jnp.zeros((LSLOT, mbs, rows_dev, width), jnp.bfloat16)
    blank = jnp.zeros((rows_dev, width), jnp.bfloat16)
    ticks = mbs + 2 * segments - 2
    carry = (blank, blank, stash_h, stash_y, stash_s)
    for tick in range(ticks):
        carry = tick_body(tick, carry)
    unused_f, unused_b, stash_h, stash_y, stash_s = carry
    acc = segment_dw(stash_h, stash_s, block_index, mbs)
    return dp_reduce_scatter(acc)


def solution(mesh):
    return jax.shard_map(
        on_device,
        mesh=mesh,
        in_specs=(
            P(None, "dp", None),
            P(None, "dp", None),
            P("segment", None, None),
            P("segment", None),
        ),
        out_specs=P(("segment", "dp"), None, None),
        check_vma=False,
    )
```

```python
import functools

import jax
import jax.numpy as jnp
from jax import lax
from jax.experimental import pallas as pl
from jax.experimental.pallas import tpu as pltpu
from jax.sharding import PartitionSpec as P

BLK = 128
LSLOT = 2
KMAX = 128
CH = 512
NSUB = 16
SPLIT = 2
GROUP = 8
VMEM_LIMIT = 60 * 1024 * 1024

_SMEM = pl.BlockSpec(memory_space=pltpu.SMEM)
_VMEM = pl.BlockSpec(memory_space=pltpu.VMEM)
_ANY = pl.BlockSpec(memory_space=pl.ANY)


def shifted(value, axis, steps):
    count = lax.axis_size(axis)
    leading, last = (max(0, -steps), min(count, count - steps))
    return lax.ppermute(value, axis, [(source, source + steps) for source in range(leading, last)])


def _blk(i):
    return pl.ds(pl.multiple_of(i * BLK, BLK), BLK)


def _chunk(j):
    return pl.ds(pl.multiple_of(j * CH, CH), CH)


def _flag(idx_ref, k):
    return jnp.where(idx_ref[3 * k + 2] > 0, 1.0, 0.0).astype(jnp.float32)


def _w_copies(w_hbm, base, w_vmem, sems):
    copies = []
    for j in range(w_vmem.shape[0] // NSUB):
        copy = pltpu.make_async_copy(
            w_hbm.at[pl.ds(base + j * NSUB, NSUB)], w_vmem.at[pl.ds(j * NSUB, NSUB)], sems.at[j]
        )
        copy.start()
        copies.append(copy)
    return copies


def _slot_chunks(idx_ref, base, copies, product, update):
    for j, copy in enumerate(copies):
        copy.wait()

        @pl.when(idx_ref[3 * (base + j * NSUB) + 2] > 0)
        def _():
            for g in range(j * NSUB, (j + 1) * NSUB, GROUP):
                parts = [product(k) for k in range(g, g + GROUP)]
                for k, part in zip(range(g, g + GROUP), parts):
                    update(k, part)


def _fwd_kernel(base, layer, at_ref, idx_ref, h_ref, w_hbm, sh_in, sy_in, hout_ref, sh_ref, sy_ref, w_vmem, y_vmem, sems, io_sems):
    del sh_in, sy_in
    width = h_ref.shape[1]
    at = at_ref[0]
    copies = _w_copies(w_hbm, base, w_vmem, sems)
    save_h = pltpu.make_async_copy(h_ref, sh_ref.at[layer, at], io_sems.at[0])
    save_h.start()
    y_vmem[...] = jnp.zeros_like(y_vmem)

    def product(k):
        r = idx_ref[3 * (base + k)]
        return jnp.dot(h_ref[:, _blk(r)], w_vmem[k], preferred_element_type=jnp.float32)

    def update(k, p):
        c = idx_ref[3 * (base + k) + 1]
        y_vmem[:, _blk(c)] += p * _flag(idx_ref, base + k)

    _slot_chunks(idx_ref, base, copies, product, update)
    save_y = pltpu.make_async_copy(y_vmem, sy_ref.at[layer, at], io_sems.at[1])
    save_y.start()

    def epi(j, carry):
        y = y_vmem[:, _chunk(j)]
        h = h_ref[:, _chunk(j)].astype(jnp.float32)
        hout_ref[:, _chunk(j)] = (h + y / (1.0 + jnp.exp(-y))).astype(hout_ref.dtype)
        return carry

    lax.fori_loop(0, width // CH, epi, 0)
    save_h.wait()
    save_y.wait()


def layer_forward(h, weights, layer, block_index, at, stash_h, stash_y):
    rows, width = h.shape
    return pl.pallas_call(
        functools.partial(_fwd_kernel, layer * KMAX, layer),
        out_shape=(
            jax.ShapeDtypeStruct((rows, width), jnp.bfloat16),
            jax.ShapeDtypeStruct(stash_h.shape, stash_h.dtype),
            jax.ShapeDtypeStruct(stash_y.shape, stash_y.dtype),
        ),
        in_specs=[_SMEM, _SMEM, _VMEM, _ANY, _ANY, _ANY],
        out_specs=(_VMEM, _ANY, _ANY),
        scratch_shapes=[
            pltpu.VMEM((KMAX, BLK, BLK), weights.dtype),
            pltpu.VMEM((rows, width), jnp.float32),
            pltpu.SemaphoreType.DMA((KMAX // NSUB,)),
            pltpu.SemaphoreType.DMA((2,)),
        ],
        input_output_aliases={4: 1, 5: 2},
        compiler_params=pltpu.CompilerParams(vmem_limit_bytes=VMEM_LIMIT),
    )(at.reshape(1), block_index.reshape(-1), h, weights, stash_h, stash_y)


def _bwd_kernel(base, layer, at_ref, idx_ref, g_ref, sy_hbm, w_hbm, ss_in, gout_ref, ss_ref, y_vmem, s_vmem, sp_ref, w_vmem, sems, io_sems):
    del ss_in
    width = g_ref.shape[1]
    at = at_ref[0]
    load_y = pltpu.make_async_copy(sy_hbm.at[layer, at], y_vmem, io_sems.at[0])
    load_y.start()
    copies = _w_copies(w_hbm, base, w_vmem, sems)
    load_y.wait()

    def pre(j, carry):
        y = y_vmem[:, _chunk(j)]
        sig = 1.0 / (1.0 + jnp.exp(-y))
        g = g_ref[:, _chunk(j)].astype(jnp.float32)
        s_vmem[:, _chunk(j)] = (g * sig * (1.0 + y * (1.0 - sig))).astype(s_vmem.dtype)
        sp_ref[:, _chunk(j)] = jnp.zeros((g_ref.shape[0], CH), jnp.float32)
        return carry

    lax.fori_loop(0, width // CH, pre, 0)
    save_s = pltpu.make_async_copy(s_vmem, ss_ref.at[layer, at], io_sems.at[1])
    save_s.start()

    def product(k):
        c = idx_ref[3 * (base + k) + 1]
        return lax.dot_general(
            s_vmem[:, _blk(c)],
            w_vmem[k],
            (((1,), (1,)), ((), ())),
            preferred_element_type=jnp.float32,
        )

    def update(k, back):
        r = idx_ref[3 * (base + k)]
        sp_ref[:, _blk(r)] += back * _flag(idx_ref, base + k)

    _slot_chunks(idx_ref, base, copies, product, update)

    def epi(j, carry):
        g = g_ref[:, _chunk(j)].astype(jnp.float32)
        gout_ref[:, _chunk(j)] = (g + sp_ref[:, _chunk(j)]).astype(gout_ref.dtype)
        return carry

    lax.fori_loop(0, width // CH, epi, 0)
    save_s.wait()


def layer_backward(g, stash_y, weights, layer, block_index, at, stash_s):
    rows, width = g.shape
    return pl.pallas_call(
        functools.partial(_bwd_kernel, layer * KMAX, layer),
        out_shape=(
            jax.ShapeDtypeStruct((rows, width), jnp.bfloat16),
            jax.ShapeDtypeStruct(stash_s.shape, stash_s.dtype),
        ),
        in_specs=[_SMEM, _SMEM, _VMEM, _ANY, _ANY, _ANY],
        out_specs=(_VMEM, _ANY),
        scratch_shapes=[
            pltpu.VMEM((rows, width), jnp.float32),
            pltpu.VMEM((rows, width), jnp.bfloat16),
            pltpu.VMEM((rows, width), jnp.float32),
            pltpu.VMEM((KMAX, BLK, BLK), weights.dtype),
            pltpu.SemaphoreType.DMA((KMAX // NSUB,)),
            pltpu.SemaphoreType.DMA((2,)),
        ],
        input_output_aliases={5: 1},
        compiler_params=pltpu.CompilerParams(vmem_limit_bytes=VMEM_LIMIT),
    )(at.reshape(1), block_index.reshape(-1), g, stash_y, weights, stash_s)


def _dw_kernel(mbs, idx_ref, h_ref, s_ref, dw_ref):
    rows = h_ref.shape[1] * h_ref.shape[2]
    for j in range(dw_ref.shape[0] // NSUB):
        layer = j * NSUB // KMAX

        @pl.when(idx_ref[3 * j * NSUB + 2] > 0)
        def _():
            for k in range(j * NSUB, (j + 1) * NSUB):
                r = idx_ref[3 * k]
                c = idx_ref[3 * k + 1]
                hb = h_ref[layer, :, :, _blk(r)]
                sb = s_ref[layer, :, :, _blk(c)]
                dw_ref[k] = lax.dot_general(
                    hb.reshape(rows, BLK),
                    sb.reshape(rows, BLK),
                    (((0,), (0,)), ((), ())),
                    preferred_element_type=jnp.float32,
                ) * _flag(idx_ref, k)

        @pl.when(idx_ref[3 * j * NSUB + 2] <= 0)
        def _():
            dw_ref[pl.ds(j * NSUB, NSUB)] = jnp.zeros((NSUB, BLK, BLK), jnp.float32)


def segment_dw(stash_h, stash_s, block_index, mbs):
    return pl.pallas_call(
        functools.partial(_dw_kernel, mbs),
        out_shape=jax.ShapeDtypeStruct((block_index.shape[0], BLK, BLK), jnp.float32),
        in_specs=[_SMEM, _VMEM, _VMEM],
        out_specs=_VMEM,
        compiler_params=pltpu.CompilerParams(vmem_limit_bytes=VMEM_LIMIT),
    )(block_index.reshape(-1), stash_h, stash_s)


def _dw_half_kernel(sel_ref, idx_ref, h_ref, s_ref, out_ref):
    b0 = sel_ref[0]
    rows = h_ref.shape[1] * h_ref.shape[2]
    per = out_ref.shape[1]
    for q in range(out_ref.shape[0]):
        layer = (2 * q * per) // KMAX
        for j in range(per // NSUB):
            first = 2 * q * per + b0 * per + j * NSUB

            @pl.when(idx_ref[3 * first + 2] > 0)
            def _():
                for i in range(NSUB):
                    k = first + i
                    r = idx_ref[3 * k]
                    c = idx_ref[3 * k + 1]
                    hb = h_ref[layer, :, :, _blk(r)].reshape(rows, BLK)
                    sb = s_ref[layer, :, :, _blk(c)].reshape(rows, BLK)
                    part = lax.dot_general(
                        hb, sb, (((0,), (0,)), ((), ())), preferred_element_type=jnp.float32
                    )
                    out_ref[q, j * NSUB + i] = (part * _flag(idx_ref, k)).astype(out_ref.dtype)

            @pl.when(idx_ref[3 * first + 2] <= 0)
            def _():
                out_ref[q, pl.ds(j * NSUB, NSUB)] = jnp.zeros((NSUB, BLK, BLK), out_ref.dtype)


def dw_half(stash_h, stash_s, block_index, b0, dtype):
    per = block_index.shape[0] // 8
    return pl.pallas_call(
        _dw_half_kernel,
        out_shape=jax.ShapeDtypeStruct((4, per, BLK, BLK), dtype),
        in_specs=[_SMEM, _SMEM, _VMEM, _VMEM],
        out_specs=_VMEM,
        compiler_params=pltpu.CompilerParams(vmem_limit_bytes=VMEM_LIMIT),
    )(b0.reshape(1).astype(jnp.int32), block_index.reshape(-1), stash_h, stash_s)


def _exchange(send, pairs):
    return lax.ppermute(send.astype(jnp.bfloat16), "dp", pairs).astype(jnp.float32)


def weight_grads(stash_h, stash_s, block_index, mbs):
    n = lax.axis_size("dp")
    if n != 8:
        acc = segment_dw(stash_h, stash_s, block_index, mbs)
        return lax.psum_scatter(
            acc.astype(jnp.bfloat16), "dp", scatter_dimension=0, tiled=True
        ).astype(jnp.float32)
    d = lax.axis_index("dp")
    d0, d1, d2 = d % 2, (d // 2) % 2, d // 4
    pick = lambda a, i, axis: lax.dynamic_index_in_dim(a, i, axis, keepdims=False)
    send = dw_half(stash_h, stash_s, block_index, 1 - d0, jnp.bfloat16)
    got = lax.ppermute(send, "dp", [(i, i ^ 1) for i in range(8)])
    keep = dw_half(stash_h, stash_s, block_index, d0, jnp.float32)
    x = (keep + got.astype(jnp.float32)).reshape((2, 2) + keep.shape[1:])
    core0 = d0 == 0
    keep = jnp.where(core0, pick(x, d1, 1), pick(x, d2, 0))
    send = jnp.where(core0, pick(x, 1 - d1, 1), pick(x, 1 - d2, 0))
    x = keep + _exchange(send, [(i, i ^ (2 if i % 2 == 0 else 4)) for i in range(8)])
    rem = jnp.where(core0, d2, d1)
    send = pick(x, 1 - rem, 0)
    return pick(x, rem, 0) + _exchange(send, [(i, i ^ (4 if i % 2 == 0 else 2)) for i in range(8)])


def on_device(x_in, cotangent, weights, block_index):
    segments = lax.axis_size("segment")
    me_segment = lax.axis_index("segment")
    mbs, rows_dev, width = x_in.shape
    mbs, rows_dev = mbs * SPLIT, rows_dev // SPLIT
    x_in = x_in.reshape(mbs, rows_dev, width)
    cotangent = cotangent.reshape(mbs, rows_dev, width)
    idx = block_index.reshape(LSLOT, KMAX, 3)

    def tick_body(tick, carry):
        recv_f, recv_b, saved_h, saved_y, saved_s = carry
        micro_f = tick - me_segment
        live_f = (micro_f >= 0) & (micro_f < mbs)
        at_f = jnp.clip(micro_f, 0, mbs - 1)
        first = lax.dynamic_index_in_dim(x_in, at_f, 0, keepdims=False)
        start = jnp.where(me_segment == 0, first, recv_f)

        def run_f(operands):
            h, sh, sy = operands
            for layer in range(LSLOT):
                h, sh, sy = layer_forward(h, weights, layer, block_index, at_f, sh, sy)
            return (h, sh, sy)

        h_out, saved_h, saved_y = lax.cond(live_f, run_f, lambda ops: ops, (start, saved_h, saved_y))
        send_f = shifted(h_out, "segment", 1)

        micro_b = tick - (2 * segments - 2 - me_segment)
        live_b = (micro_b >= 0) & (micro_b < mbs)
        at_b = jnp.clip(micro_b, 0, mbs - 1)
        top = lax.dynamic_index_in_dim(cotangent, at_b, 0, keepdims=False)
        grad_in = jnp.where(me_segment == segments - 1, top, recv_b)
        stash_y_now = saved_y

        def run_b(operands):
            grad, ss = operands
            for layer in reversed(range(LSLOT)):
                grad, ss = layer_backward(grad, stash_y_now, weights, layer, block_index, at_b, ss)
            return (grad, ss)

        grad_out, saved_s = lax.cond(live_b, run_b, lambda ops: ops, (grad_in, saved_s))
        send_b = shifted(grad_out, "segment", -1)
        return (send_f, send_b, saved_h, saved_y, saved_s)

    stash_h = jnp.zeros((LSLOT, mbs, rows_dev, width), jnp.bfloat16)
    stash_y = jnp.zeros((LSLOT, mbs, rows_dev, width), jnp.float32)
    stash_s = jnp.zeros((LSLOT, mbs, rows_dev, width), jnp.bfloat16)
    blank = jnp.zeros((rows_dev, width), jnp.bfloat16)
    ticks = mbs + 2 * segments - 2
    carry = (blank, blank, stash_h, stash_y, stash_s)
    for tick in range(ticks):
        carry = tick_body(tick, carry)
    unused_f, unused_b, stash_h, stash_y, stash_s = carry
    return weight_grads(stash_h, stash_s, block_index, mbs)


def solution(mesh):
    return jax.shard_map(
        on_device,
        mesh=mesh,
        in_specs=(
            P(None, "dp", None),
            P(None, "dp", None),
            P("segment", None, None),
            P("segment", None),
        ),
        out_specs=P(("segment", "dp"), None, None),
        check_vma=False,
    )
```

```python
import functools

import jax
import jax.numpy as jnp
from jax import lax
from jax.experimental import pallas as pl
from jax.experimental.pallas import tpu as pltpu
from jax.sharding import PartitionSpec as P

BLK = 128
LSLOT = 2
KMAX = 128
CH = 512
NSUB = 16
SPLIT = 2
GROUP = 8
VMEM_LIMIT = 60 * 1024 * 1024

_SMEM = pl.BlockSpec(memory_space=pltpu.SMEM)
_VMEM = pl.BlockSpec(memory_space=pltpu.VMEM)
_ANY = pl.BlockSpec(memory_space=pl.ANY)


def shifted(value, axis, steps):
    count = lax.axis_size(axis)
    leading, last = (max(0, -steps), min(count, count - steps))
    return lax.ppermute(value, axis, [(source, source + steps) for source in range(leading, last)])


def _blk(i):
    return pl.ds(pl.multiple_of(i * BLK, BLK), BLK)


def _chunk(j):
    return pl.ds(pl.multiple_of(j * CH, CH), CH)


def _flag(idx_ref, k):
    return jnp.where(idx_ref[3 * k + 2] > 0, 1.0, 0.0).astype(jnp.float32)


class _WeightChunks:
    def __init__(self, w_hbm, base, w_vmem, sems):
        self.w_hbm, self.base, self.w_vmem, self.sems = w_hbm, base, w_vmem, sems

    def copy(self, j):
        return pltpu.make_async_copy(
            self.w_hbm.at[pl.ds(self.base + j * NSUB, NSUB)],
            self.w_vmem.at[pl.ds(j * NSUB, NSUB)],
            self.sems.at[j],
        )

    def wait_on(self, j):
        self.copy(j).wait()


def _w_copies(w_hbm, base, w_vmem, sems):
    chunks = _WeightChunks(w_hbm, base, w_vmem, sems)
    started = []
    for j in range(w_vmem.shape[0] // NSUB):
        copy = chunks.copy(j)
        copy.start()
        started.append(copy)
    return (chunks, started)


def _slot_chunks(idx_ref, base, copies, product, update):
    def chunk(j, carry):
        copies[0].wait_on(j)

        @pl.when(idx_ref[3 * (base + j * NSUB) + 2] > 0)
        def _():
            for g in range(0, NSUB, GROUP):
                ks = [j * NSUB + g + i for i in range(GROUP)]
                parts = [product(k) for k in ks]
                for k, part in zip(ks, parts):
                    update(k, part)

        return carry

    lax.fori_loop(0, len(copies[1]), chunk, 0)


def _fwd_kernel(base, layer, at_ref, idx_ref, h_ref, w_hbm, sh_in, sy_in, hout_ref, sh_ref, sy_ref, w_vmem, y_vmem, sems, io_sems):
    del sh_in, sy_in
    width = h_ref.shape[1]
    at = at_ref[0]
    copies = _w_copies(w_hbm, base, w_vmem, sems)
    save_h = pltpu.make_async_copy(h_ref, sh_ref.at[layer, at], io_sems.at[0])
    save_h.start()
    y_vmem[...] = jnp.zeros_like(y_vmem)

    def product(k):
        r = idx_ref[3 * (base + k)]
        return jnp.dot(h_ref[:, _blk(r)], w_vmem[k], preferred_element_type=jnp.float32)

    def update(k, p):
        c = idx_ref[3 * (base + k) + 1]
        y_vmem[:, _blk(c)] += p * _flag(idx_ref, base + k)

    _slot_chunks(idx_ref, base, copies, product, update)
    save_y = pltpu.make_async_copy(y_vmem, sy_ref.at[layer, at], io_sems.at[1])
    save_y.start()

    def epi(j, carry):
        y = y_vmem[:, _chunk(j)]
        h = h_ref[:, _chunk(j)].astype(jnp.float32)
        hout_ref[:, _chunk(j)] = (h + y / (1.0 + jnp.exp(-y))).astype(hout_ref.dtype)
        return carry

    lax.fori_loop(0, width // CH, epi, 0)
    save_h.wait()
    save_y.wait()


def layer_forward(h, weights, layer, block_index, at, stash_h, stash_y):
    rows, width = h.shape
    return pl.pallas_call(
        functools.partial(_fwd_kernel, layer * KMAX, layer),
        out_shape=(
            jax.ShapeDtypeStruct((rows, width), jnp.bfloat16),
            jax.ShapeDtypeStruct(stash_h.shape, stash_h.dtype),
            jax.ShapeDtypeStruct(stash_y.shape, stash_y.dtype),
        ),
        in_specs=[_SMEM, _SMEM, _VMEM, _ANY, _ANY, _ANY],
        out_specs=(_VMEM, _ANY, _ANY),
        scratch_shapes=[
            pltpu.VMEM((KMAX, BLK, BLK), weights.dtype),
            pltpu.VMEM((rows, width), jnp.float32),
            pltpu.SemaphoreType.DMA((KMAX // NSUB,)),
            pltpu.SemaphoreType.DMA((2,)),
        ],
        input_output_aliases={4: 1, 5: 2},
        compiler_params=pltpu.CompilerParams(vmem_limit_bytes=VMEM_LIMIT),
    )(at.reshape(1), block_index.reshape(-1), h, weights, stash_h, stash_y)


def _bwd_kernel(base, layer, at_ref, idx_ref, g_ref, sy_hbm, w_hbm, ss_in, gout_ref, ss_ref, y_vmem, s_vmem, sp_ref, w_vmem, sems, io_sems):
    del ss_in
    width = g_ref.shape[1]
    at = at_ref[0]
    load_y = pltpu.make_async_copy(sy_hbm.at[layer, at], y_vmem, io_sems.at[0])
    load_y.start()
    copies = _w_copies(w_hbm, base, w_vmem, sems)
    load_y.wait()

    def pre(j, carry):
        y = y_vmem[:, _chunk(j)]
        sig = 1.0 / (1.0 + jnp.exp(-y))
        g = g_ref[:, _chunk(j)].astype(jnp.float32)
        s_vmem[:, _chunk(j)] = (g * sig * (1.0 + y * (1.0 - sig))).astype(s_vmem.dtype)
        sp_ref[:, _chunk(j)] = jnp.zeros((g_ref.shape[0], CH), jnp.float32)
        return carry

    lax.fori_loop(0, width // CH, pre, 0)
    save_s = pltpu.make_async_copy(s_vmem, ss_ref.at[layer, at], io_sems.at[1])
    save_s.start()

    def product(k):
        c = idx_ref[3 * (base + k) + 1]
        return lax.dot_general(
            s_vmem[:, _blk(c)],
            w_vmem[k],
            (((1,), (1,)), ((), ())),
            preferred_element_type=jnp.float32,
        )

    def update(k, back):
        r = idx_ref[3 * (base + k)]
        sp_ref[:, _blk(r)] += back * _flag(idx_ref, base + k)

    _slot_chunks(idx_ref, base, copies, product, update)

    def epi(j, carry):
        g = g_ref[:, _chunk(j)].astype(jnp.float32)
        gout_ref[:, _chunk(j)] = (g + sp_ref[:, _chunk(j)]).astype(gout_ref.dtype)
        return carry

    lax.fori_loop(0, width // CH, epi, 0)
    save_s.wait()


def layer_backward(g, stash_y, weights, layer, block_index, at, stash_s):
    rows, width = g.shape
    return pl.pallas_call(
        functools.partial(_bwd_kernel, layer * KMAX, layer),
        out_shape=(
            jax.ShapeDtypeStruct((rows, width), jnp.bfloat16),
            jax.ShapeDtypeStruct(stash_s.shape, stash_s.dtype),
        ),
        in_specs=[_SMEM, _SMEM, _VMEM, _ANY, _ANY, _ANY],
        out_specs=(_VMEM, _ANY),
        scratch_shapes=[
            pltpu.VMEM((rows, width), jnp.float32),
            pltpu.VMEM((rows, width), jnp.bfloat16),
            pltpu.VMEM((rows, width), jnp.float32),
            pltpu.VMEM((KMAX, BLK, BLK), weights.dtype),
            pltpu.SemaphoreType.DMA((KMAX // NSUB,)),
            pltpu.SemaphoreType.DMA((2,)),
        ],
        input_output_aliases={5: 1},
        compiler_params=pltpu.CompilerParams(vmem_limit_bytes=VMEM_LIMIT),
    )(at.reshape(1), block_index.reshape(-1), g, stash_y, weights, stash_s)


def _dw_kernel(mbs, idx_ref, h_ref, s_ref, dw_ref):
    rows = h_ref.shape[1] * h_ref.shape[2]
    for j in range(dw_ref.shape[0] // NSUB):
        layer = j * NSUB // KMAX

        @pl.when(idx_ref[3 * j * NSUB + 2] > 0)
        def _():
            for k in range(j * NSUB, (j + 1) * NSUB):
                r = idx_ref[3 * k]
                c = idx_ref[3 * k + 1]
                hb = h_ref[layer, :, :, _blk(r)]
                sb = s_ref[layer, :, :, _blk(c)]
                dw_ref[k] = lax.dot_general(
                    hb.reshape(rows, BLK),
                    sb.reshape(rows, BLK),
                    (((0,), (0,)), ((), ())),
                    preferred_element_type=jnp.float32,
                ) * _flag(idx_ref, k)

        @pl.when(idx_ref[3 * j * NSUB + 2] <= 0)
        def _():
            dw_ref[pl.ds(j * NSUB, NSUB)] = jnp.zeros((NSUB, BLK, BLK), jnp.float32)


def segment_dw(stash_h, stash_s, block_index, mbs):
    return pl.pallas_call(
        functools.partial(_dw_kernel, mbs),
        out_shape=jax.ShapeDtypeStruct((block_index.shape[0], BLK, BLK), jnp.float32),
        in_specs=[_SMEM, _VMEM, _VMEM],
        out_specs=_VMEM,
        compiler_params=pltpu.CompilerParams(vmem_limit_bytes=VMEM_LIMIT),
    )(block_index.reshape(-1), stash_h, stash_s)


def _dw_half_kernel(sel_ref, idx_ref, h_ref, s_ref, out_ref):
    b0 = sel_ref[0]
    rows = h_ref.shape[1] * h_ref.shape[2]
    per = out_ref.shape[1]
    for q in range(out_ref.shape[0]):
        layer = (2 * q * per) // KMAX
        for j in range(per // NSUB):
            first = 2 * q * per + b0 * per + j * NSUB

            @pl.when(idx_ref[3 * first + 2] > 0)
            def _():
                for i in range(NSUB):
                    k = first + i
                    r = idx_ref[3 * k]
                    c = idx_ref[3 * k + 1]
                    hb = h_ref[layer, :, :, _blk(r)].reshape(rows, BLK)
                    sb = s_ref[layer, :, :, _blk(c)].reshape(rows, BLK)
                    part = lax.dot_general(
                        hb, sb, (((0,), (0,)), ((), ())), preferred_element_type=jnp.float32
                    )
                    out_ref[q, j * NSUB + i] = (part * _flag(idx_ref, k)).astype(out_ref.dtype)

            @pl.when(idx_ref[3 * first + 2] <= 0)
            def _():
                out_ref[q, pl.ds(j * NSUB, NSUB)] = jnp.zeros((NSUB, BLK, BLK), out_ref.dtype)


def dw_half(stash_h, stash_s, block_index, b0, dtype):
    per = block_index.shape[0] // 8
    return pl.pallas_call(
        _dw_half_kernel,
        out_shape=jax.ShapeDtypeStruct((4, per, BLK, BLK), dtype),
        in_specs=[_SMEM, _SMEM, _VMEM, _VMEM],
        out_specs=_VMEM,
        compiler_params=pltpu.CompilerParams(vmem_limit_bytes=VMEM_LIMIT),
    )(b0.reshape(1).astype(jnp.int32), block_index.reshape(-1), stash_h, stash_s)


def _exchange(send, pairs):
    return lax.ppermute(send.astype(jnp.bfloat16), "dp", pairs).astype(jnp.float32)


def weight_grads(stash_h, stash_s, block_index, mbs):
    n = lax.axis_size("dp")
    if n != 8:
        acc = segment_dw(stash_h, stash_s, block_index, mbs)
        return lax.psum_scatter(
            acc.astype(jnp.bfloat16), "dp", scatter_dimension=0, tiled=True
        ).astype(jnp.float32)
    d = lax.axis_index("dp")
    d0, d1, d2 = d % 2, (d // 2) % 2, d // 4
    pick = lambda a, i, axis: lax.dynamic_index_in_dim(a, i, axis, keepdims=False)
    send = dw_half(stash_h, stash_s, block_index, 1 - d0, jnp.bfloat16)
    got = lax.ppermute(send, "dp", [(i, i ^ 1) for i in range(8)])
    keep = dw_half(stash_h, stash_s, block_index, d0, jnp.float32)
    keep = keep.reshape((2, 2) + keep.shape[1:])
    got = got.reshape(keep.shape)
    core0 = d0 == 0

    def half(a, i_core0, i_core1):
        return jnp.where(core0, pick(a, i_core0, 1), pick(a, i_core1, 0)).astype(jnp.float32)

    send = half(keep, 1 - d1, 1 - d2) + half(got, 1 - d1, 1 - d2)
    got2 = _exchange(send, [(i, i ^ (2 if i % 2 == 0 else 4)) for i in range(8)])
    keep2 = half(keep, d1, d2) + half(got, d1, d2)
    rem = jnp.where(core0, d2, d1)
    send = pick(keep2, 1 - rem, 0) + pick(got2, 1 - rem, 0)
    got3 = _exchange(send, [(i, i ^ (4 if i % 2 == 0 else 2)) for i in range(8)])
    return pick(keep2, rem, 0) + pick(got2, rem, 0) + got3


def on_device(x_in, cotangent, weights, block_index):
    segments = lax.axis_size("segment")
    me_segment = lax.axis_index("segment")
    mbs, rows_dev, width = x_in.shape
    mbs, rows_dev = mbs * SPLIT, rows_dev // SPLIT
    x_in = x_in.reshape(mbs, rows_dev, width)
    cotangent = cotangent.reshape(mbs, rows_dev, width)
    idx = block_index.reshape(LSLOT, KMAX, 3)

    def tick_body(tick, carry):
        recv_f, recv_b, saved_h, saved_y, saved_s = carry
        micro_f = tick - me_segment
        live_f = (micro_f >= 0) & (micro_f < mbs)
        at_f = jnp.clip(micro_f, 0, mbs - 1)
        first = lax.dynamic_index_in_dim(x_in, at_f, 0, keepdims=False)
        start = jnp.where(me_segment == 0, first, recv_f)

        def run_f(operands):
            h, sh, sy = operands
            for layer in range(LSLOT):
                h, sh, sy = layer_forward(h, weights, layer, block_index, at_f, sh, sy)
            return (h, sh, sy)

        h_out, saved_h, saved_y = lax.cond(live_f, run_f, lambda ops: ops, (start, saved_h, saved_y))
        send_f = shifted(h_out, "segment", 1)

        micro_b = tick - (2 * segments - 2 - me_segment)
        live_b = (micro_b >= 0) & (micro_b < mbs)
        at_b = jnp.clip(micro_b, 0, mbs - 1)
        top = lax.dynamic_index_in_dim(cotangent, at_b, 0, keepdims=False)
        grad_in = jnp.where(me_segment == segments - 1, top, recv_b)
        stash_y_now = saved_y

        def run_b(operands):
            grad, ss = operands
            for layer in reversed(range(LSLOT)):
                grad, ss = layer_backward(grad, stash_y_now, weights, layer, block_index, at_b, ss)
            return (grad, ss)

        grad_out, saved_s = lax.cond(live_b, run_b, lambda ops: ops, (grad_in, saved_s))
        send_b = shifted(grad_out, "segment", -1)
        return (send_f, send_b, saved_h, saved_y, saved_s)

    stash_h = jnp.zeros((LSLOT, mbs, rows_dev, width), jnp.bfloat16)
    stash_y = jnp.zeros((LSLOT, mbs, rows_dev, width), jnp.float32)
    stash_s = jnp.zeros((LSLOT, mbs, rows_dev, width), jnp.bfloat16)
    blank = jnp.zeros((rows_dev, width), jnp.bfloat16)
    ticks = mbs + 2 * segments - 2
    carry = (blank, blank, stash_h, stash_y, stash_s)
    for tick in range(ticks):
        carry = tick_body(tick, carry)
    unused_f, unused_b, stash_h, stash_y, stash_s = carry
    return weight_grads(stash_h, stash_s, block_index, mbs)


def solution(mesh):
    return jax.shard_map(
        on_device,
        mesh=mesh,
        in_specs=(
            P(None, "dp", None),
            P(None, "dp", None),
            P("segment", None, None),
            P("segment", None),
        ),
        out_specs=P(("segment", "dp"), None, None),
        check_vma=False,
    )
```

```python
import functools

import jax
import jax.numpy as jnp
from jax import lax
from jax.experimental import pallas as pl
from jax.experimental.pallas import tpu as pltpu
from jax.sharding import PartitionSpec as P

BLK = 128
LSLOT = 2
KMAX = 128
CH = 512
NSUB = 16
SPLIT = 2
GROUP = 8
VMEM_LIMIT = 60 * 1024 * 1024

_SMEM = pl.BlockSpec(memory_space=pltpu.SMEM)
_VMEM = pl.BlockSpec(memory_space=pltpu.VMEM)
_ANY = pl.BlockSpec(memory_space=pl.ANY)


def shifted(value, axis, steps):
    count = lax.axis_size(axis)
    leading, last = (max(0, -steps), min(count, count - steps))
    return lax.ppermute(value, axis, [(source, source + steps) for source in range(leading, last)])


def _blk(i):
    return pl.ds(pl.multiple_of(i * BLK, BLK), BLK)


def _chunk(j):
    return pl.ds(pl.multiple_of(j * CH, CH), CH)


def _flag(idx_ref, k):
    return jnp.where(idx_ref[3 * k + 2] > 0, 1.0, 0.0).astype(jnp.float32)


class _WeightChunks:
    def __init__(self, w_hbm, base, w_vmem, sems):
        self.w_hbm, self.base, self.w_vmem, self.sems = w_hbm, base, w_vmem, sems

    def copy(self, j):
        return pltpu.make_async_copy(
            self.w_hbm.at[pl.ds(self.base + j * NSUB, NSUB)],
            self.w_vmem.at[pl.ds(j * NSUB, NSUB)],
            self.sems.at[j],
        )

    def wait_on(self, j):
        self.copy(j).wait()


def _w_copies(w_hbm, base, w_vmem, sems):
    chunks = _WeightChunks(w_hbm, base, w_vmem, sems)
    started = []
    for j in range(w_vmem.shape[0] // NSUB):
        copy = chunks.copy(j)
        copy.start()
        started.append(copy)
    return (chunks, started)


def _slot_chunks(idx_ref, base, copies, product, update):
    def chunk(j, carry):
        copies[0].wait_on(j)

        @pl.when(idx_ref[3 * (base + j * NSUB) + 2] > 0)
        def _():
            for g in range(0, NSUB, GROUP):
                ks = [j * NSUB + g + i for i in range(GROUP)]
                parts = [product(k) for k in ks]
                for k, part in zip(ks, parts):
                    update(k, part)

        return carry

    lax.fori_loop(0, len(copies[1]), chunk, 0)


def _pick_input(at, src_ref, local_hbm, h_ref, sem):
    @pl.when(at[1] > 0)
    def _():
        pltpu.make_async_copy(local_hbm.at[at[0]], h_ref, sem).start()

    @pl.when(at[1] <= 0)
    def _():
        pltpu.make_async_copy(src_ref, h_ref, sem).start()

    pltpu.make_async_copy(src_ref, h_ref, sem).wait()


def _fwd_kernel(base, layer, at_ref, idx_ref, h_in, w_hbm, sh_in, sy_in, *rest):
    if layer == 0:
        local_hbm, hout_ref, sh_ref, sy_ref, w_vmem, y_vmem, sems, io_sems, h_ref = rest
    else:
        hout_ref, sh_ref, sy_ref, w_vmem, y_vmem, sems, io_sems = rest
        h_ref = h_in
    del sh_in, sy_in
    width = h_ref.shape[1]
    at = at_ref[0]
    copies = _w_copies(w_hbm, base, w_vmem, sems)
    if layer == 0:
        _pick_input((at, at_ref[1]), h_in, local_hbm, h_ref, io_sems.at[2])
    save_h = pltpu.make_async_copy(h_ref, sh_ref.at[layer, at], io_sems.at[0])
    save_h.start()
    y_vmem[...] = jnp.zeros_like(y_vmem)

    def product(k):
        r = idx_ref[3 * (base + k)]
        return jnp.dot(h_ref[:, _blk(r)], w_vmem[k], preferred_element_type=jnp.float32)

    def update(k, p):
        c = idx_ref[3 * (base + k) + 1]
        y_vmem[:, _blk(c)] += p * _flag(idx_ref, base + k)

    _slot_chunks(idx_ref, base, copies, product, update)
    save_y = pltpu.make_async_copy(y_vmem, sy_ref.at[layer, at], io_sems.at[1])
    save_y.start()

    def epi(j, carry):
        y = y_vmem[:, _chunk(j)]
        h = h_ref[:, _chunk(j)].astype(jnp.float32)
        hout_ref[:, _chunk(j)] = (h + y / (1.0 + jnp.exp(-y))).astype(hout_ref.dtype)
        return carry

    lax.fori_loop(0, width // CH, epi, 0)
    save_h.wait()
    save_y.wait()


def layer_forward(h, weights, layer, block_index, at, stash_h, stash_y, local=None, use_local=None):
    rows, width = h.shape
    extra_in, extra_args, extra_scratch = [], [], []
    if layer == 0:
        extra_in, extra_args = [_ANY], [local]
        extra_scratch = [pltpu.VMEM((rows, width), h.dtype)]
        at = jnp.stack([at, use_local.astype(jnp.int32)])
    return pl.pallas_call(
        functools.partial(_fwd_kernel, layer * KMAX, layer),
        out_shape=(
            jax.ShapeDtypeStruct((rows, width), jnp.bfloat16),
            jax.ShapeDtypeStruct(stash_h.shape, stash_h.dtype),
            jax.ShapeDtypeStruct(stash_y.shape, stash_y.dtype),
        ),
        in_specs=[_SMEM, _SMEM, _VMEM, _ANY, _ANY, _ANY] + extra_in,
        out_specs=(_VMEM, _ANY, _ANY),
        scratch_shapes=[
            pltpu.VMEM((KMAX, BLK, BLK), weights.dtype),
            pltpu.VMEM((rows, width), jnp.float32),
            pltpu.SemaphoreType.DMA((KMAX // NSUB,)),
            pltpu.SemaphoreType.DMA((3,)),
        ]
        + extra_scratch,
        input_output_aliases={4: 1, 5: 2},
        compiler_params=pltpu.CompilerParams(vmem_limit_bytes=VMEM_LIMIT),
    )(at.reshape(-1), block_index.reshape(-1), h, weights, stash_h, stash_y, *extra_args)


def _bwd_kernel(base, layer, entry, at_ref, idx_ref, g_in, sy_hbm, w_hbm, ss_in, *rest):
    if entry:
        local_hbm, gout_ref, ss_ref, y_vmem, s_vmem, sp_ref, w_vmem, sems, io_sems, g_ref = rest
    else:
        gout_ref, ss_ref, y_vmem, s_vmem, sp_ref, w_vmem, sems, io_sems = rest
        g_ref = g_in
    del ss_in
    width = g_ref.shape[1]
    at = at_ref[0]
    if entry:
        _pick_input((at, at_ref[1]), g_in, local_hbm, g_ref, io_sems.at[2])
    load_y = pltpu.make_async_copy(sy_hbm.at[layer, at], y_vmem, io_sems.at[0])
    load_y.start()
    copies = _w_copies(w_hbm, base, w_vmem, sems)
    load_y.wait()

    def pre(j, carry):
        y = y_vmem[:, _chunk(j)]
        sig = 1.0 / (1.0 + jnp.exp(-y))
        g = g_ref[:, _chunk(j)].astype(jnp.float32)
        s_vmem[:, _chunk(j)] = (g * sig * (1.0 + y * (1.0 - sig))).astype(s_vmem.dtype)
        sp_ref[:, _chunk(j)] = jnp.zeros((g_ref.shape[0], CH), jnp.float32)
        return carry

    lax.fori_loop(0, width // CH, pre, 0)
    save_s = pltpu.make_async_copy(s_vmem, ss_ref.at[layer, at], io_sems.at[1])
    save_s.start()

    def product(k):
        c = idx_ref[3 * (base + k) + 1]
        return lax.dot_general(
            s_vmem[:, _blk(c)],
            w_vmem[k],
            (((1,), (1,)), ((), ())),
            preferred_element_type=jnp.float32,
        )

    def update(k, back):
        r = idx_ref[3 * (base + k)]
        sp_ref[:, _blk(r)] += back * _flag(idx_ref, base + k)

    _slot_chunks(idx_ref, base, copies, product, update)

    def epi(j, carry):
        g = g_ref[:, _chunk(j)].astype(jnp.float32)
        gout_ref[:, _chunk(j)] = (g + sp_ref[:, _chunk(j)]).astype(gout_ref.dtype)
        return carry

    lax.fori_loop(0, width // CH, epi, 0)
    save_s.wait()


def layer_backward(g, stash_y, weights, layer, block_index, at, stash_s, local=None, use_local=None):
    rows, width = g.shape
    entry = local is not None
    extra_in, extra_args, extra_scratch = [], [], []
    if entry:
        extra_in, extra_args = [_ANY], [local]
        extra_scratch = [pltpu.VMEM((rows, width), g.dtype)]
        at = jnp.stack([at, use_local.astype(jnp.int32)])
    return pl.pallas_call(
        functools.partial(_bwd_kernel, layer * KMAX, layer, entry),
        out_shape=(
            jax.ShapeDtypeStruct((rows, width), jnp.bfloat16),
            jax.ShapeDtypeStruct(stash_s.shape, stash_s.dtype),
        ),
        in_specs=[_SMEM, _SMEM, _VMEM, _ANY, _ANY, _ANY] + extra_in,
        out_specs=(_VMEM, _ANY),
        scratch_shapes=[
            pltpu.VMEM((rows, width), jnp.float32),
            pltpu.VMEM((rows, width), jnp.bfloat16),
            pltpu.VMEM((rows, width), jnp.float32),
            pltpu.VMEM((KMAX, BLK, BLK), weights.dtype),
            pltpu.SemaphoreType.DMA((KMAX // NSUB,)),
            pltpu.SemaphoreType.DMA((3,)),
        ]
        + extra_scratch,
        input_output_aliases={5: 1},
        compiler_params=pltpu.CompilerParams(vmem_limit_bytes=VMEM_LIMIT),
    )(at.reshape(-1), block_index.reshape(-1), g, stash_y, weights, stash_s, *extra_args)


def _dw_kernel(mbs, idx_ref, h_ref, s_ref, dw_ref):
    rows = h_ref.shape[1] * h_ref.shape[2]
    for j in range(dw_ref.shape[0] // NSUB):
        layer = j * NSUB // KMAX

        @pl.when(idx_ref[3 * j * NSUB + 2] > 0)
        def _():
            for k in range(j * NSUB, (j + 1) * NSUB):
                r = idx_ref[3 * k]
                c = idx_ref[3 * k + 1]
                hb = h_ref[layer, :, :, _blk(r)]
                sb = s_ref[layer, :, :, _blk(c)]
                dw_ref[k] = lax.dot_general(
                    hb.reshape(rows, BLK),
                    sb.reshape(rows, BLK),
                    (((0,), (0,)), ((), ())),
                    preferred_element_type=jnp.float32,
                ) * _flag(idx_ref, k)

        @pl.when(idx_ref[3 * j * NSUB + 2] <= 0)
        def _():
            dw_ref[pl.ds(j * NSUB, NSUB)] = jnp.zeros((NSUB, BLK, BLK), jnp.float32)


def segment_dw(stash_h, stash_s, block_index, mbs):
    return pl.pallas_call(
        functools.partial(_dw_kernel, mbs),
        out_shape=jax.ShapeDtypeStruct((block_index.shape[0], BLK, BLK), jnp.float32),
        in_specs=[_SMEM, _VMEM, _VMEM],
        out_specs=_VMEM,
        compiler_params=pltpu.CompilerParams(vmem_limit_bytes=VMEM_LIMIT),
    )(block_index.reshape(-1), stash_h, stash_s)


def _dw_half_kernel(sel_ref, idx_ref, h_ref, s_ref, out_ref):
    b0 = sel_ref[0]
    rows = h_ref.shape[1] * h_ref.shape[2]
    per = out_ref.shape[1]
    for q in range(out_ref.shape[0]):
        layer = (2 * q * per) // KMAX
        for j in range(per // NSUB):
            first = 2 * q * per + b0 * per + j * NSUB

            @pl.when(idx_ref[3 * first + 2] > 0)
            def _():
                for i in range(NSUB):
                    k = first + i
                    r = idx_ref[3 * k]
                    c = idx_ref[3 * k + 1]
                    hb = h_ref[layer, :, :, _blk(r)].reshape(rows, BLK)
                    sb = s_ref[layer, :, :, _blk(c)].reshape(rows, BLK)
                    part = lax.dot_general(
                        hb, sb, (((0,), (0,)), ((), ())), preferred_element_type=jnp.float32
                    )
                    out_ref[q, j * NSUB + i] = (part * _flag(idx_ref, k)).astype(out_ref.dtype)

            @pl.when(idx_ref[3 * first + 2] <= 0)
            def _():
                out_ref[q, pl.ds(j * NSUB, NSUB)] = jnp.zeros((NSUB, BLK, BLK), out_ref.dtype)


def dw_half(stash_h, stash_s, block_index, b0, dtype):
    per = block_index.shape[0] // 8
    return pl.pallas_call(
        _dw_half_kernel,
        out_shape=jax.ShapeDtypeStruct((4, per, BLK, BLK), dtype),
        in_specs=[_SMEM, _SMEM, _VMEM, _VMEM],
        out_specs=_VMEM,
        compiler_params=pltpu.CompilerParams(vmem_limit_bytes=VMEM_LIMIT),
    )(b0.reshape(1).astype(jnp.int32), block_index.reshape(-1), stash_h, stash_s)


def _exchange(send, pairs):
    return lax.ppermute(send.astype(jnp.bfloat16), "dp", pairs).astype(jnp.float32)


def weight_grads(stash_h, stash_s, block_index, mbs):
    n = lax.axis_size("dp")
    if n != 8:
        acc = segment_dw(stash_h, stash_s, block_index, mbs)
        return lax.psum_scatter(
            acc.astype(jnp.bfloat16), "dp", scatter_dimension=0, tiled=True
        ).astype(jnp.float32)
    d = lax.axis_index("dp")
    d0, d1, d2 = d % 2, (d // 2) % 2, d // 4
    pick = lambda a, i, axis: lax.dynamic_index_in_dim(a, i, axis, keepdims=False)
    send = dw_half(stash_h, stash_s, block_index, 1 - d0, jnp.bfloat16)
    got = lax.ppermute(send, "dp", [(i, i ^ 1) for i in range(8)])
    keep = dw_half(stash_h, stash_s, block_index, d0, jnp.float32)
    keep = keep.reshape((2, 2) + keep.shape[1:])
    got = got.reshape(keep.shape)
    core0 = d0 == 0

    def half(a, i_core0, i_core1):
        return jnp.where(core0, pick(a, i_core0, 1), pick(a, i_core1, 0)).astype(jnp.float32)

    send = half(keep, 1 - d1, 1 - d2) + half(got, 1 - d1, 1 - d2)
    got2 = _exchange(send, [(i, i ^ (2 if i % 2 == 0 else 4)) for i in range(8)])
    keep2 = half(keep, d1, d2) + half(got, d1, d2) + got2
    rem = jnp.where(core0, d2, d1)
    got3 = _exchange(pick(keep2, 1 - rem, 0), [(i, i ^ (4 if i % 2 == 0 else 2)) for i in range(8)])
    return pick(keep2, rem, 0) + got3


def on_device(x_in, cotangent, weights, block_index):
    segments = lax.axis_size("segment")
    me_segment = lax.axis_index("segment")
    mbs, rows_dev, width = x_in.shape
    mbs, rows_dev = mbs * SPLIT, rows_dev // SPLIT
    x_in = x_in.reshape(mbs, rows_dev, width)
    cotangent = cotangent.reshape(mbs, rows_dev, width)
    idx = block_index.reshape(LSLOT, KMAX, 3)

    def tick_body(tick, carry):
        recv_f, recv_b, saved_h, saved_y, saved_s = carry
        micro_f = tick - me_segment
        live_f = (micro_f >= 0) & (micro_f < mbs)
        at_f = jnp.clip(micro_f, 0, mbs - 1)
        def run_f(operands):
            h, sh, sy = operands
            for layer in range(LSLOT):
                local = (x_in, me_segment == 0) if layer == 0 else (None, None)
                h, sh, sy = layer_forward(h, weights, layer, block_index, at_f, sh, sy, *local)
            return (h, sh, sy)

        h_out, saved_h, saved_y = lax.cond(live_f, run_f, lambda ops: ops, (recv_f, saved_h, saved_y))
        send_f = shifted(h_out, "segment", 1)

        micro_b = tick - (2 * segments - 2 - me_segment)
        live_b = (micro_b >= 0) & (micro_b < mbs)
        at_b = jnp.clip(micro_b, 0, mbs - 1)
        stash_y_now = saved_y

        def run_b(operands):
            grad, ss = operands
            for layer in reversed(range(LSLOT)):
                local = (cotangent, me_segment == segments - 1) if layer == LSLOT - 1 else (None, None)
                grad, ss = layer_backward(grad, stash_y_now, weights, layer, block_index, at_b, ss, *local)
            return (grad, ss)

        grad_out, saved_s = lax.cond(live_b, run_b, lambda ops: ops, (recv_b, saved_s))
        send_b = shifted(grad_out, "segment", -1)
        return (send_f, send_b, saved_h, saved_y, saved_s)

    stash_h = jnp.zeros((LSLOT, mbs, rows_dev, width), jnp.bfloat16)
    stash_y = jnp.zeros((LSLOT, mbs, rows_dev, width), jnp.float32)
    stash_s = jnp.zeros((LSLOT, mbs, rows_dev, width), jnp.bfloat16)
    blank = jnp.zeros((rows_dev, width), jnp.bfloat16)
    ticks = mbs + 2 * segments - 2
    carry = (blank, blank, stash_h, stash_y, stash_s)
    for tick in range(ticks):
        carry = tick_body(tick, carry)
    unused_f, unused_b, stash_h, stash_y, stash_s = carry
    return weight_grads(stash_h, stash_s, block_index, mbs)


def solution(mesh):
    return jax.shard_map(
        on_device,
        mesh=mesh,
        in_specs=(
            P(None, "dp", None),
            P(None, "dp", None),
            P("segment", None, None),
            P("segment", None),
        ),
        out_specs=P(("segment", "dp"), None, None),
        check_vma=False,
    )
```

```python
import functools

import jax
import jax.numpy as jnp
from jax import lax
from jax.experimental import pallas as pl
from jax.experimental.pallas import tpu as pltpu
from jax.sharding import PartitionSpec as P

BLK = 128
LSLOT = 2
KMAX = 128
CH = 512
NSUB = 16
SPLIT = 2
GROUP = 8
VMEM_LIMIT = 60 * 1024 * 1024

_SMEM = pl.BlockSpec(memory_space=pltpu.SMEM)
_VMEM = pl.BlockSpec(memory_space=pltpu.VMEM)
_ANY = pl.BlockSpec(memory_space=pl.ANY)


def shifted(value, axis, steps):
    count = lax.axis_size(axis)
    leading, last = (max(0, -steps), min(count, count - steps))
    return lax.ppermute(value, axis, [(source, source + steps) for source in range(leading, last)])


def _blk(i):
    return pl.ds(pl.multiple_of(i * BLK, BLK), BLK)


def _chunk(j):
    return pl.ds(pl.multiple_of(j * CH, CH), CH)


def _flag(idx_ref, k):
    return jnp.where(idx_ref[3 * k + 2] > 0, 1.0, 0.0).astype(jnp.float32)


class _WeightChunks:
    def __init__(self, w_hbm, base, w_vmem, sems):
        self.w_hbm, self.base, self.w_vmem, self.sems = w_hbm, base, w_vmem, sems

    def copy(self, j):
        return pltpu.make_async_copy(
            self.w_hbm.at[pl.ds(self.base + j * NSUB, NSUB)],
            self.w_vmem.at[pl.ds(j * NSUB, NSUB)],
            self.sems.at[j],
        )

    def wait_on(self, j):
        self.copy(j).wait()


def _w_copies(w_hbm, base, w_vmem, sems):
    chunks = _WeightChunks(w_hbm, base, w_vmem, sems)
    started = []
    for j in range(w_vmem.shape[0] // NSUB):
        copy = chunks.copy(j)
        copy.start()
        started.append(copy)
    return (chunks, started)


def _slot_chunks(idx_ref, base, copies, product, update):
    def chunk(j, carry):
        copies[0].wait_on(j)

        @pl.when(idx_ref[3 * (base + j * NSUB) + 2] > 0)
        def _():
            for g in range(0, NSUB, GROUP):
                ks = [j * NSUB + g + i for i in range(GROUP)]
                parts = [product(k) for k in ks]
                for k, part in zip(ks, parts):
                    update(k, part)

        return carry

    lax.fori_loop(0, len(copies[1]), chunk, 0)


def _pick_input(at, src_ref, local_hbm, h_ref, sem):
    @pl.when(at[1] > 0)
    def _():
        pltpu.make_async_copy(local_hbm.at[at[0]], h_ref, sem).start()

    @pl.when(at[1] <= 0)
    def _():
        pltpu.make_async_copy(src_ref, h_ref, sem).start()

    pltpu.make_async_copy(src_ref, h_ref, sem).wait()


def _fwd_kernel(base, layer, at_ref, idx_ref, h_in, w_hbm, sh_in, sy_in, *rest):
    if layer == 0:
        local_hbm, hout_ref, sh_ref, sy_ref, w_vmem, y_vmem, sems, io_sems, h_ref = rest
    else:
        hout_ref, sh_ref, sy_ref, w_vmem, y_vmem, sems, io_sems = rest
        h_ref = h_in
    del sh_in, sy_in
    width = h_ref.shape[1]
    at = at_ref[0]
    copies = _w_copies(w_hbm, base, w_vmem, sems)
    if layer == 0:
        _pick_input((at, at_ref[1]), h_in, local_hbm, h_ref, io_sems.at[2])
    save_h = pltpu.make_async_copy(h_ref, sh_ref.at[layer, at], io_sems.at[0])
    save_h.start()
    y_vmem[...] = jnp.zeros_like(y_vmem)

    def product(k):
        r = idx_ref[3 * (base + k)]
        return jnp.dot(h_ref[:, _blk(r)], w_vmem[k], preferred_element_type=jnp.float32)

    def update(k, p):
        c = idx_ref[3 * (base + k) + 1]
        y_vmem[:, _blk(c)] += p * _flag(idx_ref, base + k)

    _slot_chunks(idx_ref, base, copies, product, update)
    save_y = pltpu.make_async_copy(y_vmem, sy_ref.at[layer, at], io_sems.at[1])
    save_y.start()

    def epi(j, carry):
        y = y_vmem[:, _chunk(j)]
        h = h_ref[:, _chunk(j)].astype(jnp.float32)
        hout_ref[:, _chunk(j)] = (h + y / (1.0 + jnp.exp(-y))).astype(hout_ref.dtype)
        return carry

    lax.fori_loop(0, width // CH, epi, 0)
    save_h.wait()
    save_y.wait()


def layer_forward(h, weights, layer, block_index, at, stash_h, stash_y, local=None, use_local=None):
    rows, width = h.shape
    extra_in, extra_args, extra_scratch = [], [], []
    if layer == 0:
        extra_in, extra_args = [_ANY], [local]
        extra_scratch = [pltpu.VMEM((rows, width), h.dtype)]
        at = jnp.stack([at, use_local.astype(jnp.int32)])
    return pl.pallas_call(
        functools.partial(_fwd_kernel, layer * KMAX, layer),
        out_shape=(
            jax.ShapeDtypeStruct((rows, width), jnp.bfloat16),
            jax.ShapeDtypeStruct(stash_h.shape, stash_h.dtype),
            jax.ShapeDtypeStruct(stash_y.shape, stash_y.dtype),
        ),
        in_specs=[_SMEM, _SMEM, _VMEM, _ANY, _ANY, _ANY] + extra_in,
        out_specs=(_VMEM, _ANY, _ANY),
        scratch_shapes=[
            pltpu.VMEM((KMAX, BLK, BLK), weights.dtype),
            pltpu.VMEM((rows, width), jnp.float32),
            pltpu.SemaphoreType.DMA((KMAX // NSUB,)),
            pltpu.SemaphoreType.DMA((3,)),
        ]
        + extra_scratch,
        input_output_aliases={4: 1, 5: 2},
        compiler_params=pltpu.CompilerParams(vmem_limit_bytes=VMEM_LIMIT),
    )(at.reshape(-1), block_index.reshape(-1), h, weights, stash_h, stash_y, *extra_args)


def _bwd_kernel(base, layer, entry, at_ref, idx_ref, g_in, sy_hbm, w_hbm, ss_in, *rest):
    if entry:
        local_hbm, gout_ref, ss_ref, y_vmem, s_vmem, sp_ref, w_vmem, sems, io_sems, g_ref = rest
    else:
        gout_ref, ss_ref, y_vmem, s_vmem, sp_ref, w_vmem, sems, io_sems = rest
        g_ref = g_in
    del ss_in
    width = g_ref.shape[1]
    at = at_ref[0]
    if entry:
        _pick_input((at, at_ref[1]), g_in, local_hbm, g_ref, io_sems.at[2])
    load_y = pltpu.make_async_copy(sy_hbm.at[layer, at], y_vmem, io_sems.at[0])
    load_y.start()
    copies = _w_copies(w_hbm, base, w_vmem, sems)
    load_y.wait()

    def pre(j, carry):
        y = y_vmem[:, _chunk(j)]
        sig = 1.0 / (1.0 + jnp.exp(-y))
        g = g_ref[:, _chunk(j)].astype(jnp.float32)
        s_vmem[:, _chunk(j)] = (g * sig * (1.0 + y * (1.0 - sig))).astype(s_vmem.dtype)
        sp_ref[:, _chunk(j)] = jnp.zeros((g_ref.shape[0], CH), jnp.float32)
        return carry

    lax.fori_loop(0, width // CH, pre, 0)
    save_s = pltpu.make_async_copy(s_vmem, ss_ref.at[layer, at], io_sems.at[1])
    save_s.start()

    def product(k):
        c = idx_ref[3 * (base + k) + 1]
        return lax.dot_general(
            s_vmem[:, _blk(c)],
            w_vmem[k],
            (((1,), (1,)), ((), ())),
            preferred_element_type=jnp.float32,
        )

    def update(k, back):
        r = idx_ref[3 * (base + k)]
        sp_ref[:, _blk(r)] += back * _flag(idx_ref, base + k)

    _slot_chunks(idx_ref, base, copies, product, update)

    def epi(j, carry):
        g = g_ref[:, _chunk(j)].astype(jnp.float32)
        gout_ref[:, _chunk(j)] = (g + sp_ref[:, _chunk(j)]).astype(gout_ref.dtype)
        return carry

    lax.fori_loop(0, width // CH, epi, 0)
    save_s.wait()


def layer_backward(g, stash_y, weights, layer, block_index, at, stash_s, local=None, use_local=None):
    rows, width = g.shape
    entry = local is not None
    extra_in, extra_args, extra_scratch = [], [], []
    if entry:
        extra_in, extra_args = [_ANY], [local]
        extra_scratch = [pltpu.VMEM((rows, width), g.dtype)]
        at = jnp.stack([at, use_local.astype(jnp.int32)])
    return pl.pallas_call(
        functools.partial(_bwd_kernel, layer * KMAX, layer, entry),
        out_shape=(
            jax.ShapeDtypeStruct((rows, width), jnp.bfloat16),
            jax.ShapeDtypeStruct(stash_s.shape, stash_s.dtype),
        ),
        in_specs=[_SMEM, _SMEM, _VMEM, _ANY, _ANY, _ANY] + extra_in,
        out_specs=(_VMEM, _ANY),
        scratch_shapes=[
            pltpu.VMEM((rows, width), jnp.float32),
            pltpu.VMEM((rows, width), jnp.bfloat16),
            pltpu.VMEM((rows, width), jnp.float32),
            pltpu.VMEM((KMAX, BLK, BLK), weights.dtype),
            pltpu.SemaphoreType.DMA((KMAX // NSUB,)),
            pltpu.SemaphoreType.DMA((3,)),
        ]
        + extra_scratch,
        input_output_aliases={5: 1},
        compiler_params=pltpu.CompilerParams(vmem_limit_bytes=VMEM_LIMIT),
    )(at.reshape(-1), block_index.reshape(-1), g, stash_y, weights, stash_s, *extra_args)


def _dw_kernel(mbs, idx_ref, h_ref, s_ref, dw_ref):
    rows = h_ref.shape[1] * h_ref.shape[2]
    for j in range(dw_ref.shape[0] // NSUB):
        layer = j * NSUB // KMAX

        @pl.when(idx_ref[3 * j * NSUB + 2] > 0)
        def _():
            for k in range(j * NSUB, (j + 1) * NSUB):
                r = idx_ref[3 * k]
                c = idx_ref[3 * k + 1]
                hb = h_ref[layer, :, :, _blk(r)]
                sb = s_ref[layer, :, :, _blk(c)]
                dw_ref[k] = lax.dot_general(
                    hb.reshape(rows, BLK),
                    sb.reshape(rows, BLK),
                    (((0,), (0,)), ((), ())),
                    preferred_element_type=jnp.float32,
                ) * _flag(idx_ref, k)

        @pl.when(idx_ref[3 * j * NSUB + 2] <= 0)
        def _():
            dw_ref[pl.ds(j * NSUB, NSUB)] = jnp.zeros((NSUB, BLK, BLK), jnp.float32)


def segment_dw(stash_h, stash_s, block_index, mbs):
    return pl.pallas_call(
        functools.partial(_dw_kernel, mbs),
        out_shape=jax.ShapeDtypeStruct((block_index.shape[0], BLK, BLK), jnp.float32),
        in_specs=[_SMEM, _VMEM, _VMEM],
        out_specs=_VMEM,
        compiler_params=pltpu.CompilerParams(vmem_limit_bytes=VMEM_LIMIT),
    )(block_index.reshape(-1), stash_h, stash_s)


def _dw_half_kernel(sel_ref, idx_ref, h_ref, s_ref, out_ref):
    b0 = sel_ref[0]
    rows = h_ref.shape[1] * h_ref.shape[2]
    per = out_ref.shape[1]
    for q in range(out_ref.shape[0]):
        layer = (2 * q * per) // KMAX
        spot = q + b0 * ((q % 2) * 2 + q // 2 - q)
        for j in range(per // NSUB):
            first = 2 * q * per + b0 * per + j * NSUB

            @pl.when(idx_ref[3 * first + 2] > 0)
            def _():
                for i in range(NSUB):
                    k = first + i
                    r = idx_ref[3 * k]
                    c = idx_ref[3 * k + 1]
                    hb = h_ref[layer, :, :, _blk(r)].reshape(rows, BLK)
                    sb = s_ref[layer, :, :, _blk(c)].reshape(rows, BLK)
                    part = lax.dot_general(
                        hb, sb, (((0,), (0,)), ((), ())), preferred_element_type=jnp.float32
                    )
                    out_ref[spot, j * NSUB + i] = (part * _flag(idx_ref, k)).astype(out_ref.dtype)

            @pl.when(idx_ref[3 * first + 2] <= 0)
            def _():
                out_ref[spot, pl.ds(j * NSUB, NSUB)] = jnp.zeros((NSUB, BLK, BLK), out_ref.dtype)


def dw_half(stash_h, stash_s, block_index, b0, dtype):
    per = block_index.shape[0] // 8
    return pl.pallas_call(
        _dw_half_kernel,
        out_shape=jax.ShapeDtypeStruct((4, per, BLK, BLK), dtype),
        in_specs=[_SMEM, _SMEM, _VMEM, _VMEM],
        out_specs=_VMEM,
        compiler_params=pltpu.CompilerParams(vmem_limit_bytes=VMEM_LIMIT),
    )(b0.reshape(1).astype(jnp.int32), block_index.reshape(-1), stash_h, stash_s)


def _exchange(send, pairs):
    return lax.ppermute(send.astype(jnp.bfloat16), "dp", pairs).astype(jnp.float32)


def weight_grads(stash_h, stash_s, block_index, mbs):
    n = lax.axis_size("dp")
    if n != 8:
        acc = segment_dw(stash_h, stash_s, block_index, mbs)
        return lax.psum_scatter(
            acc.astype(jnp.bfloat16), "dp", scatter_dimension=0, tiled=True
        ).astype(jnp.float32)
    d = lax.axis_index("dp")
    d0, d1, d2 = d % 2, (d // 2) % 2, d // 4
    pick = lambda a, i, axis: lax.dynamic_index_in_dim(a, i, axis, keepdims=False)
    send = dw_half(stash_h, stash_s, block_index, 1 - d0, jnp.bfloat16)
    got = lax.ppermute(send, "dp", [(i, i ^ 1) for i in range(8)])
    keep = dw_half(stash_h, stash_s, block_index, d0, jnp.float32)
    keep = keep.reshape((2, 2) + keep.shape[1:])
    got = got.reshape(keep.shape).astype(jnp.float32)
    core0 = d0 == 0
    flip = jnp.where(core0, d1, d2)
    send = pick(keep, 1 - flip, 1) + pick(got, 1 - flip, 1)
    got2 = _exchange(send, [(i, i ^ (2 if i % 2 == 0 else 4)) for i in range(8)])
    keep2 = pick(keep, flip, 1) + pick(got, flip, 1) + got2
    rem = jnp.where(core0, d2, d1)
    got3 = _exchange(pick(keep2, 1 - rem, 0), [(i, i ^ (4 if i % 2 == 0 else 2)) for i in range(8)])
    return pick(keep2, rem, 0) + got3


def _allocate_kernel(*refs):
    del refs


def allocate(specs):
    return pl.pallas_call(
        _allocate_kernel,
        out_shape=tuple(jax.ShapeDtypeStruct(shape, dtype) for shape, dtype in specs),
        out_specs=tuple(_ANY for _ in specs),
    )()


def on_device(x_in, cotangent, weights, block_index):
    segments = lax.axis_size("segment")
    me_segment = lax.axis_index("segment")
    mbs, rows_dev, width = x_in.shape
    mbs, rows_dev = mbs * SPLIT, rows_dev // SPLIT
    x_in = x_in.reshape(mbs, rows_dev, width)
    cotangent = cotangent.reshape(mbs, rows_dev, width)
    idx = block_index.reshape(LSLOT, KMAX, 3)

    def tick_body(tick, carry):
        recv_f, recv_b, saved_h, saved_y, saved_s = carry
        micro_f = tick - me_segment
        live_f = (micro_f >= 0) & (micro_f < mbs)
        at_f = jnp.clip(micro_f, 0, mbs - 1)
        def run_f(operands):
            h, sh, sy = operands
            for layer in range(LSLOT):
                local = (x_in, me_segment == 0) if layer == 0 else (None, None)
                h, sh, sy = layer_forward(h, weights, layer, block_index, at_f, sh, sy, *local)
            return (h, sh, sy)

        h_out, saved_h, saved_y = lax.cond(live_f, run_f, lambda ops: ops, (recv_f, saved_h, saved_y))
        send_f = shifted(h_out, "segment", 1)

        micro_b = tick - (2 * segments - 2 - me_segment)
        live_b = (micro_b >= 0) & (micro_b < mbs)
        at_b = jnp.clip(micro_b, 0, mbs - 1)
        stash_y_now = saved_y

        def run_b(operands):
            grad, ss = operands
            for layer in reversed(range(LSLOT)):
                local = (cotangent, me_segment == segments - 1) if layer == LSLOT - 1 else (None, None)
                grad, ss = layer_backward(grad, stash_y_now, weights, layer, block_index, at_b, ss, *local)
            return (grad, ss)

        grad_out, saved_s = lax.cond(live_b, run_b, lambda ops: ops, (recv_b, saved_s))
        send_b = shifted(grad_out, "segment", -1)
        return (send_f, send_b, saved_h, saved_y, saved_s)

    stash_shape = (LSLOT, mbs, rows_dev, width)
    stash_h, stash_y, stash_s = allocate(
        [(stash_shape, jnp.bfloat16), (stash_shape, jnp.float32), (stash_shape, jnp.bfloat16)]
    )
    blank = jnp.zeros((rows_dev, width), jnp.bfloat16)
    ticks = mbs + 2 * segments - 2
    carry = (blank, blank, stash_h, stash_y, stash_s)
    for tick in range(ticks):
        carry = tick_body(tick, carry)
    unused_f, unused_b, stash_h, stash_y, stash_s = carry
    return weight_grads(stash_h, stash_s, block_index, mbs)


def solution(mesh):
    return jax.shard_map(
        on_device,
        mesh=mesh,
        in_specs=(
            P(None, "dp", None),
            P(None, "dp", None),
            P("segment", None, None),
            P("segment", None),
        ),
        out_specs=P(("segment", "dp"), None, None),
        check_vma=False,
    )
```

```python
import functools

import jax
import jax.numpy as jnp
from jax import lax
from jax.experimental import pallas as pl
from jax.experimental.pallas import tpu as pltpu
from jax.sharding import PartitionSpec as P

BLK = 128
LSLOT = 2
KMAX = 128
CH = 512
NSUB = 16
SPLIT = 2
GROUP = 8
VMEM_LIMIT = 60 * 1024 * 1024

_SMEM = pl.BlockSpec(memory_space=pltpu.SMEM)
_VMEM = pl.BlockSpec(memory_space=pltpu.VMEM)
_ANY = pl.BlockSpec(memory_space=pl.ANY)


def shifted(value, axis, steps):
    count = lax.axis_size(axis)
    leading, last = (max(0, -steps), min(count, count - steps))
    return lax.ppermute(value, axis, [(source, source + steps) for source in range(leading, last)])


def _blk(i):
    return pl.ds(pl.multiple_of(i * BLK, BLK), BLK)


def _chunk(j):
    return pl.ds(pl.multiple_of(j * CH, CH), CH)


def _flag(idx_ref, k):
    return jnp.where(idx_ref[3 * k + 2] > 0, 1.0, 0.0).astype(jnp.float32)


class _WeightChunks:
    def __init__(self, w_hbm, base, w_vmem, sems):
        self.w_hbm, self.base, self.w_vmem, self.sems = w_hbm, base, w_vmem, sems

    def copy(self, j):
        return pltpu.make_async_copy(
            self.w_hbm.at[pl.ds(self.base + j * NSUB, NSUB)],
            self.w_vmem.at[pl.ds(j * NSUB, NSUB)],
            self.sems.at[j],
        )

    def wait_on(self, j):
        self.copy(j).wait()


def _w_copies(w_hbm, base, w_vmem, sems):
    chunks = _WeightChunks(w_hbm, base, w_vmem, sems)
    started = []
    for j in range(w_vmem.shape[0] // NSUB):
        copy = chunks.copy(j)
        copy.start()
        started.append(copy)
    return (chunks, started)


def _slot_chunks(idx_ref, base, copies, product, update):
    def chunk(j, carry):
        copies[0].wait_on(j)

        @pl.when(idx_ref[3 * (base + j * NSUB) + 2] > 0)
        def _():
            for g in range(0, NSUB, GROUP):
                ks = [j * NSUB + g + i for i in range(GROUP)]
                parts = [product(k) for k in ks]
                for k, part in zip(ks, parts):
                    update(k, part)

        return carry

    lax.fori_loop(0, len(copies[1]), chunk, 0)


def _pick_input(at, src_ref, local_hbm, h_ref, sem):
    @pl.when(at[1] > 0)
    def _():
        pltpu.make_async_copy(local_hbm.at[at[0]], h_ref, sem).start()

    @pl.when(at[1] <= 0)
    def _():
        pltpu.make_async_copy(src_ref, h_ref, sem).start()

    pltpu.make_async_copy(src_ref, h_ref, sem).wait()


def _fwd_kernel(base, layer, at_ref, idx_ref, h_in, w_hbm, sh_in, sy_in, *rest):
    if layer == 0:
        local_hbm, hout_ref, sh_ref, sy_ref, w_vmem, y_vmem, sems, io_sems, h_ref = rest
    else:
        hout_ref, sh_ref, sy_ref, w_vmem, y_vmem, sems, io_sems = rest
        h_ref = h_in
    del sh_in, sy_in
    width = h_ref.shape[1]
    at = at_ref[0]
    copies = _w_copies(w_hbm, base, w_vmem, sems)
    if layer == 0:
        _pick_input((at, at_ref[1]), h_in, local_hbm, h_ref, io_sems.at[2])
    save_h = pltpu.make_async_copy(h_ref, sh_ref.at[layer, at], io_sems.at[0])
    save_h.start()
    y_vmem[...] = jnp.zeros_like(y_vmem)

    def product(k):
        r = idx_ref[3 * (base + k)]
        return jnp.dot(h_ref[:, _blk(r)], w_vmem[k], preferred_element_type=jnp.float32)

    def update(k, p):
        c = idx_ref[3 * (base + k) + 1]
        y_vmem[:, _blk(c)] += p * _flag(idx_ref, base + k)

    _slot_chunks(idx_ref, base, copies, product, update)
    save_y = pltpu.make_async_copy(y_vmem, sy_ref.at[layer, at], io_sems.at[1])
    save_y.start()

    def epi(j, carry):
        y = y_vmem[:, _chunk(j)]
        h = h_ref[:, _chunk(j)].astype(jnp.float32)
        hout_ref[:, _chunk(j)] = (h + y / (1.0 + jnp.exp(-y))).astype(hout_ref.dtype)
        return carry

    lax.fori_loop(0, width // CH, epi, 0)
    save_h.wait()
    save_y.wait()


def layer_forward(h, weights, layer, block_index, at, stash_h, stash_y, local=None, use_local=None):
    rows, width = h.shape
    extra_in, extra_args, extra_scratch = [], [], []
    if layer == 0:
        extra_in, extra_args = [_ANY], [local]
        extra_scratch = [pltpu.VMEM((rows, width), h.dtype)]
        at = jnp.stack([at, use_local.astype(jnp.int32)])
    return pl.pallas_call(
        functools.partial(_fwd_kernel, layer * KMAX, layer),
        out_shape=(
            jax.ShapeDtypeStruct((rows, width), jnp.bfloat16),
            jax.ShapeDtypeStruct(stash_h.shape, stash_h.dtype),
            jax.ShapeDtypeStruct(stash_y.shape, stash_y.dtype),
        ),
        in_specs=[_SMEM, _SMEM, _VMEM, _ANY, _ANY, _ANY] + extra_in,
        out_specs=(_VMEM, _ANY, _ANY),
        scratch_shapes=[
            pltpu.VMEM((KMAX, BLK, BLK), weights.dtype),
            pltpu.VMEM((rows, width), jnp.float32),
            pltpu.SemaphoreType.DMA((KMAX // NSUB,)),
            pltpu.SemaphoreType.DMA((3,)),
        ]
        + extra_scratch,
        input_output_aliases={4: 1, 5: 2},
        compiler_params=pltpu.CompilerParams(vmem_limit_bytes=VMEM_LIMIT),
    )(at.reshape(-1), block_index.reshape(-1), h, weights, stash_h, stash_y, *extra_args)


def _bwd_kernel(base, layer, entry, at_ref, idx_ref, g_in, sy_hbm, w_hbm, ss_in, *rest):
    if entry:
        local_hbm, gout_ref, ss_ref, y_vmem, s_vmem, sp_ref, w_vmem, sems, io_sems, g_ref = rest
    else:
        gout_ref, ss_ref, y_vmem, s_vmem, sp_ref, w_vmem, sems, io_sems = rest
        g_ref = g_in
    del ss_in
    width = g_ref.shape[1]
    at = at_ref[0]
    if entry:
        _pick_input((at, at_ref[1]), g_in, local_hbm, g_ref, io_sems.at[2])
    load_y = pltpu.make_async_copy(sy_hbm.at[layer, at], y_vmem, io_sems.at[0])
    load_y.start()
    copies = _w_copies(w_hbm, base, w_vmem, sems)
    load_y.wait()

    def pre(j, carry):
        y = y_vmem[:, _chunk(j)]
        sig = 1.0 / (1.0 + jnp.exp(-y))
        g = g_ref[:, _chunk(j)].astype(jnp.float32)
        s_vmem[:, _chunk(j)] = (g * sig * (1.0 + y * (1.0 - sig))).astype(s_vmem.dtype)
        sp_ref[:, _chunk(j)] = jnp.zeros((g_ref.shape[0], CH), jnp.float32)
        return carry

    lax.fori_loop(0, width // CH, pre, 0)
    save_s = pltpu.make_async_copy(s_vmem, ss_ref.at[layer, at], io_sems.at[1])
    save_s.start()

    def product(k):
        c = idx_ref[3 * (base + k) + 1]
        return lax.dot_general(
            s_vmem[:, _blk(c)],
            w_vmem[k],
            (((1,), (1,)), ((), ())),
            preferred_element_type=jnp.float32,
        )

    def update(k, back):
        r = idx_ref[3 * (base + k)]
        sp_ref[:, _blk(r)] += back * _flag(idx_ref, base + k)

    _slot_chunks(idx_ref, base, copies, product, update)

    def epi(j, carry):
        g = g_ref[:, _chunk(j)].astype(jnp.float32)
        gout_ref[:, _chunk(j)] = (g + sp_ref[:, _chunk(j)]).astype(gout_ref.dtype)
        return carry

    lax.fori_loop(0, width // CH, epi, 0)
    save_s.wait()


def layer_backward(g, stash_y, weights, layer, block_index, at, stash_s, local=None, use_local=None):
    rows, width = g.shape
    entry = local is not None
    extra_in, extra_args, extra_scratch = [], [], []
    if entry:
        extra_in, extra_args = [_ANY], [local]
        extra_scratch = [pltpu.VMEM((rows, width), g.dtype)]
        at = jnp.stack([at, use_local.astype(jnp.int32)])
    return pl.pallas_call(
        functools.partial(_bwd_kernel, layer * KMAX, layer, entry),
        out_shape=(
            jax.ShapeDtypeStruct((rows, width), jnp.bfloat16),
            jax.ShapeDtypeStruct(stash_s.shape, stash_s.dtype),
        ),
        in_specs=[_SMEM, _SMEM, _VMEM, _ANY, _ANY, _ANY] + extra_in,
        out_specs=(_VMEM, _ANY),
        scratch_shapes=[
            pltpu.VMEM((rows, width), jnp.float32),
            pltpu.VMEM((rows, width), jnp.bfloat16),
            pltpu.VMEM((rows, width), jnp.float32),
            pltpu.VMEM((KMAX, BLK, BLK), weights.dtype),
            pltpu.SemaphoreType.DMA((KMAX // NSUB,)),
            pltpu.SemaphoreType.DMA((3,)),
        ]
        + extra_scratch,
        input_output_aliases={5: 1},
        compiler_params=pltpu.CompilerParams(vmem_limit_bytes=VMEM_LIMIT),
    )(at.reshape(-1), block_index.reshape(-1), g, stash_y, weights, stash_s, *extra_args)


def _dw_kernel(mbs, idx_ref, h_ref, s_ref, dw_ref):
    rows = h_ref.shape[1] * h_ref.shape[2]
    for j in range(dw_ref.shape[0] // NSUB):
        layer = j * NSUB // KMAX

        @pl.when(idx_ref[3 * j * NSUB + 2] > 0)
        def _():
            for k in range(j * NSUB, (j + 1) * NSUB):
                r = idx_ref[3 * k]
                c = idx_ref[3 * k + 1]
                hb = h_ref[layer, :, :, _blk(r)]
                sb = s_ref[layer, :, :, _blk(c)]
                dw_ref[k] = lax.dot_general(
                    hb.reshape(rows, BLK),
                    sb.reshape(rows, BLK),
                    (((0,), (0,)), ((), ())),
                    preferred_element_type=jnp.float32,
                ) * _flag(idx_ref, k)

        @pl.when(idx_ref[3 * j * NSUB + 2] <= 0)
        def _():
            dw_ref[pl.ds(j * NSUB, NSUB)] = jnp.zeros((NSUB, BLK, BLK), jnp.float32)


def segment_dw(stash_h, stash_s, block_index, mbs):
    return pl.pallas_call(
        functools.partial(_dw_kernel, mbs),
        out_shape=jax.ShapeDtypeStruct((block_index.shape[0], BLK, BLK), jnp.float32),
        in_specs=[_SMEM, _VMEM, _VMEM],
        out_specs=_VMEM,
        compiler_params=pltpu.CompilerParams(vmem_limit_bytes=VMEM_LIMIT),
    )(block_index.reshape(-1), stash_h, stash_s)


def _dw_half_kernel(sel_ref, idx_ref, h_ref, s_ref, out_ref):
    b0 = sel_ref[0]
    rows = h_ref.shape[1] * h_ref.shape[2]
    per = out_ref.shape[1]
    for q in range(out_ref.shape[0]):
        layer = (2 * q * per) // KMAX
        spot = q + b0 * ((q % 2) * 2 + q // 2 - q)
        for j in range(per // NSUB):
            first = 2 * q * per + b0 * per + j * NSUB

            @pl.when(idx_ref[3 * first + 2] > 0)
            def _():
                for i in range(NSUB):
                    k = first + i
                    r = idx_ref[3 * k]
                    c = idx_ref[3 * k + 1]
                    hb = h_ref[layer, :, :, _blk(r)].reshape(rows, BLK)
                    sb = s_ref[layer, :, :, _blk(c)].reshape(rows, BLK)
                    part = lax.dot_general(
                        hb, sb, (((0,), (0,)), ((), ())), preferred_element_type=jnp.float32
                    )
                    out_ref[spot, j * NSUB + i] = (part * _flag(idx_ref, k)).astype(out_ref.dtype)

            @pl.when(idx_ref[3 * first + 2] <= 0)
            def _():
                out_ref[spot, pl.ds(j * NSUB, NSUB)] = jnp.zeros((NSUB, BLK, BLK), out_ref.dtype)


def dw_half(stash_h, stash_s, block_index, b0, dtype):
    per = block_index.shape[0] // 8
    return pl.pallas_call(
        _dw_half_kernel,
        out_shape=jax.ShapeDtypeStruct((4, per, BLK, BLK), dtype),
        in_specs=[_SMEM, _SMEM, _VMEM, _VMEM],
        out_specs=_VMEM,
        compiler_params=pltpu.CompilerParams(vmem_limit_bytes=VMEM_LIMIT),
    )(b0.reshape(1).astype(jnp.int32), block_index.reshape(-1), stash_h, stash_s)


def _exchange(send, pairs):
    return lax.ppermute(send.astype(jnp.bfloat16), "dp", pairs).astype(jnp.float32)


def weight_grads(stash_h, stash_s, block_index, mbs):
    n = lax.axis_size("dp")
    if n != 8:
        acc = segment_dw(stash_h, stash_s, block_index, mbs)
        return lax.psum_scatter(
            acc.astype(jnp.bfloat16), "dp", scatter_dimension=0, tiled=True
        ).astype(jnp.float32)
    d = lax.axis_index("dp")
    d0, d1, d2 = d % 2, (d // 2) % 2, d // 4
    pick = lambda a, i, axis: lax.dynamic_index_in_dim(a, i, axis, keepdims=False)
    send = dw_half(stash_h, stash_s, block_index, 1 - d0, jnp.bfloat16)
    got = lax.ppermute(send, "dp", [(i, i ^ 1) for i in range(8)])
    keep = dw_half(stash_h, stash_s, block_index, d0, jnp.float32)
    keep = keep.reshape((2, 2) + keep.shape[1:])
    got = got.reshape(keep.shape)
    core0 = d0 == 0
    flip = jnp.where(core0, d1, d2)
    rem = jnp.where(core0, d2, d1)

    def summed(a, b, i):
        return pick(a, i, 1) + pick(b, i, 1).astype(jnp.float32)

    got2 = _exchange(summed(keep, got, 1 - flip), [(i, i ^ (2 if i % 2 == 0 else 4)) for i in range(8)])

    def part(i):
        return pick(pick(keep, flip, 1), i, 0) + pick(pick(got, flip, 1), i, 0).astype(jnp.float32) + pick(got2, i, 0)

    got3 = _exchange(part(1 - rem), [(i, i ^ (4 if i % 2 == 0 else 2)) for i in range(8)])
    return part(rem) + got3


def _allocate_kernel(*refs):
    del refs


def allocate(specs):
    return pl.pallas_call(
        _allocate_kernel,
        out_shape=tuple(jax.ShapeDtypeStruct(shape, dtype) for shape, dtype in specs),
        out_specs=tuple(_ANY for _ in specs),
    )()


def on_device(x_in, cotangent, weights, block_index):
    segments = lax.axis_size("segment")
    me_segment = lax.axis_index("segment")
    mbs, rows_dev, width = x_in.shape
    mbs, rows_dev = mbs * SPLIT, rows_dev // SPLIT
    x_in = x_in.reshape(mbs, rows_dev, width)
    cotangent = cotangent.reshape(mbs, rows_dev, width)
    idx = block_index.reshape(LSLOT, KMAX, 3)

    def tick_body(tick, carry):
        recv_f, recv_b, saved_h, saved_y, saved_s = carry
        micro_f = tick - me_segment
        live_f = (micro_f >= 0) & (micro_f < mbs)
        at_f = jnp.clip(micro_f, 0, mbs - 1)
        def run_f(operands):
            h, sh, sy = operands
            for layer in range(LSLOT):
                local = (x_in, me_segment == 0) if layer == 0 else (None, None)
                h, sh, sy = layer_forward(h, weights, layer, block_index, at_f, sh, sy, *local)
            return (h, sh, sy)

        h_out, saved_h, saved_y = lax.cond(live_f, run_f, lambda ops: ops, (recv_f, saved_h, saved_y))
        send_f = shifted(h_out, "segment", 1)

        micro_b = tick - (2 * segments - 2 - me_segment)
        live_b = (micro_b >= 0) & (micro_b < mbs)
        at_b = jnp.clip(micro_b, 0, mbs - 1)
        stash_y_now = saved_y

        def run_b(operands):
            grad, ss = operands
            for layer in reversed(range(LSLOT)):
                local = (cotangent, me_segment == segments - 1) if layer == LSLOT - 1 else (None, None)
                grad, ss = layer_backward(grad, stash_y_now, weights, layer, block_index, at_b, ss, *local)
            return (grad, ss)

        grad_out, saved_s = lax.cond(live_b, run_b, lambda ops: ops, (recv_b, saved_s))
        send_b = shifted(grad_out, "segment", -1)
        return (send_f, send_b, saved_h, saved_y, saved_s)

    stash_shape = (LSLOT, mbs, rows_dev, width)
    stash_h, stash_y, stash_s = allocate(
        [(stash_shape, jnp.bfloat16), (stash_shape, jnp.float32), (stash_shape, jnp.bfloat16)]
    )
    blank = jnp.zeros((rows_dev, width), jnp.bfloat16)
    ticks = mbs + 2 * segments - 2
    carry = (blank, blank, stash_h, stash_y, stash_s)
    for tick in range(ticks):
        carry = tick_body(tick, carry)
    unused_f, unused_b, stash_h, stash_y, stash_s = carry
    return weight_grads(stash_h, stash_s, block_index, mbs)


def solution(mesh):
    return jax.shard_map(
        on_device,
        mesh=mesh,
        in_specs=(
            P(None, "dp", None),
            P(None, "dp", None),
            P("segment", None, None),
            P("segment", None),
        ),
        out_specs=P(("segment", "dp"), None, None),
        check_vma=False,
    )
```

```python
import functools

import jax
import jax.numpy as jnp
from jax import lax
from jax.experimental import pallas as pl
from jax.experimental.pallas import tpu as pltpu
from jax.sharding import PartitionSpec as P

BLK = 128
LSLOT = 2
KMAX = 128
CH = 512
NSUB = 16
SPLIT = 2
GROUP = 16
VMEM_LIMIT = 60 * 1024 * 1024

_SMEM = pl.BlockSpec(memory_space=pltpu.SMEM)
_VMEM = pl.BlockSpec(memory_space=pltpu.VMEM)
_ANY = pl.BlockSpec(memory_space=pl.ANY)


def shifted(value, axis, steps):
    count = lax.axis_size(axis)
    leading, last = (max(0, -steps), min(count, count - steps))
    return lax.ppermute(value, axis, [(source, source + steps) for source in range(leading, last)])


def _blk(i):
    return pl.ds(pl.multiple_of(i * BLK, BLK), BLK)


def _chunk(j):
    return pl.ds(pl.multiple_of(j * CH, CH), CH)


def _flag(idx_ref, k):
    return jnp.where(idx_ref[3 * k + 2] > 0, 1.0, 0.0).astype(jnp.float32)


class _WeightChunks:
    def __init__(self, w_hbm, base, w_vmem, sems):
        self.w_hbm, self.base, self.w_vmem, self.sems = w_hbm, base, w_vmem, sems

    def copy(self, j):
        return pltpu.make_async_copy(
            self.w_hbm.at[pl.ds(self.base + j * NSUB, NSUB)],
            self.w_vmem.at[pl.ds(j * NSUB, NSUB)],
            self.sems.at[j],
        )

    def wait_on(self, j):
        self.copy(j).wait()


def _w_copies(w_hbm, base, w_vmem, sems):
    chunks = _WeightChunks(w_hbm, base, w_vmem, sems)
    started = []
    for j in range(w_vmem.shape[0] // NSUB):
        copy = chunks.copy(j)
        copy.start()
        started.append(copy)
    return (chunks, started)


def _slot_chunks(idx_ref, base, copies, product, update):
    def chunk(j, carry):
        copies[0].wait_on(j)

        @pl.when(idx_ref[3 * (base + j * NSUB) + 2] > 0)
        def _():
            for g in range(0, NSUB, GROUP):
                ks = [j * NSUB + g + i for i in range(GROUP)]
                parts = [product(k) for k in ks]
                for k, part in zip(ks, parts):
                    update(k, part)

        return carry

    lax.fori_loop(0, len(copies[1]), chunk, 0)


def _pick_input(at, src_ref, local_hbm, h_ref, sem):
    @pl.when(at[1] > 0)
    def _():
        pltpu.make_async_copy(local_hbm.at[at[0]], h_ref, sem).start()

    @pl.when(at[1] <= 0)
    def _():
        pltpu.make_async_copy(src_ref, h_ref, sem).start()

    pltpu.make_async_copy(src_ref, h_ref, sem).wait()


def _fwd_kernel(base, layer, at_ref, idx_ref, h_in, w_hbm, sh_in, sy_in, *rest):
    if layer == 0:
        local_hbm, hout_ref, sh_ref, sy_ref, w_vmem, y_vmem, sems, io_sems, h_ref = rest
    else:
        hout_ref, sh_ref, sy_ref, w_vmem, y_vmem, sems, io_sems = rest
        h_ref = h_in
    del sh_in, sy_in
    width = h_ref.shape[1]
    at = at_ref[0]
    copies = _w_copies(w_hbm, base, w_vmem, sems)
    if layer == 0:
        _pick_input((at, at_ref[1]), h_in, local_hbm, h_ref, io_sems.at[2])
    save_h = pltpu.make_async_copy(h_ref, sh_ref.at[layer, at], io_sems.at[0])
    save_h.start()
    y_vmem[...] = jnp.zeros_like(y_vmem)

    def product(k):
        r = idx_ref[3 * (base + k)]
        return jnp.dot(h_ref[:, _blk(r)], w_vmem[k], preferred_element_type=jnp.float32)

    def update(k, p):
        c = idx_ref[3 * (base + k) + 1]
        y_vmem[:, _blk(c)] += p * _flag(idx_ref, base + k)

    _slot_chunks(idx_ref, base, copies, product, update)
    save_y = pltpu.make_async_copy(y_vmem, sy_ref.at[layer, at], io_sems.at[1])
    save_y.start()

    def epi(j, carry):
        y = y_vmem[:, _chunk(j)]
        h = h_ref[:, _chunk(j)].astype(jnp.float32)
        hout_ref[:, _chunk(j)] = (h + y / (1.0 + jnp.exp(-y))).astype(hout_ref.dtype)
        return carry

    lax.fori_loop(0, width // CH, epi, 0)
    save_h.wait()
    save_y.wait()


def layer_forward(h, weights, layer, block_index, at, stash_h, stash_y, local=None, use_local=None):
    rows, width = h.shape
    extra_in, extra_args, extra_scratch = [], [], []
    if layer == 0:
        extra_in, extra_args = [_ANY], [local]
        extra_scratch = [pltpu.VMEM((rows, width), h.dtype)]
        at = jnp.stack([at, use_local.astype(jnp.int32)])
    return pl.pallas_call(
        functools.partial(_fwd_kernel, layer * KMAX, layer),
        out_shape=(
            jax.ShapeDtypeStruct((rows, width), jnp.bfloat16),
            jax.ShapeDtypeStruct(stash_h.shape, stash_h.dtype),
            jax.ShapeDtypeStruct(stash_y.shape, stash_y.dtype),
        ),
        in_specs=[_SMEM, _SMEM, _VMEM, _ANY, _ANY, _ANY] + extra_in,
        out_specs=(_VMEM, _ANY, _ANY),
        scratch_shapes=[
            pltpu.VMEM((KMAX, BLK, BLK), weights.dtype),
            pltpu.VMEM((rows, width), jnp.float32),
            pltpu.SemaphoreType.DMA((KMAX // NSUB,)),
            pltpu.SemaphoreType.DMA((3,)),
        ]
        + extra_scratch,
        input_output_aliases={4: 1, 5: 2},
        compiler_params=pltpu.CompilerParams(vmem_limit_bytes=VMEM_LIMIT),
    )(at.reshape(-1), block_index.reshape(-1), h, weights, stash_h, stash_y, *extra_args)


def _bwd_kernel(base, layer, entry, at_ref, idx_ref, g_in, sy_hbm, w_hbm, ss_in, *rest):
    if entry:
        local_hbm, gout_ref, ss_ref, y_vmem, s_vmem, sp_ref, w_vmem, sems, io_sems, g_ref = rest
    else:
        gout_ref, ss_ref, y_vmem, s_vmem, sp_ref, w_vmem, sems, io_sems = rest
        g_ref = g_in
    del ss_in
    width = g_ref.shape[1]
    at = at_ref[0]
    if entry:
        _pick_input((at, at_ref[1]), g_in, local_hbm, g_ref, io_sems.at[2])
    load_y = pltpu.make_async_copy(sy_hbm.at[layer, at], y_vmem, io_sems.at[0])
    load_y.start()
    copies = _w_copies(w_hbm, base, w_vmem, sems)
    load_y.wait()

    def pre(j, carry):
        y = y_vmem[:, _chunk(j)]
        sig = 1.0 / (1.0 + jnp.exp(-y))
        g = g_ref[:, _chunk(j)].astype(jnp.float32)
        s_vmem[:, _chunk(j)] = (g * sig * (1.0 + y * (1.0 - sig))).astype(s_vmem.dtype)
        sp_ref[:, _chunk(j)] = jnp.zeros((g_ref.shape[0], CH), jnp.float32)
        return carry

    lax.fori_loop(0, width // CH, pre, 0)
    save_s = pltpu.make_async_copy(s_vmem, ss_ref.at[layer, at], io_sems.at[1])
    save_s.start()

    def product(k):
        c = idx_ref[3 * (base + k) + 1]
        return lax.dot_general(
            s_vmem[:, _blk(c)],
            w_vmem[k],
            (((1,), (1,)), ((), ())),
            preferred_element_type=jnp.float32,
        )

    def update(k, back):
        r = idx_ref[3 * (base + k)]
        sp_ref[:, _blk(r)] += back * _flag(idx_ref, base + k)

    _slot_chunks(idx_ref, base, copies, product, update)

    def epi(j, carry):
        g = g_ref[:, _chunk(j)].astype(jnp.float32)
        gout_ref[:, _chunk(j)] = (g + sp_ref[:, _chunk(j)]).astype(gout_ref.dtype)
        return carry

    lax.fori_loop(0, width // CH, epi, 0)
    save_s.wait()


def layer_backward(g, stash_y, weights, layer, block_index, at, stash_s, local=None, use_local=None):
    rows, width = g.shape
    entry = local is not None
    extra_in, extra_args, extra_scratch = [], [], []
    if entry:
        extra_in, extra_args = [_ANY], [local]
        extra_scratch = [pltpu.VMEM((rows, width), g.dtype)]
        at = jnp.stack([at, use_local.astype(jnp.int32)])
    return pl.pallas_call(
        functools.partial(_bwd_kernel, layer * KMAX, layer, entry),
        out_shape=(
            jax.ShapeDtypeStruct((rows, width), jnp.bfloat16),
            jax.ShapeDtypeStruct(stash_s.shape, stash_s.dtype),
        ),
        in_specs=[_SMEM, _SMEM, _VMEM, _ANY, _ANY, _ANY] + extra_in,
        out_specs=(_VMEM, _ANY),
        scratch_shapes=[
            pltpu.VMEM((rows, width), jnp.float32),
            pltpu.VMEM((rows, width), jnp.bfloat16),
            pltpu.VMEM((rows, width), jnp.float32),
            pltpu.VMEM((KMAX, BLK, BLK), weights.dtype),
            pltpu.SemaphoreType.DMA((KMAX // NSUB,)),
            pltpu.SemaphoreType.DMA((3,)),
        ]
        + extra_scratch,
        input_output_aliases={5: 1},
        compiler_params=pltpu.CompilerParams(vmem_limit_bytes=VMEM_LIMIT),
    )(at.reshape(-1), block_index.reshape(-1), g, stash_y, weights, stash_s, *extra_args)


def _dw_kernel(mbs, idx_ref, h_ref, s_ref, dw_ref):
    rows = h_ref.shape[1] * h_ref.shape[2]
    for j in range(dw_ref.shape[0] // NSUB):
        layer = j * NSUB // KMAX

        @pl.when(idx_ref[3 * j * NSUB + 2] > 0)
        def _():
            for k in range(j * NSUB, (j + 1) * NSUB):
                r = idx_ref[3 * k]
                c = idx_ref[3 * k + 1]
                hb = h_ref[layer, :, :, _blk(r)]
                sb = s_ref[layer, :, :, _blk(c)]
                dw_ref[k] = lax.dot_general(
                    hb.reshape(rows, BLK),
                    sb.reshape(rows, BLK),
                    (((0,), (0,)), ((), ())),
                    preferred_element_type=jnp.float32,
                ) * _flag(idx_ref, k)

        @pl.when(idx_ref[3 * j * NSUB + 2] <= 0)
        def _():
            dw_ref[pl.ds(j * NSUB, NSUB)] = jnp.zeros((NSUB, BLK, BLK), jnp.float32)


def segment_dw(stash_h, stash_s, block_index, mbs):
    return pl.pallas_call(
        functools.partial(_dw_kernel, mbs),
        out_shape=jax.ShapeDtypeStruct((block_index.shape[0], BLK, BLK), jnp.float32),
        in_specs=[_SMEM, _VMEM, _VMEM],
        out_specs=_VMEM,
        compiler_params=pltpu.CompilerParams(vmem_limit_bytes=VMEM_LIMIT),
    )(block_index.reshape(-1), stash_h, stash_s)


def _dw_half_kernel(sel_ref, idx_ref, h_ref, s_ref, out_ref):
    b0 = sel_ref[0]
    rows = h_ref.shape[1] * h_ref.shape[2]
    per = out_ref.shape[1]
    for q in range(out_ref.shape[0]):
        layer = (2 * q * per) // KMAX
        spot = q + b0 * ((q % 2) * 2 + q // 2 - q)
        for j in range(per // NSUB):
            first = 2 * q * per + b0 * per + j * NSUB

            @pl.when(idx_ref[3 * first + 2] > 0)
            def _():
                for i in range(NSUB):
                    k = first + i
                    r = idx_ref[3 * k]
                    c = idx_ref[3 * k + 1]
                    hb = h_ref[layer, :, :, _blk(r)].reshape(rows, BLK)
                    sb = s_ref[layer, :, :, _blk(c)].reshape(rows, BLK)
                    part = lax.dot_general(
                        hb, sb, (((0,), (0,)), ((), ())), preferred_element_type=jnp.float32
                    )
                    out_ref[spot, j * NSUB + i] = (part * _flag(idx_ref, k)).astype(out_ref.dtype)

            @pl.when(idx_ref[3 * first + 2] <= 0)
            def _():
                out_ref[spot, pl.ds(j * NSUB, NSUB)] = jnp.zeros((NSUB, BLK, BLK), out_ref.dtype)


def dw_half(stash_h, stash_s, block_index, b0, dtype):
    per = block_index.shape[0] // 8
    return pl.pallas_call(
        _dw_half_kernel,
        out_shape=jax.ShapeDtypeStruct((4, per, BLK, BLK), dtype),
        in_specs=[_SMEM, _SMEM, _VMEM, _VMEM],
        out_specs=_VMEM,
        compiler_params=pltpu.CompilerParams(vmem_limit_bytes=VMEM_LIMIT),
    )(b0.reshape(1).astype(jnp.int32), block_index.reshape(-1), stash_h, stash_s)


def _exchange(send, pairs):
    return lax.ppermute(send.astype(jnp.bfloat16), "dp", pairs).astype(jnp.float32)


def weight_grads(stash_h, stash_s, block_index, mbs):
    n = lax.axis_size("dp")
    if n != 8:
        acc = segment_dw(stash_h, stash_s, block_index, mbs)
        return lax.psum_scatter(
            acc.astype(jnp.bfloat16), "dp", scatter_dimension=0, tiled=True
        ).astype(jnp.float32)
    d = lax.axis_index("dp")
    d0, d1, d2 = d % 2, (d // 2) % 2, d // 4
    pick = lambda a, i, axis: lax.dynamic_index_in_dim(a, i, axis, keepdims=False)
    send = dw_half(stash_h, stash_s, block_index, 1 - d0, jnp.bfloat16)
    got = lax.ppermute(send, "dp", [(i, i ^ 1) for i in range(8)])
    keep = dw_half(stash_h, stash_s, block_index, d0, jnp.float32)
    keep = keep.reshape((2, 2) + keep.shape[1:])
    got = got.reshape(keep.shape)
    core0 = d0 == 0
    flip = jnp.where(core0, d1, d2)
    rem = jnp.where(core0, d2, d1)

    def summed(a, b, i):
        return pick(a, i, 1) + pick(b, i, 1).astype(jnp.float32)

    got2 = _exchange(summed(keep, got, 1 - flip), [(i, i ^ (2 if i % 2 == 0 else 4)) for i in range(8)])

    def part(i):
        return pick(pick(keep, flip, 1), i, 0) + pick(pick(got, flip, 1), i, 0).astype(jnp.float32) + pick(got2, i, 0)

    got3 = _exchange(part(1 - rem), [(i, i ^ (4 if i % 2 == 0 else 2)) for i in range(8)])
    return part(rem) + got3


def _allocate_kernel(*refs):
    del refs


def allocate(specs):
    return pl.pallas_call(
        _allocate_kernel,
        out_shape=tuple(jax.ShapeDtypeStruct(shape, dtype) for shape, dtype in specs),
        out_specs=tuple(_ANY for _ in specs),
    )()


def on_device(x_in, cotangent, weights, block_index):
    segments = lax.axis_size("segment")
    me_segment = lax.axis_index("segment")
    mbs, rows_dev, width = x_in.shape
    mbs, rows_dev = mbs * SPLIT, rows_dev // SPLIT
    x_in = x_in.reshape(mbs, rows_dev, width)
    cotangent = cotangent.reshape(mbs, rows_dev, width)
    idx = block_index.reshape(LSLOT, KMAX, 3)

    def tick_body(tick, carry):
        recv_f, recv_b, saved_h, saved_y, saved_s = carry
        micro_f = tick - me_segment
        live_f = (micro_f >= 0) & (micro_f < mbs)
        at_f = jnp.clip(micro_f, 0, mbs - 1)
        def run_f(operands):
            h, sh, sy = operands
            for layer in range(LSLOT):
                local = (x_in, me_segment == 0) if layer == 0 else (None, None)
                h, sh, sy = layer_forward(h, weights, layer, block_index, at_f, sh, sy, *local)
            return (h, sh, sy)

        h_out, saved_h, saved_y = lax.cond(live_f, run_f, lambda ops: ops, (recv_f, saved_h, saved_y))
        send_f = shifted(h_out, "segment", 1)

        micro_b = tick - (2 * segments - 2 - me_segment)
        live_b = (micro_b >= 0) & (micro_b < mbs)
        at_b = jnp.clip(micro_b, 0, mbs - 1)
        stash_y_now = saved_y

        def run_b(operands):
            grad, ss = operands
            for layer in reversed(range(LSLOT)):
                local = (cotangent, me_segment == segments - 1) if layer == LSLOT - 1 else (None, None)
                grad, ss = layer_backward(grad, stash_y_now, weights, layer, block_index, at_b, ss, *local)
            return (grad, ss)

        grad_out, saved_s = lax.cond(live_b, run_b, lambda ops: ops, (recv_b, saved_s))
        send_b = shifted(grad_out, "segment", -1)
        return (send_f, send_b, saved_h, saved_y, saved_s)

    stash_shape = (LSLOT, mbs, rows_dev, width)
    stash_h, stash_y, stash_s = allocate(
        [(stash_shape, jnp.bfloat16), (stash_shape, jnp.float32), (stash_shape, jnp.bfloat16)]
    )
    blank = jnp.zeros((rows_dev, width), jnp.bfloat16)
    ticks = mbs + 2 * segments - 2
    carry = (blank, blank, stash_h, stash_y, stash_s)
    for tick in range(ticks):
        carry = tick_body(tick, carry)
    unused_f, unused_b, stash_h, stash_y, stash_s = carry
    return weight_grads(stash_h, stash_s, block_index, mbs)


def solution(mesh):
    return jax.shard_map(
        on_device,
        mesh=mesh,
        in_specs=(
            P(None, "dp", None),
            P(None, "dp", None),
            P("segment", None, None),
            P("segment", None),
        ),
        out_specs=P(("segment", "dp"), None, None),
        check_vma=False,
    )
```

```python
import functools

import jax
import jax.numpy as jnp
from jax import lax
from jax.experimental import pallas as pl
from jax.experimental.pallas import tpu as pltpu
from jax.sharding import PartitionSpec as P

BLK = 128
LSLOT = 2
KMAX = 128
CH = 512
NSUB = 32
SPLIT = 2
GROUP = 16
VMEM_LIMIT = 60 * 1024 * 1024

_SMEM = pl.BlockSpec(memory_space=pltpu.SMEM)
_VMEM = pl.BlockSpec(memory_space=pltpu.VMEM)
_ANY = pl.BlockSpec(memory_space=pl.ANY)


def shifted(value, axis, steps):
    count = lax.axis_size(axis)
    leading, last = (max(0, -steps), min(count, count - steps))
    return lax.ppermute(value, axis, [(source, source + steps) for source in range(leading, last)])


def _blk(i):
    return pl.ds(pl.multiple_of(i * BLK, BLK), BLK)


def _chunk(j):
    return pl.ds(pl.multiple_of(j * CH, CH), CH)


def _flag(idx_ref, k):
    return jnp.where(idx_ref[3 * k + 2] > 0, 1.0, 0.0).astype(jnp.float32)


class _WeightChunks:
    def __init__(self, w_hbm, base, w_vmem, sems):
        self.w_hbm, self.base, self.w_vmem, self.sems = w_hbm, base, w_vmem, sems

    def copy(self, j):
        return pltpu.make_async_copy(
            self.w_hbm.at[pl.ds(self.base + j * NSUB, NSUB)],
            self.w_vmem.at[pl.ds(j * NSUB, NSUB)],
            self.sems.at[j],
        )

    def wait_on(self, j):
        self.copy(j).wait()


def _w_copies(w_hbm, base, w_vmem, sems):
    chunks = _WeightChunks(w_hbm, base, w_vmem, sems)
    started = []
    for j in range(w_vmem.shape[0] // NSUB):
        copy = chunks.copy(j)
        copy.start()
        started.append(copy)
    return (chunks, started)


def _slot_chunks(idx_ref, base, copies, product, update):
    def chunk(j, carry):
        copies[0].wait_on(j)

        @pl.when(idx_ref[3 * (base + j * NSUB) + 2] > 0)
        def _():
            for g in range(0, NSUB, GROUP):
                ks = [j * NSUB + g + i for i in range(GROUP)]
                parts = [product(k) for k in ks]
                for k, part in zip(ks, parts):
                    update(k, part)

        return carry

    lax.fori_loop(0, len(copies[1]), chunk, 0)


def _pick_input(at, src_ref, local_hbm, h_ref, sem):
    @pl.when(at[1] > 0)
    def _():
        pltpu.make_async_copy(local_hbm.at[at[0]], h_ref, sem).start()

    @pl.when(at[1] <= 0)
    def _():
        pltpu.make_async_copy(src_ref, h_ref, sem).start()

    pltpu.make_async_copy(src_ref, h_ref, sem).wait()


def _fwd_kernel(base, layer, at_ref, idx_ref, h_in, w_hbm, sh_in, sy_in, *rest):
    if layer == 0:
        local_hbm, hout_ref, sh_ref, sy_ref, w_vmem, y_vmem, sems, io_sems, h_ref = rest
    else:
        hout_ref, sh_ref, sy_ref, w_vmem, y_vmem, sems, io_sems = rest
        h_ref = h_in
    del sh_in, sy_in
    width = h_ref.shape[1]
    at = at_ref[0]
    copies = _w_copies(w_hbm, base, w_vmem, sems)
    if layer == 0:
        _pick_input((at, at_ref[1]), h_in, local_hbm, h_ref, io_sems.at[2])
    save_h = pltpu.make_async_copy(h_ref, sh_ref.at[layer, at], io_sems.at[0])
    save_h.start()
    y_vmem[...] = jnp.zeros_like(y_vmem)

    def product(k):
        r = idx_ref[3 * (base + k)]
        return jnp.dot(h_ref[:, _blk(r)], w_vmem[k], preferred_element_type=jnp.float32)

    def update(k, p):
        c = idx_ref[3 * (base + k) + 1]
        y_vmem[:, _blk(c)] += p * _flag(idx_ref, base + k)

    _slot_chunks(idx_ref, base, copies, product, update)
    save_y = pltpu.make_async_copy(y_vmem, sy_ref.at[layer, at], io_sems.at[1])
    save_y.start()

    def epi(j, carry):
        y = y_vmem[:, _chunk(j)]
        h = h_ref[:, _chunk(j)].astype(jnp.float32)
        hout_ref[:, _chunk(j)] = (h + y / (1.0 + jnp.exp(-y))).astype(hout_ref.dtype)
        return carry

    lax.fori_loop(0, width // CH, epi, 0)
    save_h.wait()
    save_y.wait()


def layer_forward(h, weights, layer, block_index, at, stash_h, stash_y, local=None, use_local=None):
    rows, width = h.shape
    extra_in, extra_args, extra_scratch = [], [], []
    if layer == 0:
        extra_in, extra_args = [_ANY], [local]
        extra_scratch = [pltpu.VMEM((rows, width), h.dtype)]
        at = jnp.stack([at, use_local.astype(jnp.int32)])
    return pl.pallas_call(
        functools.partial(_fwd_kernel, layer * KMAX, layer),
        out_shape=(
            jax.ShapeDtypeStruct((rows, width), jnp.bfloat16),
            jax.ShapeDtypeStruct(stash_h.shape, stash_h.dtype),
            jax.ShapeDtypeStruct(stash_y.shape, stash_y.dtype),
        ),
        in_specs=[_SMEM, _SMEM, _VMEM, _ANY, _ANY, _ANY] + extra_in,
        out_specs=(_VMEM, _ANY, _ANY),
        scratch_shapes=[
            pltpu.VMEM((KMAX, BLK, BLK), weights.dtype),
            pltpu.VMEM((rows, width), jnp.float32),
            pltpu.SemaphoreType.DMA((KMAX // NSUB,)),
            pltpu.SemaphoreType.DMA((3,)),
        ]
        + extra_scratch,
        input_output_aliases={4: 1, 5: 2},
        compiler_params=pltpu.CompilerParams(vmem_limit_bytes=VMEM_LIMIT),
    )(at.reshape(-1), block_index.reshape(-1), h, weights, stash_h, stash_y, *extra_args)


def _bwd_kernel(base, layer, entry, at_ref, idx_ref, g_in, sy_hbm, w_hbm, ss_in, *rest):
    if entry:
        local_hbm, gout_ref, ss_ref, y_vmem, s_vmem, sp_ref, w_vmem, sems, io_sems, g_ref = rest
    else:
        gout_ref, ss_ref, y_vmem, s_vmem, sp_ref, w_vmem, sems, io_sems = rest
        g_ref = g_in
    del ss_in
    width = g_ref.shape[1]
    at = at_ref[0]
    if entry:
        _pick_input((at, at_ref[1]), g_in, local_hbm, g_ref, io_sems.at[2])
    load_y = pltpu.make_async_copy(sy_hbm.at[layer, at], y_vmem, io_sems.at[0])
    load_y.start()
    copies = _w_copies(w_hbm, base, w_vmem, sems)
    load_y.wait()

    def pre(j, carry):
        y = y_vmem[:, _chunk(j)]
        sig = 1.0 / (1.0 + jnp.exp(-y))
        g = g_ref[:, _chunk(j)].astype(jnp.float32)
        s_vmem[:, _chunk(j)] = (g * sig * (1.0 + y * (1.0 - sig))).astype(s_vmem.dtype)
        sp_ref[:, _chunk(j)] = jnp.zeros((g_ref.shape[0], CH), jnp.float32)
        return carry

    lax.fori_loop(0, width // CH, pre, 0)
    save_s = pltpu.make_async_copy(s_vmem, ss_ref.at[layer, at], io_sems.at[1])
    save_s.start()

    def product(k):
        c = idx_ref[3 * (base + k) + 1]
        return lax.dot_general(
            s_vmem[:, _blk(c)],
            w_vmem[k],
            (((1,), (1,)), ((), ())),
            preferred_element_type=jnp.float32,
        )

    def update(k, back):
        r = idx_ref[3 * (base + k)]
        sp_ref[:, _blk(r)] += back * _flag(idx_ref, base + k)

    _slot_chunks(idx_ref, base, copies, product, update)

    def epi(j, carry):
        g = g_ref[:, _chunk(j)].astype(jnp.float32)
        gout_ref[:, _chunk(j)] = (g + sp_ref[:, _chunk(j)]).astype(gout_ref.dtype)
        return carry

    lax.fori_loop(0, width // CH, epi, 0)
    save_s.wait()


def layer_backward(g, stash_y, weights, layer, block_index, at, stash_s, local=None, use_local=None):
    rows, width = g.shape
    entry = local is not None
    extra_in, extra_args, extra_scratch = [], [], []
    if entry:
        extra_in, extra_args = [_ANY], [local]
        extra_scratch = [pltpu.VMEM((rows, width), g.dtype)]
        at = jnp.stack([at, use_local.astype(jnp.int32)])
    return pl.pallas_call(
        functools.partial(_bwd_kernel, layer * KMAX, layer, entry),
        out_shape=(
            jax.ShapeDtypeStruct((rows, width), jnp.bfloat16),
            jax.ShapeDtypeStruct(stash_s.shape, stash_s.dtype),
        ),
        in_specs=[_SMEM, _SMEM, _VMEM, _ANY, _ANY, _ANY] + extra_in,
        out_specs=(_VMEM, _ANY),
        scratch_shapes=[
            pltpu.VMEM((rows, width), jnp.float32),
            pltpu.VMEM((rows, width), jnp.bfloat16),
            pltpu.VMEM((rows, width), jnp.float32),
            pltpu.VMEM((KMAX, BLK, BLK), weights.dtype),
            pltpu.SemaphoreType.DMA((KMAX // NSUB,)),
            pltpu.SemaphoreType.DMA((3,)),
        ]
        + extra_scratch,
        input_output_aliases={5: 1},
        compiler_params=pltpu.CompilerParams(vmem_limit_bytes=VMEM_LIMIT),
    )(at.reshape(-1), block_index.reshape(-1), g, stash_y, weights, stash_s, *extra_args)


def _dw_kernel(mbs, idx_ref, h_ref, s_ref, dw_ref):
    rows = h_ref.shape[1] * h_ref.shape[2]
    for j in range(dw_ref.shape[0] // NSUB):
        layer = j * NSUB // KMAX

        @pl.when(idx_ref[3 * j * NSUB + 2] > 0)
        def _():
            for k in range(j * NSUB, (j + 1) * NSUB):
                r = idx_ref[3 * k]
                c = idx_ref[3 * k + 1]
                hb = h_ref[layer, :, :, _blk(r)]
                sb = s_ref[layer, :, :, _blk(c)]
                dw_ref[k] = lax.dot_general(
                    hb.reshape(rows, BLK),
                    sb.reshape(rows, BLK),
                    (((0,), (0,)), ((), ())),
                    preferred_element_type=jnp.float32,
                ) * _flag(idx_ref, k)

        @pl.when(idx_ref[3 * j * NSUB + 2] <= 0)
        def _():
            dw_ref[pl.ds(j * NSUB, NSUB)] = jnp.zeros((NSUB, BLK, BLK), jnp.float32)


def segment_dw(stash_h, stash_s, block_index, mbs):
    return pl.pallas_call(
        functools.partial(_dw_kernel, mbs),
        out_shape=jax.ShapeDtypeStruct((block_index.shape[0], BLK, BLK), jnp.float32),
        in_specs=[_SMEM, _VMEM, _VMEM],
        out_specs=_VMEM,
        compiler_params=pltpu.CompilerParams(vmem_limit_bytes=VMEM_LIMIT),
    )(block_index.reshape(-1), stash_h, stash_s)


def _dw_half_kernel(sel_ref, idx_ref, h_ref, s_ref, out_ref):
    b0 = sel_ref[0]
    rows = h_ref.shape[1] * h_ref.shape[2]
    per = out_ref.shape[1]
    for q in range(out_ref.shape[0]):
        layer = (2 * q * per) // KMAX
        spot = q + b0 * ((q % 2) * 2 + q // 2 - q)
        for j in range(per // NSUB):
            first = 2 * q * per + b0 * per + j * NSUB

            @pl.when(idx_ref[3 * first + 2] > 0)
            def _():
                for i in range(NSUB):
                    k = first + i
                    r = idx_ref[3 * k]
                    c = idx_ref[3 * k + 1]
                    hb = h_ref[layer, :, :, _blk(r)].reshape(rows, BLK)
                    sb = s_ref[layer, :, :, _blk(c)].reshape(rows, BLK)
                    part = lax.dot_general(
                        hb, sb, (((0,), (0,)), ((), ())), preferred_element_type=jnp.float32
                    )
                    out_ref[spot, j * NSUB + i] = (part * _flag(idx_ref, k)).astype(out_ref.dtype)

            @pl.when(idx_ref[3 * first + 2] <= 0)
            def _():
                out_ref[spot, pl.ds(j * NSUB, NSUB)] = jnp.zeros((NSUB, BLK, BLK), out_ref.dtype)


def dw_half(stash_h, stash_s, block_index, b0, dtype):
    per = block_index.shape[0] // 8
    return pl.pallas_call(
        _dw_half_kernel,
        out_shape=jax.ShapeDtypeStruct((4, per, BLK, BLK), dtype),
        in_specs=[_SMEM, _SMEM, _VMEM, _VMEM],
        out_specs=_VMEM,
        compiler_params=pltpu.CompilerParams(vmem_limit_bytes=VMEM_LIMIT),
    )(b0.reshape(1).astype(jnp.int32), block_index.reshape(-1), stash_h, stash_s)


def _exchange(send, pairs):
    return lax.ppermute(send.astype(jnp.bfloat16), "dp", pairs).astype(jnp.float32)


def weight_grads(stash_h, stash_s, block_index, mbs):
    n = lax.axis_size("dp")
    if n != 8:
        acc = segment_dw(stash_h, stash_s, block_index, mbs)
        return lax.psum_scatter(
            acc.astype(jnp.bfloat16), "dp", scatter_dimension=0, tiled=True
        ).astype(jnp.float32)
    d = lax.axis_index("dp")
    d0, d1, d2 = d % 2, (d // 2) % 2, d // 4
    pick = lambda a, i, axis: lax.dynamic_index_in_dim(a, i, axis, keepdims=False)
    send = dw_half(stash_h, stash_s, block_index, 1 - d0, jnp.bfloat16)
    got = lax.ppermute(send, "dp", [(i, i ^ 1) for i in range(8)])
    keep = dw_half(stash_h, stash_s, block_index, d0, jnp.float32)
    keep = keep.reshape((2, 2) + keep.shape[1:])
    got = got.reshape(keep.shape)
    core0 = d0 == 0
    flip = jnp.where(core0, d1, d2)
    rem = jnp.where(core0, d2, d1)

    def summed(a, b, i):
        return pick(a, i, 1) + pick(b, i, 1).astype(jnp.float32)

    got2 = _exchange(summed(keep, got, 1 - flip), [(i, i ^ (2 if i % 2 == 0 else 4)) for i in range(8)])

    def part(i):
        return pick(pick(keep, flip, 1), i, 0) + pick(pick(got, flip, 1), i, 0).astype(jnp.float32) + pick(got2, i, 0)

    got3 = _exchange(part(1 - rem), [(i, i ^ (4 if i % 2 == 0 else 2)) for i in range(8)])
    return part(rem) + got3


def _allocate_kernel(*refs):
    del refs


def allocate(specs):
    return pl.pallas_call(
        _allocate_kernel,
        out_shape=tuple(jax.ShapeDtypeStruct(shape, dtype) for shape, dtype in specs),
        out_specs=tuple(_ANY for _ in specs),
    )()


def on_device(x_in, cotangent, weights, block_index):
    segments = lax.axis_size("segment")
    me_segment = lax.axis_index("segment")
    mbs, rows_dev, width = x_in.shape
    mbs, rows_dev = mbs * SPLIT, rows_dev // SPLIT
    x_in = x_in.reshape(mbs, rows_dev, width)
    cotangent = cotangent.reshape(mbs, rows_dev, width)
    idx = block_index.reshape(LSLOT, KMAX, 3)

    def tick_body(tick, carry):
        recv_f, recv_b, saved_h, saved_y, saved_s = carry
        micro_f = tick - me_segment
        live_f = (micro_f >= 0) & (micro_f < mbs)
        at_f = jnp.clip(micro_f, 0, mbs - 1)
        def run_f(operands):
            h, sh, sy = operands
            for layer in range(LSLOT):
                local = (x_in, me_segment == 0) if layer == 0 else (None, None)
                h, sh, sy = layer_forward(h, weights, layer, block_index, at_f, sh, sy, *local)
            return (h, sh, sy)

        h_out, saved_h, saved_y = lax.cond(live_f, run_f, lambda ops: ops, (recv_f, saved_h, saved_y))
        send_f = shifted(h_out, "segment", 1)

        micro_b = tick - (2 * segments - 2 - me_segment)
        live_b = (micro_b >= 0) & (micro_b < mbs)
        at_b = jnp.clip(micro_b, 0, mbs - 1)
        stash_y_now = saved_y

        def run_b(operands):
            grad, ss = operands
            for layer in reversed(range(LSLOT)):
                local = (cotangent, me_segment == segments - 1) if layer == LSLOT - 1 else (None, None)
                grad, ss = layer_backward(grad, stash_y_now, weights, layer, block_index, at_b, ss, *local)
            return (grad, ss)

        grad_out, saved_s = lax.cond(live_b, run_b, lambda ops: ops, (recv_b, saved_s))
        send_b = shifted(grad_out, "segment", -1)
        return (send_f, send_b, saved_h, saved_y, saved_s)

    stash_shape = (LSLOT, mbs, rows_dev, width)
    stash_h, stash_y, stash_s = allocate(
        [(stash_shape, jnp.bfloat16), (stash_shape, jnp.float32), (stash_shape, jnp.bfloat16)]
    )
    blank = jnp.zeros((rows_dev, width), jnp.bfloat16)
    ticks = mbs + 2 * segments - 2
    carry = (blank, blank, stash_h, stash_y, stash_s)
    for tick in range(ticks):
        carry = tick_body(tick, carry)
    unused_f, unused_b, stash_h, stash_y, stash_s = carry
    return weight_grads(stash_h, stash_s, block_index, mbs)


def solution(mesh):
    return jax.shard_map(
        on_device,
        mesh=mesh,
        in_specs=(
            P(None, "dp", None),
            P(None, "dp", None),
            P("segment", None, None),
            P("segment", None),
        ),
        out_specs=P(("segment", "dp"), None, None),
        check_vma=False,
    )
```

```python
import functools

import jax
import jax.numpy as jnp
from jax import lax
from jax.experimental import pallas as pl
from jax.experimental.pallas import tpu as pltpu
from jax.sharding import PartitionSpec as P

BLK = 128
LSLOT = 2
KMAX = 128
CH = 1024
NSUB = 32
SPLIT = 2
GROUP = 16
VMEM_LIMIT = 60 * 1024 * 1024

_SMEM = pl.BlockSpec(memory_space=pltpu.SMEM)
_VMEM = pl.BlockSpec(memory_space=pltpu.VMEM)
_ANY = pl.BlockSpec(memory_space=pl.ANY)


def shifted(value, axis, steps):
    count = lax.axis_size(axis)
    leading, last = (max(0, -steps), min(count, count - steps))
    return lax.ppermute(value, axis, [(source, source + steps) for source in range(leading, last)])


def _blk(i):
    return pl.ds(pl.multiple_of(i * BLK, BLK), BLK)


def _chunk(j):
    return pl.ds(pl.multiple_of(j * CH, CH), CH)


def _flag(idx_ref, k):
    return jnp.where(idx_ref[3 * k + 2] > 0, 1.0, 0.0).astype(jnp.float32)


class _WeightChunks:
    def __init__(self, w_hbm, base, w_vmem, sems):
        self.w_hbm, self.base, self.w_vmem, self.sems = w_hbm, base, w_vmem, sems

    def copy(self, j):
        return pltpu.make_async_copy(
            self.w_hbm.at[pl.ds(self.base + j * NSUB, NSUB)],
            self.w_vmem.at[pl.ds(j * NSUB, NSUB)],
            self.sems.at[j],
        )

    def wait_on(self, j):
        self.copy(j).wait()


def _w_copies(w_hbm, base, w_vmem, sems):
    chunks = _WeightChunks(w_hbm, base, w_vmem, sems)
    started = []
    for j in range(w_vmem.shape[0] // NSUB):
        copy = chunks.copy(j)
        copy.start()
        started.append(copy)
    return (chunks, started)


def _slot_chunks(idx_ref, base, copies, product, update):
    def chunk(j, carry):
        copies[0].wait_on(j)

        @pl.when(idx_ref[3 * (base + j * NSUB) + 2] > 0)
        def _():
            for g in range(0, NSUB, GROUP):
                ks = [j * NSUB + g + i for i in range(GROUP)]
                parts = [product(k) for k in ks]
                for k, part in zip(ks, parts):
                    update(k, part)

        return carry

    lax.fori_loop(0, len(copies[1]), chunk, 0)


def _pick_input(at, src_ref, local_hbm, h_ref, sem):
    @pl.when(at[1] > 0)
    def _():
        pltpu.make_async_copy(local_hbm.at[at[0]], h_ref, sem).start()

    @pl.when(at[1] <= 0)
    def _():
        pltpu.make_async_copy(src_ref, h_ref, sem).start()

    pltpu.make_async_copy(src_ref, h_ref, sem).wait()


def _fwd_kernel(base, layer, at_ref, idx_ref, h_in, w_hbm, sh_in, sy_in, *rest):
    if layer == 0:
        local_hbm, hout_ref, sh_ref, sy_ref, w_vmem, y_vmem, sems, io_sems, h_ref = rest
    else:
        hout_ref, sh_ref, sy_ref, w_vmem, y_vmem, sems, io_sems = rest
        h_ref = h_in
    del sh_in, sy_in
    width = h_ref.shape[1]
    at = at_ref[0]
    copies = _w_copies(w_hbm, base, w_vmem, sems)
    if layer == 0:
        _pick_input((at, at_ref[1]), h_in, local_hbm, h_ref, io_sems.at[2])
    save_h = pltpu.make_async_copy(h_ref, sh_ref.at[layer, at], io_sems.at[0])
    save_h.start()
    y_vmem[...] = jnp.zeros_like(y_vmem)

    def product(k):
        r = idx_ref[3 * (base + k)]
        return jnp.dot(h_ref[:, _blk(r)], w_vmem[k], preferred_element_type=jnp.float32)

    def update(k, p):
        c = idx_ref[3 * (base + k) + 1]
        y_vmem[:, _blk(c)] += p * _flag(idx_ref, base + k)

    _slot_chunks(idx_ref, base, copies, product, update)
    save_y = pltpu.make_async_copy(y_vmem, sy_ref.at[layer, at], io_sems.at[1])
    save_y.start()

    def epi(j, carry):
        y = y_vmem[:, _chunk(j)]
        h = h_ref[:, _chunk(j)].astype(jnp.float32)
        hout_ref[:, _chunk(j)] = (h + y / (1.0 + jnp.exp(-y))).astype(hout_ref.dtype)
        return carry

    lax.fori_loop(0, width // CH, epi, 0)
    save_h.wait()
    save_y.wait()


def layer_forward(h, weights, layer, block_index, at, stash_h, stash_y, local=None, use_local=None):
    rows, width = h.shape
    extra_in, extra_args, extra_scratch = [], [], []
    if layer == 0:
        extra_in, extra_args = [_ANY], [local]
        extra_scratch = [pltpu.VMEM((rows, width), h.dtype)]
        at = jnp.stack([at, use_local.astype(jnp.int32)])
    return pl.pallas_call(
        functools.partial(_fwd_kernel, layer * KMAX, layer),
        out_shape=(
            jax.ShapeDtypeStruct((rows, width), jnp.bfloat16),
            jax.ShapeDtypeStruct(stash_h.shape, stash_h.dtype),
            jax.ShapeDtypeStruct(stash_y.shape, stash_y.dtype),
        ),
        in_specs=[_SMEM, _SMEM, _VMEM, _ANY, _ANY, _ANY] + extra_in,
        out_specs=(_VMEM, _ANY, _ANY),
        scratch_shapes=[
            pltpu.VMEM((KMAX, BLK, BLK), weights.dtype),
            pltpu.VMEM((rows, width), jnp.float32),
            pltpu.SemaphoreType.DMA((KMAX // NSUB,)),
            pltpu.SemaphoreType.DMA((3,)),
        ]
        + extra_scratch,
        input_output_aliases={4: 1, 5: 2},
        compiler_params=pltpu.CompilerParams(vmem_limit_bytes=VMEM_LIMIT),
    )(at.reshape(-1), block_index.reshape(-1), h, weights, stash_h, stash_y, *extra_args)


def _bwd_kernel(base, layer, entry, at_ref, idx_ref, g_in, sy_hbm, w_hbm, ss_in, *rest):
    if entry:
        local_hbm, gout_ref, ss_ref, y_vmem, s_vmem, sp_ref, w_vmem, sems, io_sems, g_ref = rest
    else:
        gout_ref, ss_ref, y_vmem, s_vmem, sp_ref, w_vmem, sems, io_sems = rest
        g_ref = g_in
    del ss_in
    width = g_ref.shape[1]
    at = at_ref[0]
    if entry:
        _pick_input((at, at_ref[1]), g_in, local_hbm, g_ref, io_sems.at[2])
    load_y = pltpu.make_async_copy(sy_hbm.at[layer, at], y_vmem, io_sems.at[0])
    load_y.start()
    copies = _w_copies(w_hbm, base, w_vmem, sems)
    load_y.wait()

    def pre(j, carry):
        y = y_vmem[:, _chunk(j)]
        sig = 1.0 / (1.0 + jnp.exp(-y))
        g = g_ref[:, _chunk(j)].astype(jnp.float32)
        s_vmem[:, _chunk(j)] = (g * sig * (1.0 + y * (1.0 - sig))).astype(s_vmem.dtype)
        sp_ref[:, _chunk(j)] = jnp.zeros((g_ref.shape[0], CH), jnp.float32)
        return carry

    lax.fori_loop(0, width // CH, pre, 0)
    save_s = pltpu.make_async_copy(s_vmem, ss_ref.at[layer, at], io_sems.at[1])
    save_s.start()

    def product(k):
        c = idx_ref[3 * (base + k) + 1]
        return lax.dot_general(
            s_vmem[:, _blk(c)],
            w_vmem[k],
            (((1,), (1,)), ((), ())),
            preferred_element_type=jnp.float32,
        )

    def update(k, back):
        r = idx_ref[3 * (base + k)]
        sp_ref[:, _blk(r)] += back * _flag(idx_ref, base + k)

    _slot_chunks(idx_ref, base, copies, product, update)

    def epi(j, carry):
        g = g_ref[:, _chunk(j)].astype(jnp.float32)
        gout_ref[:, _chunk(j)] = (g + sp_ref[:, _chunk(j)]).astype(gout_ref.dtype)
        return carry

    lax.fori_loop(0, width // CH, epi, 0)
    save_s.wait()


def layer_backward(g, stash_y, weights, layer, block_index, at, stash_s, local=None, use_local=None):
    rows, width = g.shape
    entry = local is not None
    extra_in, extra_args, extra_scratch = [], [], []
    if entry:
        extra_in, extra_args = [_ANY], [local]
        extra_scratch = [pltpu.VMEM((rows, width), g.dtype)]
        at = jnp.stack([at, use_local.astype(jnp.int32)])
    return pl.pallas_call(
        functools.partial(_bwd_kernel, layer * KMAX, layer, entry),
        out_shape=(
            jax.ShapeDtypeStruct((rows, width), jnp.bfloat16),
            jax.ShapeDtypeStruct(stash_s.shape, stash_s.dtype),
        ),
        in_specs=[_SMEM, _SMEM, _VMEM, _ANY, _ANY, _ANY] + extra_in,
        out_specs=(_VMEM, _ANY),
        scratch_shapes=[
            pltpu.VMEM((rows, width), jnp.float32),
            pltpu.VMEM((rows, width), jnp.bfloat16),
            pltpu.VMEM((rows, width), jnp.float32),
            pltpu.VMEM((KMAX, BLK, BLK), weights.dtype),
            pltpu.SemaphoreType.DMA((KMAX // NSUB,)),
            pltpu.SemaphoreType.DMA((3,)),
        ]
        + extra_scratch,
        input_output_aliases={5: 1},
        compiler_params=pltpu.CompilerParams(vmem_limit_bytes=VMEM_LIMIT),
    )(at.reshape(-1), block_index.reshape(-1), g, stash_y, weights, stash_s, *extra_args)


def _dw_kernel(mbs, idx_ref, h_ref, s_ref, dw_ref):
    rows = h_ref.shape[1] * h_ref.shape[2]
    for j in range(dw_ref.shape[0] // NSUB):
        layer = j * NSUB // KMAX

        @pl.when(idx_ref[3 * j * NSUB + 2] > 0)
        def _():
            for k in range(j * NSUB, (j + 1) * NSUB):
                r = idx_ref[3 * k]
                c = idx_ref[3 * k + 1]
                hb = h_ref[layer, :, :, _blk(r)]
                sb = s_ref[layer, :, :, _blk(c)]
                dw_ref[k] = lax.dot_general(
                    hb.reshape(rows, BLK),
                    sb.reshape(rows, BLK),
                    (((0,), (0,)), ((), ())),
                    preferred_element_type=jnp.float32,
                ) * _flag(idx_ref, k)

        @pl.when(idx_ref[3 * j * NSUB + 2] <= 0)
        def _():
            dw_ref[pl.ds(j * NSUB, NSUB)] = jnp.zeros((NSUB, BLK, BLK), jnp.float32)


def segment_dw(stash_h, stash_s, block_index, mbs):
    return pl.pallas_call(
        functools.partial(_dw_kernel, mbs),
        out_shape=jax.ShapeDtypeStruct((block_index.shape[0], BLK, BLK), jnp.float32),
        in_specs=[_SMEM, _VMEM, _VMEM],
        out_specs=_VMEM,
        compiler_params=pltpu.CompilerParams(vmem_limit_bytes=VMEM_LIMIT),
    )(block_index.reshape(-1), stash_h, stash_s)


def _dw_half_kernel(sel_ref, idx_ref, h_ref, s_ref, out_ref):
    b0 = sel_ref[0]
    rows = h_ref.shape[1] * h_ref.shape[2]
    per = out_ref.shape[1]
    for q in range(out_ref.shape[0]):
        layer = (2 * q * per) // KMAX
        spot = q + b0 * ((q % 2) * 2 + q // 2 - q)
        for j in range(per // NSUB):
            first = 2 * q * per + b0 * per + j * NSUB

            @pl.when(idx_ref[3 * first + 2] > 0)
            def _():
                for i in range(NSUB):
                    k = first + i
                    r = idx_ref[3 * k]
                    c = idx_ref[3 * k + 1]
                    hb = h_ref[layer, :, :, _blk(r)].reshape(rows, BLK)
                    sb = s_ref[layer, :, :, _blk(c)].reshape(rows, BLK)
                    part = lax.dot_general(
                        hb, sb, (((0,), (0,)), ((), ())), preferred_element_type=jnp.float32
                    )
                    out_ref[spot, j * NSUB + i] = (part * _flag(idx_ref, k)).astype(out_ref.dtype)

            @pl.when(idx_ref[3 * first + 2] <= 0)
            def _():
                out_ref[spot, pl.ds(j * NSUB, NSUB)] = jnp.zeros((NSUB, BLK, BLK), out_ref.dtype)


def dw_half(stash_h, stash_s, block_index, b0, dtype):
    per = block_index.shape[0] // 8
    return pl.pallas_call(
        _dw_half_kernel,
        out_shape=jax.ShapeDtypeStruct((4, per, BLK, BLK), dtype),
        in_specs=[_SMEM, _SMEM, _VMEM, _VMEM],
        out_specs=_VMEM,
        compiler_params=pltpu.CompilerParams(vmem_limit_bytes=VMEM_LIMIT),
    )(b0.reshape(1).astype(jnp.int32), block_index.reshape(-1), stash_h, stash_s)


def _exchange(send, pairs):
    return lax.ppermute(send.astype(jnp.bfloat16), "dp", pairs).astype(jnp.float32)


def weight_grads(stash_h, stash_s, block_index, mbs):
    n = lax.axis_size("dp")
    if n != 8:
        acc = segment_dw(stash_h, stash_s, block_index, mbs)
        return lax.psum_scatter(
            acc.astype(jnp.bfloat16), "dp", scatter_dimension=0, tiled=True
        ).astype(jnp.float32)
    d = lax.axis_index("dp")
    d0, d1, d2 = d % 2, (d // 2) % 2, d // 4
    pick = lambda a, i, axis: lax.dynamic_index_in_dim(a, i, axis, keepdims=False)
    send = dw_half(stash_h, stash_s, block_index, 1 - d0, jnp.bfloat16)
    got = lax.ppermute(send, "dp", [(i, i ^ 1) for i in range(8)])
    keep = dw_half(stash_h, stash_s, block_index, d0, jnp.float32)
    keep = keep.reshape((2, 2) + keep.shape[1:])
    got = got.reshape(keep.shape)
    core0 = d0 == 0
    flip = jnp.where(core0, d1, d2)
    rem = jnp.where(core0, d2, d1)

    def summed(a, b, i):
        return pick(a, i, 1) + pick(b, i, 1).astype(jnp.float32)

    got2 = _exchange(summed(keep, got, 1 - flip), [(i, i ^ (2 if i % 2 == 0 else 4)) for i in range(8)])

    def part(i):
        return pick(pick(keep, flip, 1), i, 0) + pick(pick(got, flip, 1), i, 0).astype(jnp.float32) + pick(got2, i, 0)

    got3 = _exchange(part(1 - rem), [(i, i ^ (4 if i % 2 == 0 else 2)) for i in range(8)])
    return part(rem) + got3


def _allocate_kernel(*refs):
    del refs


def allocate(specs):
    return pl.pallas_call(
        _allocate_kernel,
        out_shape=tuple(jax.ShapeDtypeStruct(shape, dtype) for shape, dtype in specs),
        out_specs=tuple(_ANY for _ in specs),
    )()


def on_device(x_in, cotangent, weights, block_index):
    segments = lax.axis_size("segment")
    me_segment = lax.axis_index("segment")
    mbs, rows_dev, width = x_in.shape
    mbs, rows_dev = mbs * SPLIT, rows_dev // SPLIT
    x_in = x_in.reshape(mbs, rows_dev, width)
    cotangent = cotangent.reshape(mbs, rows_dev, width)
    idx = block_index.reshape(LSLOT, KMAX, 3)

    def tick_body(tick, carry):
        recv_f, recv_b, saved_h, saved_y, saved_s = carry
        micro_f = tick - me_segment
        live_f = (micro_f >= 0) & (micro_f < mbs)
        at_f = jnp.clip(micro_f, 0, mbs - 1)
        def run_f(operands):
            h, sh, sy = operands
            for layer in range(LSLOT):
                local = (x_in, me_segment == 0) if layer == 0 else (None, None)
                h, sh, sy = layer_forward(h, weights, layer, block_index, at_f, sh, sy, *local)
            return (h, sh, sy)

        h_out, saved_h, saved_y = lax.cond(live_f, run_f, lambda ops: ops, (recv_f, saved_h, saved_y))
        send_f = shifted(h_out, "segment", 1)

        micro_b = tick - (2 * segments - 2 - me_segment)
        live_b = (micro_b >= 0) & (micro_b < mbs)
        at_b = jnp.clip(micro_b, 0, mbs - 1)
        stash_y_now = saved_y

        def run_b(operands):
            grad, ss = operands
            for layer in reversed(range(LSLOT)):
                local = (cotangent, me_segment == segments - 1) if layer == LSLOT - 1 else (None, None)
                grad, ss = layer_backward(grad, stash_y_now, weights, layer, block_index, at_b, ss, *local)
            return (grad, ss)

        grad_out, saved_s = lax.cond(live_b, run_b, lambda ops: ops, (recv_b, saved_s))
        send_b = shifted(grad_out, "segment", -1)
        return (send_f, send_b, saved_h, saved_y, saved_s)

    stash_shape = (LSLOT, mbs, rows_dev, width)
    stash_h, stash_y, stash_s = allocate(
        [(stash_shape, jnp.bfloat16), (stash_shape, jnp.float32), (stash_shape, jnp.bfloat16)]
    )
    blank = jnp.zeros((rows_dev, width), jnp.bfloat16)
    ticks = mbs + 2 * segments - 2
    carry = (blank, blank, stash_h, stash_y, stash_s)
    for tick in range(ticks):
        carry = tick_body(tick, carry)
    unused_f, unused_b, stash_h, stash_y, stash_s = carry
    return weight_grads(stash_h, stash_s, block_index, mbs)


def solution(mesh):
    return jax.shard_map(
        on_device,
        mesh=mesh,
        in_specs=(
            P(None, "dp", None),
            P(None, "dp", None),
            P("segment", None, None),
            P("segment", None),
        ),
        out_specs=P(("segment", "dp"), None, None),
        check_vma=False,
    )
```

```python
import functools

import jax
import jax.numpy as jnp
from jax import lax
from jax.experimental import pallas as pl
from jax.experimental.pallas import tpu as pltpu
from jax.sharding import PartitionSpec as P

BLK = 128
LSLOT = 2
KMAX = 128
CH = 1024
NSUB = 32
SPLIT = 2
GROUP = 32
VMEM_LIMIT = 60 * 1024 * 1024

_SMEM = pl.BlockSpec(memory_space=pltpu.SMEM)
_VMEM = pl.BlockSpec(memory_space=pltpu.VMEM)
_ANY = pl.BlockSpec(memory_space=pl.ANY)


def shifted(value, axis, steps):
    count = lax.axis_size(axis)
    leading, last = (max(0, -steps), min(count, count - steps))
    return lax.ppermute(value, axis, [(source, source + steps) for source in range(leading, last)])


def _blk(i):
    return pl.ds(pl.multiple_of(i * BLK, BLK), BLK)


def _chunk(j):
    return pl.ds(pl.multiple_of(j * CH, CH), CH)


def _flag(idx_ref, k):
    return jnp.where(idx_ref[3 * k + 2] > 0, 1.0, 0.0).astype(jnp.float32)


class _WeightChunks:
    def __init__(self, w_hbm, base, w_vmem, sems):
        self.w_hbm, self.base, self.w_vmem, self.sems = w_hbm, base, w_vmem, sems

    def copy(self, j):
        return pltpu.make_async_copy(
            self.w_hbm.at[pl.ds(self.base + j * NSUB, NSUB)],
            self.w_vmem.at[pl.ds(j * NSUB, NSUB)],
            self.sems.at[j],
        )

    def wait_on(self, j):
        self.copy(j).wait()


def _w_copies(w_hbm, base, w_vmem, sems):
    chunks = _WeightChunks(w_hbm, base, w_vmem, sems)
    started = []
    for j in range(w_vmem.shape[0] // NSUB):
        copy = chunks.copy(j)
        copy.start()
        started.append(copy)
    return (chunks, started)


def _slot_chunks(idx_ref, base, copies, product, update):
    def chunk(j, carry):
        copies[0].wait_on(j)

        @pl.when(idx_ref[3 * (base + j * NSUB) + 2] > 0)
        def _():
            for g in range(0, NSUB, GROUP):
                ks = [j * NSUB + g + i for i in range(GROUP)]
                parts = [product(k) for k in ks]
                for k, part in zip(ks, parts):
                    update(k, part)

        return carry

    lax.fori_loop(0, len(copies[1]), chunk, 0)


def _pick_input(at, src_ref, local_hbm, h_ref, sem):
    @pl.when(at[1] > 0)
    def _():
        pltpu.make_async_copy(local_hbm.at[at[0]], h_ref, sem).start()

    @pl.when(at[1] <= 0)
    def _():
        pltpu.make_async_copy(src_ref, h_ref, sem).start()

    pltpu.make_async_copy(src_ref, h_ref, sem).wait()


def _fwd_kernel(base, layer, at_ref, idx_ref, h_in, w_hbm, sh_in, sy_in, *rest):
    if layer == 0:
        local_hbm, hout_ref, sh_ref, sy_ref, w_vmem, y_vmem, sems, io_sems, h_ref = rest
    else:
        hout_ref, sh_ref, sy_ref, w_vmem, y_vmem, sems, io_sems = rest
        h_ref = h_in
    del sh_in, sy_in
    width = h_ref.shape[1]
    at = at_ref[0]
    copies = _w_copies(w_hbm, base, w_vmem, sems)
    if layer == 0:
        _pick_input((at, at_ref[1]), h_in, local_hbm, h_ref, io_sems.at[2])
    save_h = pltpu.make_async_copy(h_ref, sh_ref.at[layer, at], io_sems.at[0])
    save_h.start()
    y_vmem[...] = jnp.zeros_like(y_vmem)

    def product(k):
        r = idx_ref[3 * (base + k)]
        return jnp.dot(h_ref[:, _blk(r)], w_vmem[k], preferred_element_type=jnp.float32)

    def update(k, p):
        c = idx_ref[3 * (base + k) + 1]
        y_vmem[:, _blk(c)] += p * _flag(idx_ref, base + k)

    _slot_chunks(idx_ref, base, copies, product, update)
    save_y = pltpu.make_async_copy(y_vmem, sy_ref.at[layer, at], io_sems.at[1])
    save_y.start()

    def epi(j, carry):
        y = y_vmem[:, _chunk(j)]
        h = h_ref[:, _chunk(j)].astype(jnp.float32)
        hout_ref[:, _chunk(j)] = (h + y / (1.0 + jnp.exp(-y))).astype(hout_ref.dtype)
        return carry

    lax.fori_loop(0, width // CH, epi, 0)
    save_h.wait()
    save_y.wait()


def layer_forward(h, weights, layer, block_index, at, stash_h, stash_y, local=None, use_local=None):
    rows, width = h.shape
    extra_in, extra_args, extra_scratch = [], [], []
    if layer == 0:
        extra_in, extra_args = [_ANY], [local]
        extra_scratch = [pltpu.VMEM((rows, width), h.dtype)]
        at = jnp.stack([at, use_local.astype(jnp.int32)])
    return pl.pallas_call(
        functools.partial(_fwd_kernel, layer * KMAX, layer),
        out_shape=(
            jax.ShapeDtypeStruct((rows, width), jnp.bfloat16),
            jax.ShapeDtypeStruct(stash_h.shape, stash_h.dtype),
            jax.ShapeDtypeStruct(stash_y.shape, stash_y.dtype),
        ),
        in_specs=[_SMEM, _SMEM, _VMEM, _ANY, _ANY, _ANY] + extra_in,
        out_specs=(_VMEM, _ANY, _ANY),
        scratch_shapes=[
            pltpu.VMEM((KMAX, BLK, BLK), weights.dtype),
            pltpu.VMEM((rows, width), jnp.float32),
            pltpu.SemaphoreType.DMA((KMAX // NSUB,)),
            pltpu.SemaphoreType.DMA((3,)),
        ]
        + extra_scratch,
        input_output_aliases={4: 1, 5: 2},
        compiler_params=pltpu.CompilerParams(vmem_limit_bytes=VMEM_LIMIT),
    )(at.reshape(-1), block_index.reshape(-1), h, weights, stash_h, stash_y, *extra_args)


def _bwd_kernel(base, layer, entry, at_ref, idx_ref, g_in, sy_hbm, w_hbm, ss_in, *rest):
    if entry:
        local_hbm, gout_ref, ss_ref, y_vmem, s_vmem, sp_ref, w_vmem, sems, io_sems, g_ref = rest
    else:
        gout_ref, ss_ref, y_vmem, s_vmem, sp_ref, w_vmem, sems, io_sems = rest
        g_ref = g_in
    del ss_in
    width = g_ref.shape[1]
    at = at_ref[0]
    if entry:
        _pick_input((at, at_ref[1]), g_in, local_hbm, g_ref, io_sems.at[2])
    load_y = pltpu.make_async_copy(sy_hbm.at[layer, at], y_vmem, io_sems.at[0])
    load_y.start()
    copies = _w_copies(w_hbm, base, w_vmem, sems)
    load_y.wait()

    def pre(j, carry):
        y = y_vmem[:, _chunk(j)]
        sig = 1.0 / (1.0 + jnp.exp(-y))
        g = g_ref[:, _chunk(j)].astype(jnp.float32)
        s_vmem[:, _chunk(j)] = (g * sig * (1.0 + y * (1.0 - sig))).astype(s_vmem.dtype)
        sp_ref[:, _chunk(j)] = jnp.zeros((g_ref.shape[0], CH), jnp.float32)
        return carry

    lax.fori_loop(0, width // CH, pre, 0)
    save_s = pltpu.make_async_copy(s_vmem, ss_ref.at[layer, at], io_sems.at[1])
    save_s.start()

    def product(k):
        c = idx_ref[3 * (base + k) + 1]
        return lax.dot_general(
            s_vmem[:, _blk(c)],
            w_vmem[k],
            (((1,), (1,)), ((), ())),
            preferred_element_type=jnp.float32,
        )

    def update(k, back):
        r = idx_ref[3 * (base + k)]
        sp_ref[:, _blk(r)] += back * _flag(idx_ref, base + k)

    _slot_chunks(idx_ref, base, copies, product, update)

    def epi(j, carry):
        g = g_ref[:, _chunk(j)].astype(jnp.float32)
        gout_ref[:, _chunk(j)] = (g + sp_ref[:, _chunk(j)]).astype(gout_ref.dtype)
        return carry

    lax.fori_loop(0, width // CH, epi, 0)
    save_s.wait()


def layer_backward(g, stash_y, weights, layer, block_index, at, stash_s, local=None, use_local=None):
    rows, width = g.shape
    entry = local is not None
    extra_in, extra_args, extra_scratch = [], [], []
    if entry:
        extra_in, extra_args = [_ANY], [local]
        extra_scratch = [pltpu.VMEM((rows, width), g.dtype)]
        at = jnp.stack([at, use_local.astype(jnp.int32)])
    return pl.pallas_call(
        functools.partial(_bwd_kernel, layer * KMAX, layer, entry),
        out_shape=(
            jax.ShapeDtypeStruct((rows, width), jnp.bfloat16),
            jax.ShapeDtypeStruct(stash_s.shape, stash_s.dtype),
        ),
        in_specs=[_SMEM, _SMEM, _VMEM, _ANY, _ANY, _ANY] + extra_in,
        out_specs=(_VMEM, _ANY),
        scratch_shapes=[
            pltpu.VMEM((rows, width), jnp.float32),
            pltpu.VMEM((rows, width), jnp.bfloat16),
            pltpu.VMEM((rows, width), jnp.float32),
            pltpu.VMEM((KMAX, BLK, BLK), weights.dtype),
            pltpu.SemaphoreType.DMA((KMAX // NSUB,)),
            pltpu.SemaphoreType.DMA((3,)),
        ]
        + extra_scratch,
        input_output_aliases={5: 1},
        compiler_params=pltpu.CompilerParams(vmem_limit_bytes=VMEM_LIMIT),
    )(at.reshape(-1), block_index.reshape(-1), g, stash_y, weights, stash_s, *extra_args)


def _dw_kernel(mbs, idx_ref, h_ref, s_ref, dw_ref):
    rows = h_ref.shape[1] * h_ref.shape[2]
    for j in range(dw_ref.shape[0] // NSUB):
        layer = j * NSUB // KMAX

        @pl.when(idx_ref[3 * j * NSUB + 2] > 0)
        def _():
            for k in range(j * NSUB, (j + 1) * NSUB):
                r = idx_ref[3 * k]
                c = idx_ref[3 * k + 1]
                hb = h_ref[layer, :, :, _blk(r)]
                sb = s_ref[layer, :, :, _blk(c)]
                dw_ref[k] = lax.dot_general(
                    hb.reshape(rows, BLK),
                    sb.reshape(rows, BLK),
                    (((0,), (0,)), ((), ())),
                    preferred_element_type=jnp.float32,
                ) * _flag(idx_ref, k)

        @pl.when(idx_ref[3 * j * NSUB + 2] <= 0)
        def _():
            dw_ref[pl.ds(j * NSUB, NSUB)] = jnp.zeros((NSUB, BLK, BLK), jnp.float32)


def segment_dw(stash_h, stash_s, block_index, mbs):
    return pl.pallas_call(
        functools.partial(_dw_kernel, mbs),
        out_shape=jax.ShapeDtypeStruct((block_index.shape[0], BLK, BLK), jnp.float32),
        in_specs=[_SMEM, _VMEM, _VMEM],
        out_specs=_VMEM,
        compiler_params=pltpu.CompilerParams(vmem_limit_bytes=VMEM_LIMIT),
    )(block_index.reshape(-1), stash_h, stash_s)


def _dw_half_kernel(sel_ref, idx_ref, h_ref, s_ref, out_ref):
    b0 = sel_ref[0]
    rows = h_ref.shape[1] * h_ref.shape[2]
    per = out_ref.shape[1]
    for q in range(out_ref.shape[0]):
        layer = (2 * q * per) // KMAX
        spot = q + b0 * ((q % 2) * 2 + q // 2 - q)
        for j in range(per // NSUB):
            first = 2 * q * per + b0 * per + j * NSUB

            @pl.when(idx_ref[3 * first + 2] > 0)
            def _():
                for i in range(NSUB):
                    k = first + i
                    r = idx_ref[3 * k]
                    c = idx_ref[3 * k + 1]
                    hb = h_ref[layer, :, :, _blk(r)].reshape(rows, BLK)
                    sb = s_ref[layer, :, :, _blk(c)].reshape(rows, BLK)
                    part = lax.dot_general(
                        hb, sb, (((0,), (0,)), ((), ())), preferred_element_type=jnp.float32
                    )
                    out_ref[spot, j * NSUB + i] = (part * _flag(idx_ref, k)).astype(out_ref.dtype)

            @pl.when(idx_ref[3 * first + 2] <= 0)
            def _():
                out_ref[spot, pl.ds(j * NSUB, NSUB)] = jnp.zeros((NSUB, BLK, BLK), out_ref.dtype)


def dw_half(stash_h, stash_s, block_index, b0, dtype):
    per = block_index.shape[0] // 8
    return pl.pallas_call(
        _dw_half_kernel,
        out_shape=jax.ShapeDtypeStruct((4, per, BLK, BLK), dtype),
        in_specs=[_SMEM, _SMEM, _VMEM, _VMEM],
        out_specs=_VMEM,
        compiler_params=pltpu.CompilerParams(vmem_limit_bytes=VMEM_LIMIT),
    )(b0.reshape(1).astype(jnp.int32), block_index.reshape(-1), stash_h, stash_s)


def _exchange(send, pairs):
    return lax.ppermute(send.astype(jnp.bfloat16), "dp", pairs).astype(jnp.float32)


def weight_grads(stash_h, stash_s, block_index, mbs):
    n = lax.axis_size("dp")
    if n != 8:
        acc = segment_dw(stash_h, stash_s, block_index, mbs)
        return lax.psum_scatter(
            acc.astype(jnp.bfloat16), "dp", scatter_dimension=0, tiled=True
        ).astype(jnp.float32)
    d = lax.axis_index("dp")
    d0, d1, d2 = d % 2, (d // 2) % 2, d // 4
    pick = lambda a, i, axis: lax.dynamic_index_in_dim(a, i, axis, keepdims=False)
    send = dw_half(stash_h, stash_s, block_index, 1 - d0, jnp.bfloat16)
    got = lax.ppermute(send, "dp", [(i, i ^ 1) for i in range(8)])
    keep = dw_half(stash_h, stash_s, block_index, d0, jnp.float32)
    keep = keep.reshape((2, 2) + keep.shape[1:])
    got = got.reshape(keep.shape)
    core0 = d0 == 0
    flip = jnp.where(core0, d1, d2)
    rem = jnp.where(core0, d2, d1)

    def summed(a, b, i):
        return pick(a, i, 1) + pick(b, i, 1).astype(jnp.float32)

    got2 = _exchange(summed(keep, got, 1 - flip), [(i, i ^ (2 if i % 2 == 0 else 4)) for i in range(8)])

    def part(i):
        return pick(pick(keep, flip, 1), i, 0) + pick(pick(got, flip, 1), i, 0).astype(jnp.float32) + pick(got2, i, 0)

    got3 = _exchange(part(1 - rem), [(i, i ^ (4 if i % 2 == 0 else 2)) for i in range(8)])
    return part(rem) + got3


def _allocate_kernel(*refs):
    del refs


def allocate(specs):
    return pl.pallas_call(
        _allocate_kernel,
        out_shape=tuple(jax.ShapeDtypeStruct(shape, dtype) for shape, dtype in specs),
        out_specs=tuple(_ANY for _ in specs),
    )()


def on_device(x_in, cotangent, weights, block_index):
    segments = lax.axis_size("segment")
    me_segment = lax.axis_index("segment")
    mbs, rows_dev, width = x_in.shape
    mbs, rows_dev = mbs * SPLIT, rows_dev // SPLIT
    x_in = x_in.reshape(mbs, rows_dev, width)
    cotangent = cotangent.reshape(mbs, rows_dev, width)
    idx = block_index.reshape(LSLOT, KMAX, 3)

    def tick_body(tick, carry):
        recv_f, recv_b, saved_h, saved_y, saved_s = carry
        micro_f = tick - me_segment
        live_f = (micro_f >= 0) & (micro_f < mbs)
        at_f = jnp.clip(micro_f, 0, mbs - 1)
        def run_f(operands):
            h, sh, sy = operands
            for layer in range(LSLOT):
                local = (x_in, me_segment == 0) if layer == 0 else (None, None)
                h, sh, sy = layer_forward(h, weights, layer, block_index, at_f, sh, sy, *local)
            return (h, sh, sy)

        h_out, saved_h, saved_y = lax.cond(live_f, run_f, lambda ops: ops, (recv_f, saved_h, saved_y))
        send_f = shifted(h_out, "segment", 1)

        micro_b = tick - (2 * segments - 2 - me_segment)
        live_b = (micro_b >= 0) & (micro_b < mbs)
        at_b = jnp.clip(micro_b, 0, mbs - 1)
        stash_y_now = saved_y

        def run_b(operands):
            grad, ss = operands
            for layer in reversed(range(LSLOT)):
                local = (cotangent, me_segment == segments - 1) if layer == LSLOT - 1 else (None, None)
                grad, ss = layer_backward(grad, stash_y_now, weights, layer, block_index, at_b, ss, *local)
            return (grad, ss)

        grad_out, saved_s = lax.cond(live_b, run_b, lambda ops: ops, (recv_b, saved_s))
        send_b = shifted(grad_out, "segment", -1)
        return (send_f, send_b, saved_h, saved_y, saved_s)

    stash_shape = (LSLOT, mbs, rows_dev, width)
    stash_h, stash_y, stash_s = allocate(
        [(stash_shape, jnp.bfloat16), (stash_shape, jnp.float32), (stash_shape, jnp.bfloat16)]
    )
    blank = jnp.zeros((rows_dev, width), jnp.bfloat16)
    ticks = mbs + 2 * segments - 2
    carry = (blank, blank, stash_h, stash_y, stash_s)
    for tick in range(ticks):
        carry = tick_body(tick, carry)
    unused_f, unused_b, stash_h, stash_y, stash_s = carry
    return weight_grads(stash_h, stash_s, block_index, mbs)


def solution(mesh):
    return jax.shard_map(
        on_device,
        mesh=mesh,
        in_specs=(
            P(None, "dp", None),
            P(None, "dp", None),
            P("segment", None, None),
            P("segment", None),
        ),
        out_specs=P(("segment", "dp"), None, None),
        check_vma=False,
    )
```

```python
import functools

import jax
import jax.numpy as jnp
from jax import lax
from jax.experimental import pallas as pl
from jax.experimental.pallas import tpu as pltpu
from jax.sharding import PartitionSpec as P

BLK = 128
LSLOT = 2
KMAX = 128
CH = 2048
NSUB = 32
SPLIT = 2
GROUP = 16
VMEM_LIMIT = 60 * 1024 * 1024

_SMEM = pl.BlockSpec(memory_space=pltpu.SMEM)
_VMEM = pl.BlockSpec(memory_space=pltpu.VMEM)
_ANY = pl.BlockSpec(memory_space=pl.ANY)


def shifted(value, axis, steps):
    count = lax.axis_size(axis)
    leading, last = (max(0, -steps), min(count, count - steps))
    return lax.ppermute(value, axis, [(source, source + steps) for source in range(leading, last)])


def _blk(i):
    return pl.ds(pl.multiple_of(i * BLK, BLK), BLK)


def _chunk(j):
    return pl.ds(pl.multiple_of(j * CH, CH), CH)


def _flag(idx_ref, k):
    return jnp.where(idx_ref[3 * k + 2] > 0, 1.0, 0.0).astype(jnp.float32)


class _WeightChunks:
    def __init__(self, w_hbm, base, w_vmem, sems):
        self.w_hbm, self.base, self.w_vmem, self.sems = w_hbm, base, w_vmem, sems

    def copy(self, j):
        return pltpu.make_async_copy(
            self.w_hbm.at[pl.ds(self.base + j * NSUB, NSUB)],
            self.w_vmem.at[pl.ds(j * NSUB, NSUB)],
            self.sems.at[j],
        )

    def wait_on(self, j):
        self.copy(j).wait()


def _w_copies(w_hbm, base, w_vmem, sems):
    chunks = _WeightChunks(w_hbm, base, w_vmem, sems)
    started = []
    for j in range(w_vmem.shape[0] // NSUB):
        copy = chunks.copy(j)
        copy.start()
        started.append(copy)
    return (chunks, started)


def _slot_chunks(idx_ref, base, copies, product, update):
    def chunk(j, carry):
        copies[0].wait_on(j)

        @pl.when(idx_ref[3 * (base + j * NSUB) + 2] > 0)
        def _():
            for g in range(0, NSUB, GROUP):
                ks = [j * NSUB + g + i for i in range(GROUP)]
                parts = [product(k) for k in ks]
                for k, part in zip(ks, parts):
                    update(k, part)

        return carry

    lax.fori_loop(0, len(copies[1]), chunk, 0)


def _pick_input(at, src_ref, local_hbm, h_ref, sem):
    @pl.when(at[1] > 0)
    def _():
        pltpu.make_async_copy(local_hbm.at[at[0]], h_ref, sem).start()

    @pl.when(at[1] <= 0)
    def _():
        pltpu.make_async_copy(src_ref, h_ref, sem).start()

    pltpu.make_async_copy(src_ref, h_ref, sem).wait()


def _fwd_kernel(base, layer, at_ref, idx_ref, h_in, w_hbm, sh_in, sy_in, *rest):
    if layer == 0:
        local_hbm, hout_ref, sh_ref, sy_ref, w_vmem, y_vmem, sems, io_sems, h_ref = rest
    else:
        hout_ref, sh_ref, sy_ref, w_vmem, y_vmem, sems, io_sems = rest
        h_ref = h_in
    del sh_in, sy_in
    width = h_ref.shape[1]
    at = at_ref[0]
    copies = _w_copies(w_hbm, base, w_vmem, sems)
    if layer == 0:
        _pick_input((at, at_ref[1]), h_in, local_hbm, h_ref, io_sems.at[2])
    save_h = pltpu.make_async_copy(h_ref, sh_ref.at[layer, at], io_sems.at[0])
    save_h.start()
    y_vmem[...] = jnp.zeros_like(y_vmem)

    def product(k):
        r = idx_ref[3 * (base + k)]
        return jnp.dot(h_ref[:, _blk(r)], w_vmem[k], preferred_element_type=jnp.float32)

    def update(k, p):
        c = idx_ref[3 * (base + k) + 1]
        y_vmem[:, _blk(c)] += p * _flag(idx_ref, base + k)

    _slot_chunks(idx_ref, base, copies, product, update)
    save_y = pltpu.make_async_copy(y_vmem, sy_ref.at[layer, at], io_sems.at[1])
    save_y.start()

    def epi(j, carry):
        y = y_vmem[:, _chunk(j)]
        h = h_ref[:, _chunk(j)].astype(jnp.float32)
        hout_ref[:, _chunk(j)] = (h + y / (1.0 + jnp.exp(-y))).astype(hout_ref.dtype)
        return carry

    lax.fori_loop(0, width // CH, epi, 0)
    save_h.wait()
    save_y.wait()


def layer_forward(h, weights, layer, block_index, at, stash_h, stash_y, local=None, use_local=None):
    rows, width = h.shape
    extra_in, extra_args, extra_scratch = [], [], []
    if layer == 0:
        extra_in, extra_args = [_ANY], [local]
        extra_scratch = [pltpu.VMEM((rows, width), h.dtype)]
        at = jnp.stack([at, use_local.astype(jnp.int32)])
    return pl.pallas_call(
        functools.partial(_fwd_kernel, layer * KMAX, layer),
        out_shape=(
            jax.ShapeDtypeStruct((rows, width), jnp.bfloat16),
            jax.ShapeDtypeStruct(stash_h.shape, stash_h.dtype),
            jax.ShapeDtypeStruct(stash_y.shape, stash_y.dtype),
        ),
        in_specs=[_SMEM, _SMEM, _VMEM, _ANY, _ANY, _ANY] + extra_in,
        out_specs=(_VMEM, _ANY, _ANY),
        scratch_shapes=[
            pltpu.VMEM((KMAX, BLK, BLK), weights.dtype),
            pltpu.VMEM((rows, width), jnp.float32),
            pltpu.SemaphoreType.DMA((KMAX // NSUB,)),
            pltpu.SemaphoreType.DMA((3,)),
        ]
        + extra_scratch,
        input_output_aliases={4: 1, 5: 2},
        compiler_params=pltpu.CompilerParams(vmem_limit_bytes=VMEM_LIMIT),
    )(at.reshape(-1), block_index.reshape(-1), h, weights, stash_h, stash_y, *extra_args)


def _bwd_kernel(base, layer, entry, at_ref, idx_ref, g_in, sy_hbm, w_hbm, ss_in, *rest):
    if entry:
        local_hbm, gout_ref, ss_ref, y_vmem, s_vmem, sp_ref, w_vmem, sems, io_sems, g_ref = rest
    else:
        gout_ref, ss_ref, y_vmem, s_vmem, sp_ref, w_vmem, sems, io_sems = rest
        g_ref = g_in
    del ss_in
    width = g_ref.shape[1]
    at = at_ref[0]
    if entry:
        _pick_input((at, at_ref[1]), g_in, local_hbm, g_ref, io_sems.at[2])
    load_y = pltpu.make_async_copy(sy_hbm.at[layer, at], y_vmem, io_sems.at[0])
    load_y.start()
    copies = _w_copies(w_hbm, base, w_vmem, sems)
    load_y.wait()

    def pre(j, carry):
        y = y_vmem[:, _chunk(j)]
        sig = 1.0 / (1.0 + jnp.exp(-y))
        g = g_ref[:, _chunk(j)].astype(jnp.float32)
        s_vmem[:, _chunk(j)] = (g * sig * (1.0 + y * (1.0 - sig))).astype(s_vmem.dtype)
        sp_ref[:, _chunk(j)] = jnp.zeros((g_ref.shape[0], CH), jnp.float32)
        return carry

    lax.fori_loop(0, width // CH, pre, 0)
    save_s = pltpu.make_async_copy(s_vmem, ss_ref.at[layer, at], io_sems.at[1])
    save_s.start()

    def product(k):
        c = idx_ref[3 * (base + k) + 1]
        return lax.dot_general(
            s_vmem[:, _blk(c)],
            w_vmem[k],
            (((1,), (1,)), ((), ())),
            preferred_element_type=jnp.float32,
        )

    def update(k, back):
        r = idx_ref[3 * (base + k)]
        sp_ref[:, _blk(r)] += back * _flag(idx_ref, base + k)

    _slot_chunks(idx_ref, base, copies, product, update)

    def epi(j, carry):
        g = g_ref[:, _chunk(j)].astype(jnp.float32)
        gout_ref[:, _chunk(j)] = (g + sp_ref[:, _chunk(j)]).astype(gout_ref.dtype)
        return carry

    lax.fori_loop(0, width // CH, epi, 0)
    save_s.wait()


def layer_backward(g, stash_y, weights, layer, block_index, at, stash_s, local=None, use_local=None):
    rows, width = g.shape
    entry = local is not None
    extra_in, extra_args, extra_scratch = [], [], []
    if entry:
        extra_in, extra_args = [_ANY], [local]
        extra_scratch = [pltpu.VMEM((rows, width), g.dtype)]
        at = jnp.stack([at, use_local.astype(jnp.int32)])
    return pl.pallas_call(
        functools.partial(_bwd_kernel, layer * KMAX, layer, entry),
        out_shape=(
            jax.ShapeDtypeStruct((rows, width), jnp.bfloat16),
            jax.ShapeDtypeStruct(stash_s.shape, stash_s.dtype),
        ),
        in_specs=[_SMEM, _SMEM, _VMEM, _ANY, _ANY, _ANY] + extra_in,
        out_specs=(_VMEM, _ANY),
        scratch_shapes=[
            pltpu.VMEM((rows, width), jnp.float32),
            pltpu.VMEM((rows, width), jnp.bfloat16),
            pltpu.VMEM((rows, width), jnp.float32),
            pltpu.VMEM((KMAX, BLK, BLK), weights.dtype),
            pltpu.SemaphoreType.DMA((KMAX // NSUB,)),
            pltpu.SemaphoreType.DMA((3,)),
        ]
        + extra_scratch,
        input_output_aliases={5: 1},
        compiler_params=pltpu.CompilerParams(vmem_limit_bytes=VMEM_LIMIT),
    )(at.reshape(-1), block_index.reshape(-1), g, stash_y, weights, stash_s, *extra_args)


def _dw_kernel(mbs, idx_ref, h_ref, s_ref, dw_ref):
    rows = h_ref.shape[1] * h_ref.shape[2]
    for j in range(dw_ref.shape[0] // NSUB):
        layer = j * NSUB // KMAX

        @pl.when(idx_ref[3 * j * NSUB + 2] > 0)
        def _():
            for k in range(j * NSUB, (j + 1) * NSUB):
                r = idx_ref[3 * k]
                c = idx_ref[3 * k + 1]
                hb = h_ref[layer, :, :, _blk(r)]
                sb = s_ref[layer, :, :, _blk(c)]
                dw_ref[k] = lax.dot_general(
                    hb.reshape(rows, BLK),
                    sb.reshape(rows, BLK),
                    (((0,), (0,)), ((), ())),
                    preferred_element_type=jnp.float32,
                ) * _flag(idx_ref, k)

        @pl.when(idx_ref[3 * j * NSUB + 2] <= 0)
        def _():
            dw_ref[pl.ds(j * NSUB, NSUB)] = jnp.zeros((NSUB, BLK, BLK), jnp.float32)


def segment_dw(stash_h, stash_s, block_index, mbs):
    return pl.pallas_call(
        functools.partial(_dw_kernel, mbs),
        out_shape=jax.ShapeDtypeStruct((block_index.shape[0], BLK, BLK), jnp.float32),
        in_specs=[_SMEM, _VMEM, _VMEM],
        out_specs=_VMEM,
        compiler_params=pltpu.CompilerParams(vmem_limit_bytes=VMEM_LIMIT),
    )(block_index.reshape(-1), stash_h, stash_s)


def _dw_half_kernel(sel_ref, idx_ref, h_ref, s_ref, out_ref):
    b0 = sel_ref[0]
    rows = h_ref.shape[1] * h_ref.shape[2]
    per = out_ref.shape[1]
    for q in range(out_ref.shape[0]):
        layer = (2 * q * per) // KMAX
        spot = q + b0 * ((q % 2) * 2 + q // 2 - q)
        for j in range(per // NSUB):
            first = 2 * q * per + b0 * per + j * NSUB

            @pl.when(idx_ref[3 * first + 2] > 0)
            def _():
                for i in range(NSUB):
                    k = first + i
                    r = idx_ref[3 * k]
                    c = idx_ref[3 * k + 1]
                    hb = h_ref[layer, :, :, _blk(r)].reshape(rows, BLK)
                    sb = s_ref[layer, :, :, _blk(c)].reshape(rows, BLK)
                    part = lax.dot_general(
                        hb, sb, (((0,), (0,)), ((), ())), preferred_element_type=jnp.float32
                    )
                    out_ref[spot, j * NSUB + i] = (part * _flag(idx_ref, k)).astype(out_ref.dtype)

            @pl.when(idx_ref[3 * first + 2] <= 0)
            def _():
                out_ref[spot, pl.ds(j * NSUB, NSUB)] = jnp.zeros((NSUB, BLK, BLK), out_ref.dtype)


def dw_half(stash_h, stash_s, block_index, b0, dtype):
    per = block_index.shape[0] // 8
    return pl.pallas_call(
        _dw_half_kernel,
        out_shape=jax.ShapeDtypeStruct((4, per, BLK, BLK), dtype),
        in_specs=[_SMEM, _SMEM, _VMEM, _VMEM],
        out_specs=_VMEM,
        compiler_params=pltpu.CompilerParams(vmem_limit_bytes=VMEM_LIMIT),
    )(b0.reshape(1).astype(jnp.int32), block_index.reshape(-1), stash_h, stash_s)


def _exchange(send, pairs):
    return lax.ppermute(send.astype(jnp.bfloat16), "dp", pairs).astype(jnp.float32)


def weight_grads(stash_h, stash_s, block_index, mbs):
    n = lax.axis_size("dp")
    if n != 8:
        acc = segment_dw(stash_h, stash_s, block_index, mbs)
        return lax.psum_scatter(
            acc.astype(jnp.bfloat16), "dp", scatter_dimension=0, tiled=True
        ).astype(jnp.float32)
    d = lax.axis_index("dp")
    d0, d1, d2 = d % 2, (d // 2) % 2, d // 4
    pick = lambda a, i, axis: lax.dynamic_index_in_dim(a, i, axis, keepdims=False)
    send = dw_half(stash_h, stash_s, block_index, 1 - d0, jnp.bfloat16)
    got = lax.ppermute(send, "dp", [(i, i ^ 1) for i in range(8)])
    keep = dw_half(stash_h, stash_s, block_index, d0, jnp.float32)
    keep = keep.reshape((2, 2) + keep.shape[1:])
    got = got.reshape(keep.shape)
    core0 = d0 == 0
    flip = jnp.where(core0, d1, d2)
    rem = jnp.where(core0, d2, d1)

    def summed(a, b, i):
        return pick(a, i, 1) + pick(b, i, 1).astype(jnp.float32)

    got2 = _exchange(summed(keep, got, 1 - flip), [(i, i ^ (2 if i % 2 == 0 else 4)) for i in range(8)])

    def part(i):
        return pick(pick(keep, flip, 1), i, 0) + pick(pick(got, flip, 1), i, 0).astype(jnp.float32) + pick(got2, i, 0)

    got3 = _exchange(part(1 - rem), [(i, i ^ (4 if i % 2 == 0 else 2)) for i in range(8)])
    return part(rem) + got3


def _allocate_kernel(*refs):
    del refs


def allocate(specs):
    return pl.pallas_call(
        _allocate_kernel,
        out_shape=tuple(jax.ShapeDtypeStruct(shape, dtype) for shape, dtype in specs),
        out_specs=tuple(_ANY for _ in specs),
    )()


def on_device(x_in, cotangent, weights, block_index):
    segments = lax.axis_size("segment")
    me_segment = lax.axis_index("segment")
    mbs, rows_dev, width = x_in.shape
    mbs, rows_dev = mbs * SPLIT, rows_dev // SPLIT
    x_in = x_in.reshape(mbs, rows_dev, width)
    cotangent = cotangent.reshape(mbs, rows_dev, width)
    idx = block_index.reshape(LSLOT, KMAX, 3)

    def tick_body(tick, carry):
        recv_f, recv_b, saved_h, saved_y, saved_s = carry
        micro_f = tick - me_segment
        live_f = (micro_f >= 0) & (micro_f < mbs)
        at_f = jnp.clip(micro_f, 0, mbs - 1)
        def run_f(operands):
            h, sh, sy = operands
            for layer in range(LSLOT):
                local = (x_in, me_segment == 0) if layer == 0 else (None, None)
                h, sh, sy = layer_forward(h, weights, layer, block_index, at_f, sh, sy, *local)
            return (h, sh, sy)

        h_out, saved_h, saved_y = lax.cond(live_f, run_f, lambda ops: ops, (recv_f, saved_h, saved_y))
        send_f = shifted(h_out, "segment", 1)

        micro_b = tick - (2 * segments - 2 - me_segment)
        live_b = (micro_b >= 0) & (micro_b < mbs)
        at_b = jnp.clip(micro_b, 0, mbs - 1)
        stash_y_now = saved_y

        def run_b(operands):
            grad, ss = operands
            for layer in reversed(range(LSLOT)):
                local = (cotangent, me_segment == segments - 1) if layer == LSLOT - 1 else (None, None)
                grad, ss = layer_backward(grad, stash_y_now, weights, layer, block_index, at_b, ss, *local)
            return (grad, ss)

        grad_out, saved_s = lax.cond(live_b, run_b, lambda ops: ops, (recv_b, saved_s))
        send_b = shifted(grad_out, "segment", -1)
        return (send_f, send_b, saved_h, saved_y, saved_s)

    stash_shape = (LSLOT, mbs, rows_dev, width)
    stash_h, stash_y, stash_s = allocate(
        [(stash_shape, jnp.bfloat16), (stash_shape, jnp.float32), (stash_shape, jnp.bfloat16)]
    )
    blank = jnp.zeros((rows_dev, width), jnp.bfloat16)
    ticks = mbs + 2 * segments - 2
    carry = (blank, blank, stash_h, stash_y, stash_s)
    for tick in range(ticks):
        carry = tick_body(tick, carry)
    unused_f, unused_b, stash_h, stash_y, stash_s = carry
    return weight_grads(stash_h, stash_s, block_index, mbs)


def solution(mesh):
    return jax.shard_map(
        on_device,
        mesh=mesh,
        in_specs=(
            P(None, "dp", None),
            P(None, "dp", None),
            P("segment", None, None),
            P("segment", None),
        ),
        out_specs=P(("segment", "dp"), None, None),
        check_vma=False,
    )
```
